512 devices in a mesh: ctx: 128 (over y, z, core), head: 4 (over x).
Axes of the slice: x: 4, y: 4, z: 16, core: 2. Of those that a mesh axis runs over, the one named last changes fastest.
Arguments:
- lin_query: bfloat16 [16384, 2048], P('ctx', 'head'), may hold values from -6 to 6
- lin_key: bfloat16 [16384, 2048], P('ctx', 'head'), may hold values from -6 to 6
- lin_value: bfloat16 [16384, 2048], P('ctx', 'head'), may hold values from -64 to 64
- norm_gain: float32 [2048], P('head'), may hold values from 0.1 to 1.9
- lin_grad: bfloat16 [16384, 2048], P('ctx', 'head'), may hold values from -6 to 6
- sm_query: bfloat16 [16384, 2048], P('ctx', 'head'), may hold values from -5 to 5
- sm_key: bfloat16 [16384, 2048], P('ctx', 'head'), may hold values from -5 to 5
- sm_value: bfloat16 [16384, 2048], P('ctx', 'head'), may hold values from -6 to 6
- sm_grad: bfloat16 [16384, 2048], P('ctx', 'head'), may hold values from -6 to 6
- tile_lists: int32 [128, 3], P('ctx'), may hold values from -1 to 126, as said below
Outputs:
- lin_dq: bfloat16 [16384, 2048], P('ctx', 'head')
- lin_dk: bfloat16 [16384, 2048], P('ctx', 'head')
- lin_dv: bfloat16 [16384, 2048], P('ctx', 'head')
- sm_dq: bfloat16 [16384, 2048], P('ctx', 'head')
- sm_dk: bfloat16 [16384, 2048], P('ctx', 'head')
- sm_dv: bfloat16 [16384, 2048], P('ctx', 'head')
The draws below stay inside these ranges and needn't reach their ends.
Inputs may be any that keep to these rules, and one draw needn't show every extreme that they name: `tile_lists`: entry 0 of row i is i - 1 (-1 for i = 0). The other entries of row i are -1 or distinct tiles j with j < i - 1 and j >= i - 4.
All inputs are finite; a program needn't handle non-finite values.
Results may differ from the reference program's by a relative error of at most 0.012.
Values may be sent and summed in bfloat16 or wider, within the bound.
No kernel may reach another device: no remote copies, remote signals or barrier semaphores. Data moves between devices by JAX's collectives and lax.ppermute only.
A program may use at most 128 MiB of HBM per device.

```python
import math
import jax
import jax.numpy as jnp
from jax import lax

HEAD = 128
LIN_HEADS = 16
SM_HEADS = 16
TILE = 128
LIST = 3
SPAN = 4
TOK_DEV = 128
TOKENS = 16384
N_CTX = 128


def softmax_pair(key):
    base_key = jax.random.fold_in(key, 7)
    query_key, key_key = jax.random.split(base_key, 2)
    shape_all = (TOKENS, SM_HEADS * HEAD)
    queries = jnp.clip(jax.random.normal(query_key, shape_all, jnp.float32), -5.0, 5.0)
    keys_drawn = jnp.clip(jax.random.normal(key_key, shape_all, jnp.float32), -5.0, 5.0)
    return (queries, keys_drawn)


def draw_sm_query(key, part):
    return softmax_pair(key)[0].astype(jnp.bfloat16)


def draw_sm_key(key, part):
    return softmax_pair(key)[1].astype(jnp.bfloat16)


def draw_lin_value(key, part):
    shape_all = (TOKENS, LIN_HEADS * HEAD)
    value_key = jax.random.fold_in(jax.random.fold_in(key, 5), 0)
    head_pos = (jnp.arange(LIN_HEADS * HEAD)[None, :] // HEAD).astype(jnp.float32) / (LIN_HEADS - 1)
    base = jnp.clip(jax.random.normal(value_key, shape_all, jnp.float32), -5.0, 5.0)
    values = base * jnp.exp(head_pos * math.log(3.0))
    return values.astype(jnp.bfloat16)


def draw_tile_lists(key, part):
    tile_total = TOKENS // TILE
    tiles_dev = TOK_DEV // TILE
    most_back = SPAN * tiles_dev + tiles_dev - 1
    tile_pos = jnp.arange(tile_total, dtype=jnp.int32)[:, None]
    lowest = jnp.maximum(0, (tile_pos // tiles_dev - SPAN) * tiles_dev)
    reach = tile_pos - lowest
    first_entry = jnp.where(reach >= 1, tile_pos - 1, -1)
    offsets = jnp.arange(2, most_back + 1, dtype=jnp.int32)[None, :]
    scores = jax.random.randint(jax.random.fold_in(key, 3), (tile_total, most_back - 1), 0, 2 ** 20, dtype=jnp.int32) * most_back + offsets
    scores = scores + jnp.where(offsets > reach, 2 ** 30, 0)
    order = jnp.argsort(scores, axis=1, stable=True)[:, :LIST - 1]
    chosen = jnp.take_along_axis(jnp.broadcast_to(offsets, (tile_total, most_back - 1)), order, axis=1)
    entries = jnp.where(chosen <= reach, tile_pos - chosen, -1)
    return jnp.concatenate([first_entry, entries], axis=1).astype(jnp.int32)


def levels(key, shape, shards, smallest, largest):
    def one(dim, parts):
        heights = jax.random.uniform(jax.random.fold_in(jax.random.fold_in(key, 6), dim), (parts,), jnp.float32, smallest / len(shards), largest / len(shards))
        return jnp.repeat(jnp.exp(heights), shape[dim] // parts).reshape((-1,) + (1,) * (len(shape) - dim - 1))

    gain = one(*shards[0])
    for cut in shards[1:]:
        gain = gain * one(*cut)
    return gain


def normal_values(stream_key, dims, scale, limit, cuts=(), kind=jnp.bfloat16):
    array = jax.random.normal(stream_key, dims, jnp.float32) * scale
    if len(cuts) > 0:
        array = levels(stream_key, dims, cuts, -0.22, 0.18) * array
    return jnp.clip(array, min=-limit, max=limit).astype(kind)


def setup_inputs(seed: int = 0) -> dict:
    keys = jax.random.split(jax.random.key(seed), 11)
    return {
        "lin_query": normal_values(keys[0], (TOKENS, LIN_HEADS * HEAD), 1.0, 6.0, ((0, 128), (1, 4))),
        "lin_key": normal_values(keys[1], (TOKENS, LIN_HEADS * HEAD), 1.0, 6.0, ((0, 128), (1, 4))),
        "lin_value": draw_lin_value(jax.random.fold_in(keys[10], 71), 0),
        "norm_gain": jnp.clip(1.0 + 0.18 * jax.random.normal(keys[3], (LIN_HEADS * HEAD,), jnp.float32), 0.1, 1.9),
        "lin_grad": normal_values(keys[4], (TOKENS, LIN_HEADS * HEAD), 1.0, 6.0, ((0, 128), (1, 4))),
        "sm_query": draw_sm_query(jax.random.fold_in(keys[10], 71), 0),
        "sm_key": draw_sm_key(jax.random.fold_in(keys[10], 71), 0),
        "sm_value": normal_values(keys[7], (TOKENS, SM_HEADS * HEAD), 1.0, 6.0, ((0, 128), (1, 4))),
        "sm_grad": normal_values(keys[8], (TOKENS, SM_HEADS * HEAD), 1.0, 6.0, ((0, 128), (1, 4))),
        "tile_lists": draw_tile_lists(jax.random.fold_in(keys[10], 71), 0),
    }


def tile_attention(query, grad, key_window, value_window, lists, shard):
    token_count, width = query.shape
    heads = width // HEAD
    tiles_dev = token_count // TILE
    window_tiles = key_window.shape[0] // TILE
    valid = lists >= 0
    local_index = jnp.where(valid, lists - (shard - SPAN) * tiles_dev, 0).astype(jnp.int32)
    own_index = (SPAN * tiles_dev + jnp.arange(tiles_dev, dtype=jnp.int32))[:, None]
    picked = jnp.concatenate([own_index, local_index], axis=1)
    keep = jnp.concatenate([jnp.ones((tiles_dev, 1), jnp.bool_), valid], axis=1)
    key_set = key_window.reshape(window_tiles, TILE, heads, HEAD)[picked].reshape(tiles_dev, (LIST + 1) * TILE, heads, HEAD).astype(jnp.float32)
    value_set = value_window.reshape(window_tiles, TILE, heads, HEAD)[picked].reshape(tiles_dev, (LIST + 1) * TILE, heads, HEAD).astype(jnp.float32)
    query_tiles = query.reshape(tiles_dev, TILE, heads, HEAD).astype(jnp.float32)
    grad_tiles = grad.reshape(tiles_dev, TILE, heads, HEAD).astype(jnp.float32)
    scale = HEAD ** (-0.5)
    scores = jnp.einsum('athd,ashd->ahts', query_tiles, key_set) * scale
    rows_idx = jnp.arange(TILE)[:, None]
    cols_idx = jnp.arange((LIST + 1) * TILE)[None, :]
    allowed = jnp.where(cols_idx // TILE == 0, cols_idx % TILE <= rows_idx, True)
    live = jnp.repeat(keep, TILE, axis=1)
    allowed_all = allowed[None, None, :, :] & live[:, None, None, :]
    scores = jnp.where(allowed_all, scores, -jnp.inf)
    top_score = lax.optimization_barrier(jnp.max(scores, axis=-1, keepdims=True))
    expo = jnp.exp(scores - top_score)
    probs = expo / lax.optimization_barrier(jnp.sum(expo, axis=-1, keepdims=True))
    probs_half = probs.astype(jnp.bfloat16)
    probs_wide = probs_half.astype(jnp.float32)
    attended = jnp.einsum('ahts,ashd->athd', probs_wide, value_set)
    delta = jnp.transpose(lax.optimization_barrier(jnp.sum(grad_tiles * attended, axis=-1)), (0, 2, 1))[..., None]
    grad_probs = jnp.einsum('athd,ashd->ahts', grad_tiles, value_set)
    grad_logits = (probs * (grad_probs - delta) * scale).astype(jnp.bfloat16).astype(jnp.float32)
    query_grad = jnp.einsum('ahts,ashd->athd', grad_logits, key_set).reshape(token_count, width).astype(jnp.bfloat16)
    key_part = jnp.einsum('ahts,athd->ashd', grad_logits, query_tiles).reshape(tiles_dev * (LIST + 1), TILE, width)
    value_part = jnp.einsum('ahts,athd->ashd', probs_wide, grad_tiles).reshape(tiles_dev * (LIST + 1), TILE, width)
    flat_index = picked.reshape(-1)
    key_acc = jnp.zeros((window_tiles, TILE, width), jnp.float32).at[flat_index].add(key_part)
    value_acc = jnp.zeros((window_tiles, TILE, width), jnp.float32).at[flat_index].add(value_part)
    return (query_grad, key_acc.reshape(SPAN + 1, token_count, width), value_acc.reshape(SPAN + 1, token_count, width))

def reference(lin_query, lin_key, lin_value, norm_gain, lin_grad, sm_query, sm_key, sm_value, sm_grad, tile_lists):
    lin_width = LIN_HEADS * HEAD
    shape_lin = (N_CTX, TOK_DEV, LIN_HEADS, HEAD)
    query_lin = lin_query.reshape(shape_lin)
    key_lin = lin_key.reshape(shape_lin)
    value_lin = lin_value.reshape(shape_lin)
    grad_lin = lin_grad.reshape(shape_lin)
    gain_heads = norm_gain.reshape(LIN_HEADS, HEAD).astype(jnp.float32)
    key_value = jnp.einsum('nthi,nthj->nhij', key_lin.astype(jnp.float32), value_lin.astype(jnp.float32))
    prefix_sum = jnp.cumsum(key_value, axis=0)
    state_half = jnp.concatenate([jnp.zeros_like(key_value[:1]), prefix_sum[:-1]], axis=0).astype(jnp.bfloat16)
    causal = jnp.tril(jnp.ones((TOK_DEV, TOK_DEV), jnp.bool_))

    def first_pass(items):
        query_blk, key_blk, value_blk, grad_blk, state_blk = items
        query_wide = query_blk.astype(jnp.float32)
        attn_lin = jnp.where(causal[None], jnp.einsum('thd,shd->hts', query_wide, key_blk.astype(jnp.float32)), 0.0).astype(jnp.bfloat16)
        output_lin = jnp.einsum('hts,shd->thd', attn_lin.astype(jnp.float32), value_blk.astype(jnp.float32)) + jnp.einsum('thi,hij->thj', query_wide, state_blk.astype(jnp.float32))
        gain_grad = gain_heads[None] * grad_blk.astype(jnp.float32)
        square_sum = lax.optimization_barrier(jnp.sum(output_lin * output_lin, axis=(1, 2)))
        cross_sum = lax.optimization_barrier(jnp.sum(gain_grad * output_lin, axis=(1, 2)))
        inv_rms = lax.rsqrt(square_sum / lin_width + 1e-06)[:, None, None]
        grad_out = (gain_grad * inv_rms - output_lin * inv_rms ** 3 * (cross_sum / lin_width)[:, None, None]).astype(jnp.bfloat16)
        adjoint_local = jnp.einsum('thi,thj->hij', query_wide, grad_out.astype(jnp.float32))
        return (grad_out, adjoint_local)
    grads_out, adjoint_local = lax.map(first_pass, (query_lin, key_lin, value_lin, grad_lin, state_half))
    reverse_sum = jnp.flip(jnp.cumsum(jnp.flip(adjoint_local, axis=0), axis=0), axis=0)
    adjoint_half = jnp.concatenate([reverse_sum[1:], jnp.zeros_like(reverse_sum[:1])], axis=0).astype(jnp.bfloat16)

    def second_pass(items):
        query_blk, key_blk, value_blk, grad_blk, state_blk, adjoint_blk = items
        query_wide = query_blk.astype(jnp.float32)
        key_wide = key_blk.astype(jnp.float32)
        value_wide = value_blk.astype(jnp.float32)
        grad_wide = grad_blk.astype(jnp.float32)
        state_wide = state_blk.astype(jnp.float32)
        adjoint_wide = adjoint_blk.astype(jnp.float32)
        attn_lin = jnp.where(causal[None], jnp.einsum('thd,shd->hts', query_wide, key_wide), 0.0).astype(jnp.bfloat16).astype(jnp.float32)
        grad_scores = jnp.where(causal[None], jnp.einsum('thd,shd->hts', grad_wide, value_wide), 0.0).astype(jnp.bfloat16).astype(jnp.float32)
        query_grad = jnp.einsum('hts,shd->thd', grad_scores, key_wide) + jnp.einsum('thj,hij->thi', grad_wide, state_wide)
        key_grad = jnp.einsum('hts,thd->shd', grad_scores, query_wide) + jnp.einsum('shj,hij->shi', value_wide, adjoint_wide)
        value_grad = jnp.einsum('hts,thd->shd', attn_lin, grad_wide) + jnp.einsum('shi,hij->shj', key_wide, adjoint_wide)
        return (query_grad.astype(jnp.bfloat16), key_grad.astype(jnp.bfloat16), value_grad.astype(jnp.bfloat16))
    lin_dq, lin_dk, lin_dv = lax.map(second_pass, (query_lin, key_lin, value_lin, grads_out, state_half, adjoint_half))
    lin_dq = lin_dq.reshape(TOKENS, lin_width)
    lin_dk = lin_dk.reshape(TOKENS, lin_width)
    lin_dv = lin_dv.reshape(TOKENS, lin_width)
    sm_width = SM_HEADS * HEAD
    pad_rows = SPAN * TOK_DEV
    window_rows = (SPAN + 1) * TOK_DEV
    key_pad = jnp.concatenate([jnp.zeros((pad_rows, sm_width), jnp.bfloat16), sm_key], axis=0)
    value_pad = jnp.concatenate([jnp.zeros((pad_rows, sm_width), jnp.bfloat16), sm_value], axis=0)
    lists_blocks = tile_lists.reshape(N_CTX, TOK_DEV // TILE, LIST)

    def shard_step(carry, shard):
        key_total, value_total = carry
        start = (shard * TOK_DEV).astype(jnp.int32)
        key_window = lax.dynamic_slice_in_dim(key_pad, start, window_rows, 0)
        value_window = lax.dynamic_slice_in_dim(value_pad, start, window_rows, 0)
        query_shard = lax.dynamic_slice_in_dim(sm_query, start, TOK_DEV, 0)
        grad_shard = lax.dynamic_slice_in_dim(sm_grad, start, TOK_DEV, 0)
        lists_shard = lax.dynamic_index_in_dim(lists_blocks, shard, 0, keepdims=False)
        query_grad, key_acc, value_acc = tile_attention(query_shard, grad_shard, key_window, value_window, lists_shard, shard)
        key_far = lax.optimization_barrier(key_acc[:SPAN].astype(jnp.bfloat16)).astype(jnp.float32)
        value_far = lax.optimization_barrier(value_acc[:SPAN].astype(jnp.bfloat16)).astype(jnp.float32)
        key_terms = jnp.concatenate([key_far, key_acc[SPAN:]], axis=0).reshape(window_rows, sm_width)
        value_terms = jnp.concatenate([value_far, value_acc[SPAN:]], axis=0).reshape(window_rows, sm_width)
        key_total = lax.dynamic_update_slice_in_dim(key_total, lax.dynamic_slice_in_dim(key_total, start, window_rows, 0) + key_terms, start, 0)
        value_total = lax.dynamic_update_slice_in_dim(value_total, lax.dynamic_slice_in_dim(value_total, start, window_rows, 0) + value_terms, start, 0)
        return ((key_total, value_total), query_grad)
    zeros_total = jnp.zeros((pad_rows + TOKENS, sm_width), jnp.float32)
    carry_end, query_grads = lax.scan(shard_step, (zeros_total, zeros_total), jnp.arange(N_CTX, dtype=jnp.int32))
    sm_dq = query_grads.reshape(TOKENS, sm_width)
    sm_dk = carry_end[0][pad_rows:].astype(jnp.bfloat16)
    sm_dv = carry_end[1][pad_rows:].astype(jnp.bfloat16)
    return (lin_dq, lin_dk, lin_dv, sm_dq, sm_dk, sm_dv)
```

```python
import jax
import jax.numpy as jnp
from jax import lax
from jax.sharding import PartitionSpec as P

HEAD = 128
LIN_HEADS = 16
TILE = 128
LIST = 3
SPAN = 4


def carried_in(shard, axis, join, neutral, backward):
    count = lax.axis_size(axis)
    total = shard.astype(jnp.float32)
    distance = 1
    while distance < count:
        if backward:
            pairs = [(i, i - distance) for i in range(distance, count)]
        else:
            pairs = [(i, i + distance) for i in range(count - distance)]
        total = join(total, lax.ppermute(total, axis, pairs))
        distance *= 2
    return (total - shard.astype(jnp.float32)).astype(shard.dtype)


def from_behind(shard, axis, by):
    length = lax.axis_size(axis)
    pairs = [(i, i + by) for i in range(length) if 0 <= i + by < length]
    return lax.ppermute(shard, axis, pairs)


def add_states(earlier, later):
    return earlier + later


def tile_attention(query, grad, key_window, value_window, lists, shard):
    token_count, width = query.shape
    heads = width // HEAD
    tiles_dev = token_count // TILE
    window_tiles = key_window.shape[0] // TILE
    valid = lists >= 0
    local_index = jnp.where(valid, lists - (shard - SPAN) * tiles_dev, 0)
    own_index = (SPAN * tiles_dev + jnp.arange(tiles_dev, dtype=jnp.int32))[:, None]
    picked = jnp.concatenate([own_index, local_index], axis=1)
    keep = jnp.concatenate([jnp.ones((tiles_dev, 1), jnp.bool_), valid], axis=1)
    key_set = key_window.reshape(window_tiles, TILE, heads, HEAD)[picked].reshape(
        tiles_dev, (LIST + 1) * TILE, heads, HEAD
    )
    value_set = value_window.reshape(window_tiles, TILE, heads, HEAD)[picked].reshape(
        tiles_dev, (LIST + 1) * TILE, heads, HEAD
    )
    query_tiles = query.reshape(tiles_dev, TILE, heads, HEAD)
    grad_tiles = grad.reshape(tiles_dev, TILE, heads, HEAD)
    scale = HEAD ** (-0.5)
    scores = (
        jnp.einsum("athd,ashd->ahts", query_tiles, key_set, preferred_element_type=jnp.float32)
        * scale
    )
    rows_idx = jnp.arange(TILE)[:, None]
    cols_idx = jnp.arange((LIST + 1) * TILE)[None, :]
    allowed = jnp.where(cols_idx // TILE == 0, cols_idx % TILE <= rows_idx, True)
    live = jnp.repeat(keep, TILE, axis=1)
    allowed_all = allowed[None, None, :, :] & live[:, None, None, :]
    scores = jnp.where(allowed_all, scores, -jnp.inf)
    top_score = jnp.max(scores, axis=-1, keepdims=True)
    expo = jnp.exp(scores - top_score)
    probs = expo / jnp.sum(expo, axis=-1, keepdims=True)
    probs_half = probs.astype(jnp.bfloat16)
    attended = jnp.einsum(
        "ahts,ashd->athd", probs_half, value_set, preferred_element_type=jnp.float32
    )
    delta = jnp.transpose(jnp.sum(grad_tiles.astype(jnp.float32) * attended, axis=-1), (0, 2, 1))[
        ..., None
    ]
    grad_probs = jnp.einsum(
        "athd,ashd->ahts", grad_tiles, value_set, preferred_element_type=jnp.float32
    )
    grad_logits = (probs * (grad_probs - delta) * scale).astype(jnp.bfloat16)
    query_grad = (
        jnp.einsum("ahts,ashd->athd", grad_logits, key_set, preferred_element_type=jnp.float32)
        .reshape(token_count, width)
        .astype(jnp.bfloat16)
    )
    key_part = jnp.einsum(
        "ahts,athd->ashd", grad_logits, query_tiles, preferred_element_type=jnp.float32
    ).reshape(tiles_dev * (LIST + 1), TILE, width)
    value_part = jnp.einsum(
        "ahts,athd->ashd", probs_half, grad_tiles, preferred_element_type=jnp.float32
    ).reshape(tiles_dev * (LIST + 1), TILE, width)
    flat_index = picked.reshape(-1)
    key_acc = jnp.zeros((window_tiles, TILE, width), jnp.float32).at[flat_index].add(key_part)
    value_acc = jnp.zeros((window_tiles, TILE, width), jnp.float32).at[flat_index].add(value_part)
    return (query_grad, key_acc, value_acc)


def per_device(
    lin_query,
    lin_key,
    lin_value,
    norm_gain,
    lin_grad,
    sm_query,
    sm_key,
    sm_value,
    sm_grad,
    tile_lists,
):
    token_count = lin_query.shape[0]
    lin_width = lin_query.shape[1]
    heads_lin = lin_width // HEAD
    query_lin = lin_query.reshape(token_count, heads_lin, HEAD)
    key_lin = lin_key.reshape(token_count, heads_lin, HEAD)
    value_lin = lin_value.reshape(token_count, heads_lin, HEAD)
    key_value = jnp.einsum("thi,thj->hij", key_lin, value_lin, preferred_element_type=jnp.float32)
    state_low = carried_in(key_value, "ctx", add_states, jnp.zeros_like(key_value), False)
    state_half = state_low.astype(jnp.bfloat16)
    causal = jnp.tril(jnp.ones((token_count, token_count), jnp.bool_))
    attn_lin = jnp.where(
        causal[None],
        jnp.einsum("thd,shd->hts", query_lin, key_lin, preferred_element_type=jnp.float32),
        0.0,
    ).astype(jnp.bfloat16)
    output_lin = jnp.einsum(
        "hts,shd->thd", attn_lin, value_lin, preferred_element_type=jnp.float32
    ) + jnp.einsum("thi,hij->thj", query_lin, state_half, preferred_element_type=jnp.float32)
    gain_grad = norm_gain.reshape(1, heads_lin, HEAD) * lin_grad.reshape(
        token_count, heads_lin, HEAD
    ).astype(jnp.float32)
    square_sum = jnp.sum(output_lin * output_lin, axis=(1, 2))
    cross_sum = jnp.sum(gain_grad * output_lin, axis=(1, 2))
    square_sum, cross_sum = lax.psum((square_sum, cross_sum), "head")
    full_width = LIN_HEADS * HEAD
    inv_rms = lax.rsqrt(square_sum / full_width + 1e-06)[:, None, None]
    grad_out = (
        gain_grad * inv_rms - output_lin * inv_rms**3 * (cross_sum / full_width)[:, None, None]
    ).astype(jnp.bfloat16)
    adjoint_local = jnp.einsum(
        "thi,thj->hij", query_lin, grad_out, preferred_element_type=jnp.float32
    )
    adjoint_high = carried_in(adjoint_local, "ctx", add_states, jnp.zeros_like(adjoint_local), True)
    adjoint_half = adjoint_high.astype(jnp.bfloat16)
    grad_scores = jnp.where(
        causal[None],
        jnp.einsum("thd,shd->hts", grad_out, value_lin, preferred_element_type=jnp.float32),
        0.0,
    ).astype(jnp.bfloat16)
    lin_dq = jnp.einsum(
        "hts,shd->thd", grad_scores, key_lin, preferred_element_type=jnp.float32
    ) + jnp.einsum("thj,hij->thi", grad_out, state_half, preferred_element_type=jnp.float32)
    lin_dk = jnp.einsum(
        "hts,thd->shd", grad_scores, query_lin, preferred_element_type=jnp.float32
    ) + jnp.einsum("shj,hij->shi", value_lin, adjoint_half, preferred_element_type=jnp.float32)
    lin_dv = jnp.einsum(
        "hts,thd->shd", attn_lin, grad_out, preferred_element_type=jnp.float32
    ) + jnp.einsum("shi,hij->shj", key_lin, adjoint_half, preferred_element_type=jnp.float32)
    lin_dq = lin_dq.reshape(token_count, lin_width).astype(jnp.bfloat16)
    lin_dk = lin_dk.reshape(token_count, lin_width).astype(jnp.bfloat16)
    lin_dv = lin_dv.reshape(token_count, lin_width).astype(jnp.bfloat16)
    width = sm_key.shape[1]
    pair = jnp.concatenate([sm_key, sm_value], axis=1)
    arrived = [from_behind(pair, "ctx", distance) for distance in range(1, SPAN + 1)]
    key_window = jnp.concatenate(
        [arrived[SPAN - 1 - place][:, :width] for place in range(SPAN)] + [sm_key], axis=0
    )
    value_window = jnp.concatenate(
        [arrived[SPAN - 1 - place][:, width:] for place in range(SPAN)] + [sm_value], axis=0
    )
    shard = lax.axis_index("ctx")
    sm_dq, key_acc, value_acc = tile_attention(
        sm_query, sm_grad, key_window, value_window, tile_lists, shard
    )
    key_total = key_acc[SPAN]
    value_total = value_acc[SPAN]
    for distance in range(1, SPAN + 1):
        back = from_behind(
            jnp.concatenate(
                [key_acc[SPAN - distance], value_acc[SPAN - distance]], axis=1
            ).astype(jnp.bfloat16),
            "ctx",
            -distance,
        ).astype(jnp.float32)
        key_total = key_total + back[:, :width]
        value_total = value_total + back[:, width:]
    return (
        lin_dq,
        lin_dk,
        lin_dv,
        sm_dq,
        key_total.astype(jnp.bfloat16),
        value_total.astype(jnp.bfloat16),
    )


def solution(mesh):
    placed = (
        P("ctx", "head"),
        P("ctx", "head"),
        P("ctx", "head"),
        P("head"),
        P("ctx", "head"),
        P("ctx", "head"),
        P("ctx", "head"),
        P("ctx", "head"),
        P("ctx", "head"),
        P("ctx", None),
    )
    return jax.shard_map(
        per_device,
        mesh=mesh,
        in_specs=placed,
        out_specs=(
            P("ctx", "head"),
            P("ctx", "head"),
            P("ctx", "head"),
            P("ctx", "head"),
            P("ctx", "head"),
            P("ctx", "head"),
        ),
        check_vma=False,
    )
```

```python
import jax
import jax.numpy as jnp
from jax import lax
from jax.sharding import PartitionSpec as P

HEAD = 128
LIN_HEADS = 16
TILE = 128
LIST = 3
SPAN = 4


CTX = ("outer", "inner")
INNER = 8


def carried_in(shard, backward):
    wide = shard.astype(jnp.float32)

    def before(axis, full):
        place = lax.axis_index(axis)
        index = jnp.arange(lax.axis_size(axis))
        mask = index > place if backward else index < place
        gathered = lax.all_gather(full.astype(jnp.bfloat16), axis).astype(jnp.float32)
        picked = jnp.where(mask.reshape((-1,) + (1,) * full.ndim), gathered, 0.0)
        return jnp.sum(picked, axis=0), jnp.sum(gathered, axis=0)

    near, group = before("inner", wide)
    far, _ = before("outer", group)
    return near + far


def from_behind(shard, axis, by):
    length = lax.axis_size(axis)
    pairs = [(i, i + by) for i in range(length) if 0 <= i + by < length]
    return lax.ppermute(shard, axis, pairs)


def add_states(earlier, later):
    return earlier + later


def tile_attention(query, grad, key_window, value_window, lists, shard):
    token_count, width = query.shape
    heads = width // HEAD
    tiles_dev = token_count // TILE
    window_tiles = key_window.shape[0] // TILE
    valid = lists >= 0
    local_index = jnp.where(valid, lists - (shard - SPAN) * tiles_dev, 0)
    own_index = (SPAN * tiles_dev + jnp.arange(tiles_dev, dtype=jnp.int32))[:, None]
    picked = jnp.concatenate([own_index, local_index], axis=1)
    keep = jnp.concatenate([jnp.ones((tiles_dev, 1), jnp.bool_), valid], axis=1)
    key_set = key_window.reshape(window_tiles, TILE, heads, HEAD)[picked].reshape(
        tiles_dev, (LIST + 1) * TILE, heads, HEAD
    )
    value_set = value_window.reshape(window_tiles, TILE, heads, HEAD)[picked].reshape(
        tiles_dev, (LIST + 1) * TILE, heads, HEAD
    )
    query_tiles = query.reshape(tiles_dev, TILE, heads, HEAD)
    grad_tiles = grad.reshape(tiles_dev, TILE, heads, HEAD)
    scale = HEAD ** (-0.5)
    scores = (
        jnp.einsum("athd,ashd->ahts", query_tiles, key_set, preferred_element_type=jnp.float32)
        * scale
    )
    rows_idx = jnp.arange(TILE)[:, None]
    cols_idx = jnp.arange((LIST + 1) * TILE)[None, :]
    allowed = jnp.where(cols_idx // TILE == 0, cols_idx % TILE <= rows_idx, True)
    live = jnp.repeat(keep, TILE, axis=1)
    allowed_all = allowed[None, None, :, :] & live[:, None, None, :]
    scores = jnp.where(allowed_all, scores, -jnp.inf)
    top_score = jnp.max(scores, axis=-1, keepdims=True)
    expo = jnp.exp(scores - top_score)
    probs = expo / jnp.sum(expo, axis=-1, keepdims=True)
    probs_half = probs.astype(jnp.bfloat16)
    attended = jnp.einsum(
        "ahts,ashd->athd", probs_half, value_set, preferred_element_type=jnp.float32
    )
    delta = jnp.transpose(jnp.sum(grad_tiles.astype(jnp.float32) * attended, axis=-1), (0, 2, 1))[
        ..., None
    ]
    grad_probs = jnp.einsum(
        "athd,ashd->ahts", grad_tiles, value_set, preferred_element_type=jnp.float32
    )
    grad_logits = (probs * (grad_probs - delta) * scale).astype(jnp.bfloat16)
    query_grad = (
        jnp.einsum("ahts,ashd->athd", grad_logits, key_set, preferred_element_type=jnp.float32)
        .reshape(token_count, width)
        .astype(jnp.bfloat16)
    )
    key_part = jnp.einsum(
        "ahts,athd->ashd", grad_logits, query_tiles, preferred_element_type=jnp.float32
    ).reshape(tiles_dev * (LIST + 1), TILE, width)
    value_part = jnp.einsum(
        "ahts,athd->ashd", probs_half, grad_tiles, preferred_element_type=jnp.float32
    ).reshape(tiles_dev * (LIST + 1), TILE, width)
    flat_index = picked.reshape(-1)
    key_acc = jnp.zeros((window_tiles, TILE, width), jnp.float32).at[flat_index].add(key_part)
    value_acc = jnp.zeros((window_tiles, TILE, width), jnp.float32).at[flat_index].add(value_part)
    return (query_grad, key_acc, value_acc)


def per_device(
    lin_query,
    lin_key,
    lin_value,
    norm_gain,
    lin_grad,
    sm_query,
    sm_key,
    sm_value,
    sm_grad,
    tile_lists,
):
    token_count = lin_query.shape[0]
    lin_width = lin_query.shape[1]
    heads_lin = lin_width // HEAD
    query_lin = lin_query.reshape(token_count, heads_lin, HEAD)
    key_lin = lin_key.reshape(token_count, heads_lin, HEAD)
    value_lin = lin_value.reshape(token_count, heads_lin, HEAD)
    key_value = jnp.einsum("thi,thj->hij", key_lin, value_lin, preferred_element_type=jnp.float32)
    state_low = carried_in(key_value, False)
    state_half = state_low.astype(jnp.bfloat16)
    causal = jnp.tril(jnp.ones((token_count, token_count), jnp.bool_))
    attn_lin = jnp.where(
        causal[None],
        jnp.einsum("thd,shd->hts", query_lin, key_lin, preferred_element_type=jnp.float32),
        0.0,
    ).astype(jnp.bfloat16)
    output_lin = jnp.einsum(
        "hts,shd->thd", attn_lin, value_lin, preferred_element_type=jnp.float32
    ) + jnp.einsum("thi,hij->thj", query_lin, state_half, preferred_element_type=jnp.float32)
    gain_grad = norm_gain.reshape(1, heads_lin, HEAD) * lin_grad.reshape(
        token_count, heads_lin, HEAD
    ).astype(jnp.float32)
    square_sum = jnp.sum(output_lin * output_lin, axis=(1, 2))
    cross_sum = jnp.sum(gain_grad * output_lin, axis=(1, 2))
    square_sum, cross_sum = lax.psum((square_sum, cross_sum), "head")
    full_width = LIN_HEADS * HEAD
    inv_rms = lax.rsqrt(square_sum / full_width + 1e-06)[:, None, None]
    grad_out = (
        gain_grad * inv_rms - output_lin * inv_rms**3 * (cross_sum / full_width)[:, None, None]
    ).astype(jnp.bfloat16)
    adjoint_local = jnp.einsum(
        "thi,thj->hij", query_lin, grad_out, preferred_element_type=jnp.float32
    )
    adjoint_high = carried_in(adjoint_local, True)
    adjoint_half = adjoint_high.astype(jnp.bfloat16)
    grad_scores = jnp.where(
        causal[None],
        jnp.einsum("thd,shd->hts", grad_out, value_lin, preferred_element_type=jnp.float32),
        0.0,
    ).astype(jnp.bfloat16)
    lin_dq = jnp.einsum(
        "hts,shd->thd", grad_scores, key_lin, preferred_element_type=jnp.float32
    ) + jnp.einsum("thj,hij->thi", grad_out, state_half, preferred_element_type=jnp.float32)
    lin_dk = jnp.einsum(
        "hts,thd->shd", grad_scores, query_lin, preferred_element_type=jnp.float32
    ) + jnp.einsum("shj,hij->shi", value_lin, adjoint_half, preferred_element_type=jnp.float32)
    lin_dv = jnp.einsum(
        "hts,thd->shd", attn_lin, grad_out, preferred_element_type=jnp.float32
    ) + jnp.einsum("shi,hij->shj", key_lin, adjoint_half, preferred_element_type=jnp.float32)
    lin_dq = lin_dq.reshape(token_count, lin_width).astype(jnp.bfloat16)
    lin_dk = lin_dk.reshape(token_count, lin_width).astype(jnp.bfloat16)
    lin_dv = lin_dv.reshape(token_count, lin_width).astype(jnp.bfloat16)
    width = sm_key.shape[1]
    pair = jnp.concatenate([sm_key, sm_value], axis=1)
    arrived = [from_behind(pair, CTX, distance) for distance in range(1, SPAN + 1)]
    key_window = jnp.concatenate(
        [arrived[SPAN - 1 - place][:, :width] for place in range(SPAN)] + [sm_key], axis=0
    )
    value_window = jnp.concatenate(
        [arrived[SPAN - 1 - place][:, width:] for place in range(SPAN)] + [sm_value], axis=0
    )
    shard = lax.axis_index(CTX)
    sm_dq, key_acc, value_acc = tile_attention(
        sm_query, sm_grad, key_window, value_window, tile_lists, shard
    )
    key_total = key_acc[SPAN]
    value_total = value_acc[SPAN]
    for distance in range(1, SPAN + 1):
        back = from_behind(
            jnp.concatenate(
                [key_acc[SPAN - distance], value_acc[SPAN - distance]], axis=1
            ).astype(jnp.bfloat16),
            CTX,
            -distance,
        ).astype(jnp.float32)
        key_total = key_total + back[:, :width]
        value_total = value_total + back[:, width:]
    return (
        lin_dq,
        lin_dk,
        lin_dv,
        sm_dq,
        key_total.astype(jnp.bfloat16),
        value_total.astype(jnp.bfloat16),
    )


def solution(mesh):
    placed = (
        P(CTX, "head"),
        P(CTX, "head"),
        P(CTX, "head"),
        P("head"),
        P(CTX, "head"),
        P(CTX, "head"),
        P(CTX, "head"),
        P(CTX, "head"),
        P(CTX, "head"),
        P(CTX, None),
    )
    count = mesh.shape["ctx"]
    inner = INNER if count % INNER == 0 else 1
    split = jax.sharding.Mesh(
        mesh.devices.reshape(count // inner, inner, mesh.shape["head"]), CTX + ("head",)
    )
    return jax.shard_map(
        per_device,
        mesh=split,
        in_specs=placed,
        out_specs=(
            P(CTX, "head"),
            P(CTX, "head"),
            P(CTX, "head"),
            P(CTX, "head"),
            P(CTX, "head"),
            P(CTX, "head"),
        ),
        check_vma=False,
    )
```

```python
import jax
import jax.numpy as jnp
from jax import lax
from jax.sharding import PartitionSpec as P

HEAD = 128
LIN_HEADS = 16
TILE = 128
LIST = 3
SPAN = 4


RADIX = 4


def carried_in(shard, axis, join, neutral, backward):
    count = lax.axis_size(axis)
    total = shard.astype(jnp.float32)
    stride = 1
    while stride < count:
        arrived = []
        for step in range(1, RADIX):
            distance = step * stride
            if distance >= count:
                break
            if backward:
                pairs = [(i, i - distance) for i in range(distance, count)]
            else:
                pairs = [(i, i + distance) for i in range(count - distance)]
            arrived.append(lax.ppermute(total, axis, pairs))
        for part in arrived:
            total = join(total, part)
        stride *= RADIX
    return (total - shard.astype(jnp.float32)).astype(shard.dtype)


def from_behind(shard, axis, by):
    length = lax.axis_size(axis)
    pairs = [(i, i + by) for i in range(length) if 0 <= i + by < length]
    return lax.ppermute(shard, axis, pairs)


def add_states(earlier, later):
    return earlier + later


def tile_attention(query, grad, key_window, value_window, lists, shard):
    token_count, width = query.shape
    heads = width // HEAD
    tiles_dev = token_count // TILE
    window_tiles = key_window.shape[0] // TILE
    valid = lists >= 0
    local_index = jnp.where(valid, lists - (shard - SPAN) * tiles_dev, 0)
    own_index = (SPAN * tiles_dev + jnp.arange(tiles_dev, dtype=jnp.int32))[:, None]
    picked = jnp.concatenate([own_index, local_index], axis=1)
    keep = jnp.concatenate([jnp.ones((tiles_dev, 1), jnp.bool_), valid], axis=1)
    key_set = key_window.reshape(window_tiles, TILE, heads, HEAD)[picked].reshape(
        tiles_dev, (LIST + 1) * TILE, heads, HEAD
    )
    value_set = value_window.reshape(window_tiles, TILE, heads, HEAD)[picked].reshape(
        tiles_dev, (LIST + 1) * TILE, heads, HEAD
    )
    query_tiles = query.reshape(tiles_dev, TILE, heads, HEAD)
    grad_tiles = grad.reshape(tiles_dev, TILE, heads, HEAD)
    scale = HEAD ** (-0.5)
    scores = (
        jnp.einsum("athd,ashd->ahts", query_tiles, key_set, preferred_element_type=jnp.float32)
        * scale
    )
    rows_idx = jnp.arange(TILE)[:, None]
    cols_idx = jnp.arange((LIST + 1) * TILE)[None, :]
    allowed = jnp.where(cols_idx // TILE == 0, cols_idx % TILE <= rows_idx, True)
    live = jnp.repeat(keep, TILE, axis=1)
    allowed_all = allowed[None, None, :, :] & live[:, None, None, :]
    scores = jnp.where(allowed_all, scores, -jnp.inf)
    top_score = jnp.max(scores, axis=-1, keepdims=True)
    expo = jnp.exp(scores - top_score)
    probs = expo / jnp.sum(expo, axis=-1, keepdims=True)
    probs_half = probs.astype(jnp.bfloat16)
    attended = jnp.einsum(
        "ahts,ashd->athd", probs_half, value_set, preferred_element_type=jnp.float32
    )
    delta = jnp.transpose(jnp.sum(grad_tiles.astype(jnp.float32) * attended, axis=-1), (0, 2, 1))[
        ..., None
    ]
    grad_probs = jnp.einsum(
        "athd,ashd->ahts", grad_tiles, value_set, preferred_element_type=jnp.float32
    )
    grad_logits = (probs * (grad_probs - delta) * scale).astype(jnp.bfloat16)
    query_grad = (
        jnp.einsum("ahts,ashd->athd", grad_logits, key_set, preferred_element_type=jnp.float32)
        .reshape(token_count, width)
        .astype(jnp.bfloat16)
    )
    key_part = jnp.einsum(
        "ahts,athd->ashd", grad_logits, query_tiles, preferred_element_type=jnp.float32
    ).reshape(tiles_dev * (LIST + 1), TILE, width)
    value_part = jnp.einsum(
        "ahts,athd->ashd", probs_half, grad_tiles, preferred_element_type=jnp.float32
    ).reshape(tiles_dev * (LIST + 1), TILE, width)
    flat_index = picked.reshape(-1)
    key_acc = jnp.zeros((window_tiles, TILE, width), jnp.float32).at[flat_index].add(key_part)
    value_acc = jnp.zeros((window_tiles, TILE, width), jnp.float32).at[flat_index].add(value_part)
    return (query_grad, key_acc, value_acc)


def per_device(
    lin_query,
    lin_key,
    lin_value,
    norm_gain,
    lin_grad,
    sm_query,
    sm_key,
    sm_value,
    sm_grad,
    tile_lists,
):
    token_count = lin_query.shape[0]
    lin_width = lin_query.shape[1]
    heads_lin = lin_width // HEAD
    query_lin = lin_query.reshape(token_count, heads_lin, HEAD)
    key_lin = lin_key.reshape(token_count, heads_lin, HEAD)
    value_lin = lin_value.reshape(token_count, heads_lin, HEAD)
    key_value = jnp.einsum("thi,thj->hij", key_lin, value_lin, preferred_element_type=jnp.float32)
    state_low = carried_in(key_value, "ctx", add_states, jnp.zeros_like(key_value), False)
    state_half = state_low.astype(jnp.bfloat16)
    causal = jnp.tril(jnp.ones((token_count, token_count), jnp.bool_))
    attn_lin = jnp.where(
        causal[None],
        jnp.einsum("thd,shd->hts", query_lin, key_lin, preferred_element_type=jnp.float32),
        0.0,
    ).astype(jnp.bfloat16)
    output_lin = jnp.einsum(
        "hts,shd->thd", attn_lin, value_lin, preferred_element_type=jnp.float32
    ) + jnp.einsum("thi,hij->thj", query_lin, state_half, preferred_element_type=jnp.float32)
    gain_grad = norm_gain.reshape(1, heads_lin, HEAD) * lin_grad.reshape(
        token_count, heads_lin, HEAD
    ).astype(jnp.float32)
    square_sum = jnp.sum(output_lin * output_lin, axis=(1, 2))
    cross_sum = jnp.sum(gain_grad * output_lin, axis=(1, 2))
    square_sum, cross_sum = lax.psum((square_sum, cross_sum), "head")
    full_width = LIN_HEADS * HEAD
    inv_rms = lax.rsqrt(square_sum / full_width + 1e-06)[:, None, None]
    grad_out = (
        gain_grad * inv_rms - output_lin * inv_rms**3 * (cross_sum / full_width)[:, None, None]
    ).astype(jnp.bfloat16)
    adjoint_local = jnp.einsum(
        "thi,thj->hij", query_lin, grad_out, preferred_element_type=jnp.float32
    )
    adjoint_high = carried_in(adjoint_local, "ctx", add_states, jnp.zeros_like(adjoint_local), True)
    adjoint_half = adjoint_high.astype(jnp.bfloat16)
    grad_scores = jnp.where(
        causal[None],
        jnp.einsum("thd,shd->hts", grad_out, value_lin, preferred_element_type=jnp.float32),
        0.0,
    ).astype(jnp.bfloat16)
    lin_dq = jnp.einsum(
        "hts,shd->thd", grad_scores, key_lin, preferred_element_type=jnp.float32
    ) + jnp.einsum("thj,hij->thi", grad_out, state_half, preferred_element_type=jnp.float32)
    lin_dk = jnp.einsum(
        "hts,thd->shd", grad_scores, query_lin, preferred_element_type=jnp.float32
    ) + jnp.einsum("shj,hij->shi", value_lin, adjoint_half, preferred_element_type=jnp.float32)
    lin_dv = jnp.einsum(
        "hts,thd->shd", attn_lin, grad_out, preferred_element_type=jnp.float32
    ) + jnp.einsum("shi,hij->shj", key_lin, adjoint_half, preferred_element_type=jnp.float32)
    lin_dq = lin_dq.reshape(token_count, lin_width).astype(jnp.bfloat16)
    lin_dk = lin_dk.reshape(token_count, lin_width).astype(jnp.bfloat16)
    lin_dv = lin_dv.reshape(token_count, lin_width).astype(jnp.bfloat16)
    width = sm_key.shape[1]
    pair = jnp.concatenate([sm_key, sm_value], axis=1)
    arrived = [from_behind(pair, "ctx", distance) for distance in range(1, SPAN + 1)]
    key_window = jnp.concatenate(
        [arrived[SPAN - 1 - place][:, :width] for place in range(SPAN)] + [sm_key], axis=0
    )
    value_window = jnp.concatenate(
        [arrived[SPAN - 1 - place][:, width:] for place in range(SPAN)] + [sm_value], axis=0
    )
    shard = lax.axis_index("ctx")
    sm_dq, key_acc, value_acc = tile_attention(
        sm_query, sm_grad, key_window, value_window, tile_lists, shard
    )
    key_total = key_acc[SPAN]
    value_total = value_acc[SPAN]
    for distance in range(1, SPAN + 1):
        back = from_behind(
            jnp.concatenate(
                [key_acc[SPAN - distance], value_acc[SPAN - distance]], axis=1
            ).astype(jnp.bfloat16),
            "ctx",
            -distance,
        ).astype(jnp.float32)
        key_total = key_total + back[:, :width]
        value_total = value_total + back[:, width:]
    return (
        lin_dq,
        lin_dk,
        lin_dv,
        sm_dq,
        key_total.astype(jnp.bfloat16),
        value_total.astype(jnp.bfloat16),
    )


def solution(mesh):
    placed = (
        P("ctx", "head"),
        P("ctx", "head"),
        P("ctx", "head"),
        P("head"),
        P("ctx", "head"),
        P("ctx", "head"),
        P("ctx", "head"),
        P("ctx", "head"),
        P("ctx", "head"),
        P("ctx", None),
    )
    return jax.shard_map(
        per_device,
        mesh=mesh,
        in_specs=placed,
        out_specs=(
            P("ctx", "head"),
            P("ctx", "head"),
            P("ctx", "head"),
            P("ctx", "head"),
            P("ctx", "head"),
            P("ctx", "head"),
        ),
        check_vma=False,
    )
```

```python
import jax
import jax.numpy as jnp
from jax import lax
from jax.sharding import PartitionSpec as P

HEAD = 128
LIN_HEADS = 16
TILE = 128
LIST = 3
SPAN = 4


def carried_in(shard, axis, join, neutral, backward):
    count = lax.axis_size(axis)
    total = shard.astype(jnp.float32)
    distance = 1
    while distance < count:
        if backward:
            pairs = [(i, i - distance) for i in range(distance, count)]
        else:
            pairs = [(i, i + distance) for i in range(count - distance)]
        sent = lax.ppermute(total.astype(jnp.bfloat16), axis, pairs)
        total = join(total, sent.astype(jnp.float32))
        distance *= 2
    return (total - shard.astype(jnp.float32)).astype(shard.dtype)


def from_behind(shard, axis, by):
    length = lax.axis_size(axis)
    pairs = [(i, i + by) for i in range(length) if 0 <= i + by < length]
    return lax.ppermute(shard, axis, pairs)


def add_states(earlier, later):
    return earlier + later


def tile_attention(query, grad, key_window, value_window, lists, shard):
    token_count, width = query.shape
    heads = width // HEAD
    tiles_dev = token_count // TILE
    window_tiles = key_window.shape[0] // TILE
    valid = lists >= 0
    local_index = jnp.where(valid, lists - (shard - SPAN) * tiles_dev, 0)
    own_index = (SPAN * tiles_dev + jnp.arange(tiles_dev, dtype=jnp.int32))[:, None]
    picked = jnp.concatenate([own_index, local_index], axis=1)
    keep = jnp.concatenate([jnp.ones((tiles_dev, 1), jnp.bool_), valid], axis=1)
    key_set = key_window.reshape(window_tiles, TILE, heads, HEAD)[picked].reshape(
        tiles_dev, (LIST + 1) * TILE, heads, HEAD
    )
    value_set = value_window.reshape(window_tiles, TILE, heads, HEAD)[picked].reshape(
        tiles_dev, (LIST + 1) * TILE, heads, HEAD
    )
    query_tiles = query.reshape(tiles_dev, TILE, heads, HEAD)
    grad_tiles = grad.reshape(tiles_dev, TILE, heads, HEAD)
    scale = HEAD ** (-0.5)
    scores = (
        jnp.einsum("athd,ashd->ahts", query_tiles, key_set, preferred_element_type=jnp.float32)
        * scale
    )
    rows_idx = jnp.arange(TILE)[:, None]
    cols_idx = jnp.arange((LIST + 1) * TILE)[None, :]
    allowed = jnp.where(cols_idx // TILE == 0, cols_idx % TILE <= rows_idx, True)
    live = jnp.repeat(keep, TILE, axis=1)
    allowed_all = allowed[None, None, :, :] & live[:, None, None, :]
    scores = jnp.where(allowed_all, scores, -jnp.inf)
    top_score = jnp.max(scores, axis=-1, keepdims=True)
    expo = jnp.exp(scores - top_score)
    probs = expo / jnp.sum(expo, axis=-1, keepdims=True)
    probs_half = probs.astype(jnp.bfloat16)
    attended = jnp.einsum(
        "ahts,ashd->athd", probs_half, value_set, preferred_element_type=jnp.float32
    )
    delta = jnp.transpose(jnp.sum(grad_tiles.astype(jnp.float32) * attended, axis=-1), (0, 2, 1))[
        ..., None
    ]
    grad_probs = jnp.einsum(
        "athd,ashd->ahts", grad_tiles, value_set, preferred_element_type=jnp.float32
    )
    grad_logits = (probs * (grad_probs - delta) * scale).astype(jnp.bfloat16)
    query_grad = (
        jnp.einsum("ahts,ashd->athd", grad_logits, key_set, preferred_element_type=jnp.float32)
        .reshape(token_count, width)
        .astype(jnp.bfloat16)
    )
    key_part = jnp.einsum(
        "ahts,athd->ashd", grad_logits, query_tiles, preferred_element_type=jnp.float32
    ).reshape(tiles_dev * (LIST + 1), TILE, width)
    value_part = jnp.einsum(
        "ahts,athd->ashd", probs_half, grad_tiles, preferred_element_type=jnp.float32
    ).reshape(tiles_dev * (LIST + 1), TILE, width)
    flat_index = picked.reshape(-1)
    key_acc = jnp.zeros((window_tiles, TILE, width), jnp.float32).at[flat_index].add(key_part)
    value_acc = jnp.zeros((window_tiles, TILE, width), jnp.float32).at[flat_index].add(value_part)
    return (query_grad, key_acc, value_acc)


def per_device(
    lin_query,
    lin_key,
    lin_value,
    norm_gain,
    lin_grad,
    sm_query,
    sm_key,
    sm_value,
    sm_grad,
    tile_lists,
):
    token_count = lin_query.shape[0]
    lin_width = lin_query.shape[1]
    heads_lin = lin_width // HEAD
    query_lin = lin_query.reshape(token_count, heads_lin, HEAD)
    key_lin = lin_key.reshape(token_count, heads_lin, HEAD)
    value_lin = lin_value.reshape(token_count, heads_lin, HEAD)
    key_value = jnp.einsum("thi,thj->hij", key_lin, value_lin, preferred_element_type=jnp.float32)
    state_low = carried_in(key_value, "ctx", add_states, jnp.zeros_like(key_value), False)
    state_half = state_low.astype(jnp.bfloat16)
    causal = jnp.tril(jnp.ones((token_count, token_count), jnp.bool_))
    attn_lin = jnp.where(
        causal[None],
        jnp.einsum("thd,shd->hts", query_lin, key_lin, preferred_element_type=jnp.float32),
        0.0,
    ).astype(jnp.bfloat16)
    output_lin = jnp.einsum(
        "hts,shd->thd", attn_lin, value_lin, preferred_element_type=jnp.float32
    ) + jnp.einsum("thi,hij->thj", query_lin, state_half, preferred_element_type=jnp.float32)
    gain_grad = norm_gain.reshape(1, heads_lin, HEAD) * lin_grad.reshape(
        token_count, heads_lin, HEAD
    ).astype(jnp.float32)
    square_sum = jnp.sum(output_lin * output_lin, axis=(1, 2))
    cross_sum = jnp.sum(gain_grad * output_lin, axis=(1, 2))
    square_sum, cross_sum = lax.psum((square_sum, cross_sum), "head")
    full_width = LIN_HEADS * HEAD
    inv_rms = lax.rsqrt(square_sum / full_width + 1e-06)[:, None, None]
    grad_out = (
        gain_grad * inv_rms - output_lin * inv_rms**3 * (cross_sum / full_width)[:, None, None]
    ).astype(jnp.bfloat16)
    adjoint_local = jnp.einsum(
        "thi,thj->hij", query_lin, grad_out, preferred_element_type=jnp.float32
    )
    adjoint_high = carried_in(adjoint_local, "ctx", add_states, jnp.zeros_like(adjoint_local), True)
    adjoint_half = adjoint_high.astype(jnp.bfloat16)
    grad_scores = jnp.where(
        causal[None],
        jnp.einsum("thd,shd->hts", grad_out, value_lin, preferred_element_type=jnp.float32),
        0.0,
    ).astype(jnp.bfloat16)
    lin_dq = jnp.einsum(
        "hts,shd->thd", grad_scores, key_lin, preferred_element_type=jnp.float32
    ) + jnp.einsum("thj,hij->thi", grad_out, state_half, preferred_element_type=jnp.float32)
    lin_dk = jnp.einsum(
        "hts,thd->shd", grad_scores, query_lin, preferred_element_type=jnp.float32
    ) + jnp.einsum("shj,hij->shi", value_lin, adjoint_half, preferred_element_type=jnp.float32)
    lin_dv = jnp.einsum(
        "hts,thd->shd", attn_lin, grad_out, preferred_element_type=jnp.float32
    ) + jnp.einsum("shi,hij->shj", key_lin, adjoint_half, preferred_element_type=jnp.float32)
    lin_dq = lin_dq.reshape(token_count, lin_width).astype(jnp.bfloat16)
    lin_dk = lin_dk.reshape(token_count, lin_width).astype(jnp.bfloat16)
    lin_dv = lin_dv.reshape(token_count, lin_width).astype(jnp.bfloat16)
    width = sm_key.shape[1]
    pair = jnp.concatenate([sm_key, sm_value], axis=1)
    arrived = [from_behind(pair, "ctx", distance) for distance in range(1, SPAN + 1)]
    key_window = jnp.concatenate(
        [arrived[SPAN - 1 - place][:, :width] for place in range(SPAN)] + [sm_key], axis=0
    )
    value_window = jnp.concatenate(
        [arrived[SPAN - 1 - place][:, width:] for place in range(SPAN)] + [sm_value], axis=0
    )
    shard = lax.axis_index("ctx")
    sm_dq, key_acc, value_acc = tile_attention(
        sm_query, sm_grad, key_window, value_window, tile_lists, shard
    )
    key_total = key_acc[SPAN]
    value_total = value_acc[SPAN]
    for distance in range(1, SPAN + 1):
        back = from_behind(
            jnp.concatenate(
                [key_acc[SPAN - distance], value_acc[SPAN - distance]], axis=1
            ).astype(jnp.bfloat16),
            "ctx",
            -distance,
        ).astype(jnp.float32)
        key_total = key_total + back[:, :width]
        value_total = value_total + back[:, width:]
    return (
        lin_dq,
        lin_dk,
        lin_dv,
        sm_dq,
        key_total.astype(jnp.bfloat16),
        value_total.astype(jnp.bfloat16),
    )


def solution(mesh):
    placed = (
        P("ctx", "head"),
        P("ctx", "head"),
        P("ctx", "head"),
        P("head"),
        P("ctx", "head"),
        P("ctx", "head"),
        P("ctx", "head"),
        P("ctx", "head"),
        P("ctx", "head"),
        P("ctx", None),
    )
    return jax.shard_map(
        per_device,
        mesh=mesh,
        in_specs=placed,
        out_specs=(
            P("ctx", "head"),
            P("ctx", "head"),
            P("ctx", "head"),
            P("ctx", "head"),
            P("ctx", "head"),
            P("ctx", "head"),
        ),
        check_vma=False,
    )
```

```python
import jax
import jax.numpy as jnp
from jax import lax
from jax.sharding import PartitionSpec as P

HEAD = 128
LIN_HEADS = 16
TILE = 128
LIST = 3
SPAN = 4


def carried_in(shard, axis, join, neutral, backward):
    count = lax.axis_size(axis)
    total = shard.astype(jnp.float32)
    distance = 1
    while distance < count:
        if backward:
            pairs = [(i, i - distance) for i in range(distance, count)]
        else:
            pairs = [(i, i + distance) for i in range(count - distance)]
        sent = lax.ppermute(total.astype(jnp.bfloat16), axis, pairs)
        total = join(total, sent.astype(jnp.float32))
        distance *= 2
    return (total - shard.astype(jnp.float32)).astype(shard.dtype)


def from_behind(shard, axis, by):
    length = lax.axis_size(axis)
    pairs = [(i, i + by) for i in range(length) if 0 <= i + by < length]
    return lax.ppermute(shard, axis, pairs)


def add_states(earlier, later):
    return earlier + later


def tile_attention(query, grad, key_window, value_window, lists, shard):
    token_count, width = query.shape
    heads = width // HEAD
    tiles_dev = token_count // TILE
    window_tiles = key_window.shape[0] // TILE
    valid = lists >= 0
    local_index = jnp.where(valid, lists - (shard - SPAN) * tiles_dev, 0)
    own_index = (SPAN * tiles_dev + jnp.arange(tiles_dev, dtype=jnp.int32))[:, None]
    picked = jnp.concatenate([own_index, local_index], axis=1)
    keep = jnp.concatenate([jnp.ones((tiles_dev, 1), jnp.bool_), valid], axis=1)
    key_set = key_window.reshape(window_tiles, TILE, heads, HEAD)[picked].reshape(
        tiles_dev, (LIST + 1) * TILE, heads, HEAD
    )
    value_set = value_window.reshape(window_tiles, TILE, heads, HEAD)[picked].reshape(
        tiles_dev, (LIST + 1) * TILE, heads, HEAD
    )
    query_tiles = query.reshape(tiles_dev, TILE, heads, HEAD)
    grad_tiles = grad.reshape(tiles_dev, TILE, heads, HEAD)
    scale = HEAD ** (-0.5)
    scores = (
        jnp.einsum("athd,ashd->ahts", query_tiles, key_set, preferred_element_type=jnp.float32)
        * scale
    )
    rows_idx = jnp.arange(TILE)[:, None]
    cols_idx = jnp.arange((LIST + 1) * TILE)[None, :]
    allowed = jnp.where(cols_idx // TILE == 0, cols_idx % TILE <= rows_idx, True)
    live = jnp.repeat(keep, TILE, axis=1)
    allowed_all = allowed[None, None, :, :] & live[:, None, None, :]
    scores = jnp.where(allowed_all, scores, -jnp.inf)
    top_score = jnp.max(scores, axis=-1, keepdims=True)
    expo = jnp.exp(scores - top_score)
    probs = expo / jnp.sum(expo, axis=-1, keepdims=True)
    probs_half = probs.astype(jnp.bfloat16)
    attended = jnp.einsum(
        "ahts,ashd->athd", probs_half, value_set, preferred_element_type=jnp.float32
    )
    delta = jnp.transpose(jnp.sum(grad_tiles.astype(jnp.float32) * attended, axis=-1), (0, 2, 1))[
        ..., None
    ]
    grad_probs = jnp.einsum(
        "athd,ashd->ahts", grad_tiles, value_set, preferred_element_type=jnp.float32
    )
    grad_logits = (probs * (grad_probs - delta) * scale).astype(jnp.bfloat16)
    query_grad = (
        jnp.einsum("ahts,ashd->athd", grad_logits, key_set, preferred_element_type=jnp.float32)
        .reshape(token_count, width)
        .astype(jnp.bfloat16)
    )
    key_part = jnp.einsum(
        "ahts,athd->ashd", grad_logits, query_tiles, preferred_element_type=jnp.float32
    ).reshape(tiles_dev * (LIST + 1), TILE, width)
    value_part = jnp.einsum(
        "ahts,athd->ashd", probs_half, grad_tiles, preferred_element_type=jnp.float32
    ).reshape(tiles_dev * (LIST + 1), TILE, width)
    flat_index = picked.reshape(-1)
    key_acc = jnp.zeros((window_tiles, TILE, width), jnp.float32).at[flat_index].add(key_part)
    value_acc = jnp.zeros((window_tiles, TILE, width), jnp.float32).at[flat_index].add(value_part)
    return (query_grad, key_acc, value_acc)


def per_device(
    lin_query,
    lin_key,
    lin_value,
    norm_gain,
    lin_grad,
    sm_query,
    sm_key,
    sm_value,
    sm_grad,
    tile_lists,
):
    token_count = lin_query.shape[0]
    lin_width = lin_query.shape[1]
    heads_lin = lin_width // HEAD
    query_lin = lin_query.reshape(token_count, heads_lin, HEAD)
    key_lin = lin_key.reshape(token_count, heads_lin, HEAD)
    value_lin = lin_value.reshape(token_count, heads_lin, HEAD)
    key_value = jnp.einsum("thi,thj->hij", key_lin, value_lin, preferred_element_type=jnp.float32)
    state_low = carried_in(key_value, "ctx", add_states, jnp.zeros_like(key_value), False)
    state_half = state_low.astype(jnp.bfloat16)
    causal = jnp.tril(jnp.ones((token_count, token_count), jnp.bool_))
    attn_lin = jnp.where(
        causal[None],
        jnp.einsum("thd,shd->hts", query_lin, key_lin, preferred_element_type=jnp.float32),
        0.0,
    ).astype(jnp.bfloat16)
    output_lin = jnp.einsum(
        "hts,shd->thd", attn_lin, value_lin, preferred_element_type=jnp.float32
    ) + jnp.einsum("thi,hij->thj", query_lin, state_half, preferred_element_type=jnp.float32)
    gain_grad = norm_gain.reshape(1, heads_lin, HEAD) * lin_grad.reshape(
        token_count, heads_lin, HEAD
    ).astype(jnp.float32)
    square_sum = jnp.sum(output_lin * output_lin, axis=(1, 2))
    cross_sum = jnp.sum(gain_grad * output_lin, axis=(1, 2))
    square_sum, cross_sum = lax.psum((square_sum, cross_sum), "head")
    full_width = LIN_HEADS * HEAD
    inv_rms = lax.rsqrt(square_sum / full_width + 1e-06)[:, None, None]
    grad_out = (
        gain_grad * inv_rms - output_lin * inv_rms**3 * (cross_sum / full_width)[:, None, None]
    ).astype(jnp.bfloat16)
    adjoint_local = jnp.einsum(
        "thi,thj->hij", query_lin, grad_out, preferred_element_type=jnp.float32
    )
    adjoint_high = carried_in(adjoint_local, "ctx", add_states, jnp.zeros_like(adjoint_local), True)
    adjoint_half = adjoint_high.astype(jnp.bfloat16)
    grad_scores = jnp.where(
        causal[None],
        jnp.einsum("thd,shd->hts", grad_out, value_lin, preferred_element_type=jnp.float32),
        0.0,
    ).astype(jnp.bfloat16)
    lin_dq = jnp.einsum(
        "hts,shd->thd", grad_scores, key_lin, preferred_element_type=jnp.float32
    ) + jnp.einsum("thj,hij->thi", grad_out, state_half, preferred_element_type=jnp.float32)
    lin_dk = jnp.einsum(
        "hts,thd->shd", grad_scores, query_lin, preferred_element_type=jnp.float32
    ) + jnp.einsum("shj,hij->shi", value_lin, adjoint_half, preferred_element_type=jnp.float32)
    lin_dv = jnp.einsum(
        "hts,thd->shd", attn_lin, grad_out, preferred_element_type=jnp.float32
    ) + jnp.einsum("shi,hij->shj", key_lin, adjoint_half, preferred_element_type=jnp.float32)
    lin_dq = lin_dq.reshape(token_count, lin_width).astype(jnp.bfloat16)
    lin_dk = lin_dk.reshape(token_count, lin_width).astype(jnp.bfloat16)
    lin_dv = lin_dv.reshape(token_count, lin_width).astype(jnp.bfloat16)
    width = sm_key.shape[1]
    pair = jnp.concatenate([sm_key, sm_value], axis=1)
    arrived = []
    moving = pair
    for distance in range(1, SPAN + 1):
        moving = from_behind(moving, "ctx", 1)
        arrived.append(moving)
    key_window = jnp.concatenate(
        [arrived[SPAN - 1 - place][:, :width] for place in range(SPAN)] + [sm_key], axis=0
    )
    value_window = jnp.concatenate(
        [arrived[SPAN - 1 - place][:, width:] for place in range(SPAN)] + [sm_value], axis=0
    )
    shard = lax.axis_index("ctx")
    sm_dq, key_acc, value_acc = tile_attention(
        sm_query, sm_grad, key_window, value_window, tile_lists, shard
    )
    key_total = key_acc[SPAN]
    value_total = value_acc[SPAN]
    owed = None
    for distance in range(SPAN, 0, -1):
        term = jnp.concatenate(
            [key_acc[SPAN - distance], value_acc[SPAN - distance]], axis=1
        ).astype(jnp.bfloat16).astype(jnp.float32)
        owed = term if owed is None else owed + term
        owed = from_behind(owed.astype(jnp.bfloat16), "ctx", -1).astype(jnp.float32)
    key_total = key_total + owed[:, :width]
    value_total = value_total + owed[:, width:]
    return (
        lin_dq,
        lin_dk,
        lin_dv,
        sm_dq,
        key_total.astype(jnp.bfloat16),
        value_total.astype(jnp.bfloat16),
    )


def solution(mesh):
    placed = (
        P("ctx", "head"),
        P("ctx", "head"),
        P("ctx", "head"),
        P("head"),
        P("ctx", "head"),
        P("ctx", "head"),
        P("ctx", "head"),
        P("ctx", "head"),
        P("ctx", "head"),
        P("ctx", None),
    )
    return jax.shard_map(
        per_device,
        mesh=mesh,
        in_specs=placed,
        out_specs=(
            P("ctx", "head"),
            P("ctx", "head"),
            P("ctx", "head"),
            P("ctx", "head"),
            P("ctx", "head"),
            P("ctx", "head"),
        ),
        check_vma=False,
    )
```

```python
import jax
import jax.numpy as jnp
from jax import lax
from jax.sharding import PartitionSpec as P

HEAD = 128
LIN_HEADS = 16
TILE = 128
LIST = 3
SPAN = 4


def carried_in(shard, axis, join, neutral, backward):
    count = lax.axis_size(axis)
    total = shard.astype(jnp.float32)
    distance = 1
    while distance < count:
        if backward:
            pairs = [(i, i - distance) for i in range(distance, count)]
        else:
            pairs = [(i, i + distance) for i in range(count - distance)]
        sent = lax.ppermute(total.astype(jnp.bfloat16), axis, pairs)
        total = join(total, sent.astype(jnp.float32))
        distance *= 2
    return (total - shard.astype(jnp.float32)).astype(shard.dtype)


def from_behind(shard, axis, by):
    length = lax.axis_size(axis)
    pairs = [(i, i + by) for i in range(length) if 0 <= i + by < length]
    return lax.ppermute(shard, axis, pairs)


def add_states(earlier, later):
    return earlier + later


def tile_attention(query, grad, key_window, value_window, lists, shard):
    token_count, width = query.shape
    heads = width // HEAD
    tiles_dev = token_count // TILE
    window_tiles = key_window.shape[0] // TILE
    valid = lists >= 0
    local_index = jnp.where(valid, lists - (shard - SPAN) * tiles_dev, 0)
    own_index = (SPAN * tiles_dev + jnp.arange(tiles_dev, dtype=jnp.int32))[:, None]
    picked = jnp.concatenate([own_index, local_index], axis=1)
    keep = jnp.concatenate([jnp.ones((tiles_dev, 1), jnp.bool_), valid], axis=1)
    key_set = key_window.reshape(window_tiles, TILE, heads, HEAD)[picked].reshape(
        tiles_dev, (LIST + 1) * TILE, heads, HEAD
    )
    value_set = value_window.reshape(window_tiles, TILE, heads, HEAD)[picked].reshape(
        tiles_dev, (LIST + 1) * TILE, heads, HEAD
    )
    query_tiles = query.reshape(tiles_dev, TILE, heads, HEAD)
    grad_tiles = grad.reshape(tiles_dev, TILE, heads, HEAD)
    scale = HEAD ** (-0.5)
    scores = (
        jnp.einsum("athd,ashd->ahts", query_tiles, key_set, preferred_element_type=jnp.float32)
        * scale
    )
    rows_idx = jnp.arange(TILE)[:, None]
    cols_idx = jnp.arange((LIST + 1) * TILE)[None, :]
    allowed = jnp.where(cols_idx // TILE == 0, cols_idx % TILE <= rows_idx, True)
    live = jnp.repeat(keep, TILE, axis=1)
    allowed_all = allowed[None, None, :, :] & live[:, None, None, :]
    scores = jnp.where(allowed_all, scores, -jnp.inf)
    top_score = jnp.max(scores, axis=-1, keepdims=True)
    expo = jnp.exp(scores - top_score)
    probs = expo / jnp.sum(expo, axis=-1, keepdims=True)
    probs_half = probs.astype(jnp.bfloat16)
    attended = jnp.einsum(
        "ahts,ashd->athd", probs_half, value_set, preferred_element_type=jnp.float32
    )
    delta = jnp.transpose(jnp.sum(grad_tiles.astype(jnp.float32) * attended, axis=-1), (0, 2, 1))[
        ..., None
    ]
    grad_probs = jnp.einsum(
        "athd,ashd->ahts", grad_tiles, value_set, preferred_element_type=jnp.float32
    )
    grad_logits = (probs * (grad_probs - delta) * scale).astype(jnp.bfloat16)
    query_grad = (
        jnp.einsum("ahts,ashd->athd", grad_logits, key_set, preferred_element_type=jnp.float32)
        .reshape(token_count, width)
        .astype(jnp.bfloat16)
    )
    key_part = jnp.einsum(
        "ahts,athd->ashd", grad_logits, query_tiles, preferred_element_type=jnp.float32
    ).reshape(tiles_dev * (LIST + 1), TILE, width)
    value_part = jnp.einsum(
        "ahts,athd->ashd", probs_half, grad_tiles, preferred_element_type=jnp.float32
    ).reshape(tiles_dev * (LIST + 1), TILE, width)
    flat_index = picked.reshape(-1)
    key_acc = jnp.zeros((window_tiles, TILE, width), jnp.float32).at[flat_index].add(key_part)
    value_acc = jnp.zeros((window_tiles, TILE, width), jnp.float32).at[flat_index].add(value_part)
    return (query_grad, key_acc, value_acc)


def per_device(
    lin_query,
    lin_key,
    lin_value,
    norm_gain,
    lin_grad,
    sm_query,
    sm_key,
    sm_value,
    sm_grad,
    tile_lists,
):
    token_count = lin_query.shape[0]
    lin_width = lin_query.shape[1]
    heads_lin = lin_width // HEAD
    query_lin = lin_query.reshape(token_count, heads_lin, HEAD)
    key_lin = lin_key.reshape(token_count, heads_lin, HEAD)
    value_lin = lin_value.reshape(token_count, heads_lin, HEAD)
    key_value = jnp.einsum("thi,thj->hij", key_lin, value_lin, preferred_element_type=jnp.float32)
    state_low = carried_in(key_value, "ctx", add_states, jnp.zeros_like(key_value), False)
    state_half = state_low.astype(jnp.bfloat16)
    causal = jnp.tril(jnp.ones((token_count, token_count), jnp.bool_))
    attn_lin = jnp.where(
        causal[None],
        jnp.einsum("thd,shd->hts", query_lin, key_lin, preferred_element_type=jnp.float32),
        0.0,
    ).astype(jnp.bfloat16)
    output_lin = jnp.einsum(
        "hts,shd->thd", attn_lin, value_lin, preferred_element_type=jnp.float32
    ) + jnp.einsum("thi,hij->thj", query_lin, state_half, preferred_element_type=jnp.float32)
    gain_grad = norm_gain.reshape(1, heads_lin, HEAD) * lin_grad.reshape(
        token_count, heads_lin, HEAD
    ).astype(jnp.float32)
    square_sum = jnp.sum(output_lin * output_lin, axis=(1, 2))
    cross_sum = jnp.sum(gain_grad * output_lin, axis=(1, 2))
    sums = jnp.stack([square_sum, cross_sum])
    heads_dev = lax.axis_size("head")
    step = 1
    while step < heads_dev:
        sums = sums + lax.ppermute(sums, "head", [(i, i ^ step) for i in range(heads_dev)])
        step *= 2
    square_sum, cross_sum = sums[0], sums[1]
    full_width = LIN_HEADS * HEAD
    inv_rms = lax.rsqrt(square_sum / full_width + 1e-06)[:, None, None]
    grad_out = (
        gain_grad * inv_rms - output_lin * inv_rms**3 * (cross_sum / full_width)[:, None, None]
    ).astype(jnp.bfloat16)
    adjoint_local = jnp.einsum(
        "thi,thj->hij", query_lin, grad_out, preferred_element_type=jnp.float32
    )
    adjoint_high = carried_in(adjoint_local, "ctx", add_states, jnp.zeros_like(adjoint_local), True)
    adjoint_half = adjoint_high.astype(jnp.bfloat16)
    grad_scores = jnp.where(
        causal[None],
        jnp.einsum("thd,shd->hts", grad_out, value_lin, preferred_element_type=jnp.float32),
        0.0,
    ).astype(jnp.bfloat16)
    lin_dq = jnp.einsum(
        "hts,shd->thd", grad_scores, key_lin, preferred_element_type=jnp.float32
    ) + jnp.einsum("thj,hij->thi", grad_out, state_half, preferred_element_type=jnp.float32)
    lin_dk = jnp.einsum(
        "hts,thd->shd", grad_scores, query_lin, preferred_element_type=jnp.float32
    ) + jnp.einsum("shj,hij->shi", value_lin, adjoint_half, preferred_element_type=jnp.float32)
    lin_dv = jnp.einsum(
        "hts,thd->shd", attn_lin, grad_out, preferred_element_type=jnp.float32
    ) + jnp.einsum("shi,hij->shj", key_lin, adjoint_half, preferred_element_type=jnp.float32)
    lin_dq = lin_dq.reshape(token_count, lin_width).astype(jnp.bfloat16)
    lin_dk = lin_dk.reshape(token_count, lin_width).astype(jnp.bfloat16)
    lin_dv = lin_dv.reshape(token_count, lin_width).astype(jnp.bfloat16)
    width = sm_key.shape[1]
    pair = jnp.concatenate([sm_key, sm_value], axis=1)
    arrived = []
    moving = pair
    for distance in range(1, SPAN + 1):
        moving = from_behind(moving, "ctx", 1)
        arrived.append(moving)
    key_window = jnp.concatenate(
        [arrived[SPAN - 1 - place][:, :width] for place in range(SPAN)] + [sm_key], axis=0
    )
    value_window = jnp.concatenate(
        [arrived[SPAN - 1 - place][:, width:] for place in range(SPAN)] + [sm_value], axis=0
    )
    shard = lax.axis_index("ctx")
    sm_dq, key_acc, value_acc = tile_attention(
        sm_query, sm_grad, key_window, value_window, tile_lists, shard
    )
    key_total = key_acc[SPAN]
    value_total = value_acc[SPAN]
    owed = None
    for distance in range(SPAN, 0, -1):
        term = jnp.concatenate(
            [key_acc[SPAN - distance], value_acc[SPAN - distance]], axis=1
        ).astype(jnp.bfloat16).astype(jnp.float32)
        owed = term if owed is None else owed + term
        owed = from_behind(owed.astype(jnp.bfloat16), "ctx", -1).astype(jnp.float32)
    key_total = key_total + owed[:, :width]
    value_total = value_total + owed[:, width:]
    return (
        lin_dq,
        lin_dk,
        lin_dv,
        sm_dq,
        key_total.astype(jnp.bfloat16),
        value_total.astype(jnp.bfloat16),
    )


def solution(mesh):
    placed = (
        P("ctx", "head"),
        P("ctx", "head"),
        P("ctx", "head"),
        P("head"),
        P("ctx", "head"),
        P("ctx", "head"),
        P("ctx", "head"),
        P("ctx", "head"),
        P("ctx", "head"),
        P("ctx", None),
    )
    return jax.shard_map(
        per_device,
        mesh=mesh,
        in_specs=placed,
        out_specs=(
            P("ctx", "head"),
            P("ctx", "head"),
            P("ctx", "head"),
            P("ctx", "head"),
            P("ctx", "head"),
            P("ctx", "head"),
        ),
        check_vma=False,
    )
```

```python
import math

import jax
import jax.numpy as jnp
from jax import lax
from jax.sharding import PartitionSpec as P

HEAD = 128
LIN_HEADS = 16
TILE = 128
LIST = 3
SPAN = 4


PLAN = (4, 2, 2, 2, 4)


def carried_in(shard, axis, join, neutral, backward):
    count = lax.axis_size(axis)
    plan = PLAN
    if math.prod(plan) != count:
        plan = (2,) * max(1, (count - 1).bit_length())
    total = shard.astype(jnp.float32)
    stride = 1
    for radix in plan:
        arrived = []
        for step in range(1, radix):
            distance = step * stride
            if distance >= count:
                break
            if backward:
                pairs = [(i, i - distance) for i in range(distance, count)]
            else:
                pairs = [(i, i + distance) for i in range(count - distance)]
            arrived.append(lax.ppermute(total.astype(jnp.bfloat16), axis, pairs))
        for part in arrived:
            total = join(total, part.astype(jnp.float32))
        stride *= radix
    return (total - shard.astype(jnp.float32)).astype(shard.dtype)


def from_behind(shard, axis, by):
    length = lax.axis_size(axis)
    pairs = [(i, i + by) for i in range(length) if 0 <= i + by < length]
    return lax.ppermute(shard, axis, pairs)


def add_states(earlier, later):
    return earlier + later


def tile_attention(query, grad, key_window, value_window, lists, shard):
    token_count, width = query.shape
    heads = width // HEAD
    tiles_dev = token_count // TILE
    window_tiles = key_window.shape[0] // TILE
    valid = lists >= 0
    local_index = jnp.where(valid, lists - (shard - SPAN) * tiles_dev, 0)
    own_index = (SPAN * tiles_dev + jnp.arange(tiles_dev, dtype=jnp.int32))[:, None]
    picked = jnp.concatenate([own_index, local_index], axis=1)
    keep = jnp.concatenate([jnp.ones((tiles_dev, 1), jnp.bool_), valid], axis=1)
    key_set = key_window.reshape(window_tiles, TILE, heads, HEAD)[picked].reshape(
        tiles_dev, (LIST + 1) * TILE, heads, HEAD
    )
    value_set = value_window.reshape(window_tiles, TILE, heads, HEAD)[picked].reshape(
        tiles_dev, (LIST + 1) * TILE, heads, HEAD
    )
    query_tiles = query.reshape(tiles_dev, TILE, heads, HEAD)
    grad_tiles = grad.reshape(tiles_dev, TILE, heads, HEAD)
    scale = HEAD ** (-0.5)
    scores = (
        jnp.einsum("athd,ashd->ahts", query_tiles, key_set, preferred_element_type=jnp.float32)
        * scale
    )
    rows_idx = jnp.arange(TILE)[:, None]
    cols_idx = jnp.arange((LIST + 1) * TILE)[None, :]
    allowed = jnp.where(cols_idx // TILE == 0, cols_idx % TILE <= rows_idx, True)
    live = jnp.repeat(keep, TILE, axis=1)
    allowed_all = allowed[None, None, :, :] & live[:, None, None, :]
    scores = jnp.where(allowed_all, scores, -jnp.inf)
    top_score = jnp.max(scores, axis=-1, keepdims=True)
    expo = jnp.exp(scores - top_score)
    probs = expo / jnp.sum(expo, axis=-1, keepdims=True)
    probs_half = probs.astype(jnp.bfloat16)
    attended = jnp.einsum(
        "ahts,ashd->athd", probs_half, value_set, preferred_element_type=jnp.float32
    )
    delta = jnp.transpose(jnp.sum(grad_tiles.astype(jnp.float32) * attended, axis=-1), (0, 2, 1))[
        ..., None
    ]
    grad_probs = jnp.einsum(
        "athd,ashd->ahts", grad_tiles, value_set, preferred_element_type=jnp.float32
    )
    grad_logits = (probs * (grad_probs - delta) * scale).astype(jnp.bfloat16)
    query_grad = (
        jnp.einsum("ahts,ashd->athd", grad_logits, key_set, preferred_element_type=jnp.float32)
        .reshape(token_count, width)
        .astype(jnp.bfloat16)
    )
    key_part = jnp.einsum(
        "ahts,athd->ashd", grad_logits, query_tiles, preferred_element_type=jnp.float32
    ).reshape(tiles_dev * (LIST + 1), TILE, width)
    value_part = jnp.einsum(
        "ahts,athd->ashd", probs_half, grad_tiles, preferred_element_type=jnp.float32
    ).reshape(tiles_dev * (LIST + 1), TILE, width)
    flat_index = picked.reshape(-1)
    key_acc = jnp.zeros((window_tiles, TILE, width), jnp.float32).at[flat_index].add(key_part)
    value_acc = jnp.zeros((window_tiles, TILE, width), jnp.float32).at[flat_index].add(value_part)
    return (query_grad, key_acc, value_acc)


def per_device(
    lin_query,
    lin_key,
    lin_value,
    norm_gain,
    lin_grad,
    sm_query,
    sm_key,
    sm_value,
    sm_grad,
    tile_lists,
):
    token_count = lin_query.shape[0]
    lin_width = lin_query.shape[1]
    heads_lin = lin_width // HEAD
    query_lin = lin_query.reshape(token_count, heads_lin, HEAD)
    key_lin = lin_key.reshape(token_count, heads_lin, HEAD)
    value_lin = lin_value.reshape(token_count, heads_lin, HEAD)
    key_value = jnp.einsum("thi,thj->hij", key_lin, value_lin, preferred_element_type=jnp.float32)
    state_low = carried_in(key_value, "ctx", add_states, jnp.zeros_like(key_value), False)
    state_half = state_low.astype(jnp.bfloat16)
    causal = jnp.tril(jnp.ones((token_count, token_count), jnp.bool_))
    attn_lin = jnp.where(
        causal[None],
        jnp.einsum("thd,shd->hts", query_lin, key_lin, preferred_element_type=jnp.float32),
        0.0,
    ).astype(jnp.bfloat16)
    output_lin = jnp.einsum(
        "hts,shd->thd", attn_lin, value_lin, preferred_element_type=jnp.float32
    ) + jnp.einsum("thi,hij->thj", query_lin, state_half, preferred_element_type=jnp.float32)
    gain_grad = norm_gain.reshape(1, heads_lin, HEAD) * lin_grad.reshape(
        token_count, heads_lin, HEAD
    ).astype(jnp.float32)
    square_sum = jnp.sum(output_lin * output_lin, axis=(1, 2))
    cross_sum = jnp.sum(gain_grad * output_lin, axis=(1, 2))
    sums = jnp.stack([square_sum, cross_sum])
    heads_dev = lax.axis_size("head")
    step = 1
    while step < heads_dev:
        sums = sums + lax.ppermute(sums, "head", [(i, i ^ step) for i in range(heads_dev)])
        step *= 2
    square_sum, cross_sum = sums[0], sums[1]
    full_width = LIN_HEADS * HEAD
    inv_rms = lax.rsqrt(square_sum / full_width + 1e-06)[:, None, None]
    grad_out = (
        gain_grad * inv_rms - output_lin * inv_rms**3 * (cross_sum / full_width)[:, None, None]
    ).astype(jnp.bfloat16)
    adjoint_local = jnp.einsum(
        "thi,thj->hij", query_lin, grad_out, preferred_element_type=jnp.float32
    )
    adjoint_high = carried_in(adjoint_local, "ctx", add_states, jnp.zeros_like(adjoint_local), True)
    adjoint_half = adjoint_high.astype(jnp.bfloat16)
    grad_scores = jnp.where(
        causal[None],
        jnp.einsum("thd,shd->hts", grad_out, value_lin, preferred_element_type=jnp.float32),
        0.0,
    ).astype(jnp.bfloat16)
    lin_dq = jnp.einsum(
        "hts,shd->thd", grad_scores, key_lin, preferred_element_type=jnp.float32
    ) + jnp.einsum("thj,hij->thi", grad_out, state_half, preferred_element_type=jnp.float32)
    lin_dk = jnp.einsum(
        "hts,thd->shd", grad_scores, query_lin, preferred_element_type=jnp.float32
    ) + jnp.einsum("shj,hij->shi", value_lin, adjoint_half, preferred_element_type=jnp.float32)
    lin_dv = jnp.einsum(
        "hts,thd->shd", attn_lin, grad_out, preferred_element_type=jnp.float32
    ) + jnp.einsum("shi,hij->shj", key_lin, adjoint_half, preferred_element_type=jnp.float32)
    lin_dq = lin_dq.reshape(token_count, lin_width).astype(jnp.bfloat16)
    lin_dk = lin_dk.reshape(token_count, lin_width).astype(jnp.bfloat16)
    lin_dv = lin_dv.reshape(token_count, lin_width).astype(jnp.bfloat16)
    width = sm_key.shape[1]
    pair = jnp.concatenate([sm_key, sm_value], axis=1)
    arrived = []
    moving = pair
    for distance in range(1, SPAN + 1):
        moving = from_behind(moving, "ctx", 1)
        arrived.append(moving)
    key_window = jnp.concatenate(
        [arrived[SPAN - 1 - place][:, :width] for place in range(SPAN)] + [sm_key], axis=0
    )
    value_window = jnp.concatenate(
        [arrived[SPAN - 1 - place][:, width:] for place in range(SPAN)] + [sm_value], axis=0
    )
    shard = lax.axis_index("ctx")
    sm_dq, key_acc, value_acc = tile_attention(
        sm_query, sm_grad, key_window, value_window, tile_lists, shard
    )
    key_total = key_acc[SPAN]
    value_total = value_acc[SPAN]
    owed = None
    for distance in range(SPAN, 0, -1):
        term = jnp.concatenate(
            [key_acc[SPAN - distance], value_acc[SPAN - distance]], axis=1
        ).astype(jnp.bfloat16).astype(jnp.float32)
        owed = term if owed is None else owed + term
        owed = from_behind(owed.astype(jnp.bfloat16), "ctx", -1).astype(jnp.float32)
    key_total = key_total + owed[:, :width]
    value_total = value_total + owed[:, width:]
    return (
        lin_dq,
        lin_dk,
        lin_dv,
        sm_dq,
        key_total.astype(jnp.bfloat16),
        value_total.astype(jnp.bfloat16),
    )


def solution(mesh):
    placed = (
        P("ctx", "head"),
        P("ctx", "head"),
        P("ctx", "head"),
        P("head"),
        P("ctx", "head"),
        P("ctx", "head"),
        P("ctx", "head"),
        P("ctx", "head"),
        P("ctx", "head"),
        P("ctx", None),
    )
    return jax.shard_map(
        per_device,
        mesh=mesh,
        in_specs=placed,
        out_specs=(
            P("ctx", "head"),
            P("ctx", "head"),
            P("ctx", "head"),
            P("ctx", "head"),
            P("ctx", "head"),
            P("ctx", "head"),
        ),
        check_vma=False,
    )
```

```python
import math

import jax
import jax.numpy as jnp
from jax import lax
from jax.sharding import PartitionSpec as P

HEAD = 128
LIN_HEADS = 16
TILE = 128
LIST = 3
SPAN = 4


CTX = ("outer", "inner")
INNER = 8
PLAN = (4, 4)


def scan_over(total, axis, backward):
    count = lax.axis_size(axis)
    plan = PLAN
    if math.prod(plan) != count:
        plan = (2,) * max(1, (count - 1).bit_length())
    own = total
    stride = 1
    for radix in plan:
        arrived = []
        for step in range(1, radix):
            distance = step * stride
            if distance >= count:
                break
            if backward:
                pairs = [(i, i - distance) for i in range(distance, count)]
            else:
                pairs = [(i, i + distance) for i in range(count - distance)]
            arrived.append(lax.ppermute(total.astype(jnp.bfloat16), axis, pairs))
        for part in arrived:
            total = total + part.astype(jnp.float32)
        stride *= radix
    return total - own


def carried_in(shard, backward):
    members = lax.axis_size("inner")
    slices = shard.astype(jnp.bfloat16).reshape(members, -1)
    mine = lax.all_to_all(slices, "inner", 0, 0, tiled=True).astype(jnp.float32)
    if backward:
        within = jnp.flip(jnp.cumsum(jnp.flip(mine, 0), axis=0), 0) - mine
    else:
        within = jnp.cumsum(mine, axis=0) - mine
    group = jnp.sum(mine, axis=0)
    earlier = scan_over(group, "outer", backward)
    states = (within + earlier[None]).astype(jnp.bfloat16)
    back = lax.all_to_all(states, "inner", 0, 0, tiled=True)
    return back.reshape(shard.shape).astype(shard.dtype)


def from_behind(shard, axis, by):
    length = lax.axis_size(axis)
    pairs = [(i, i + by) for i in range(length) if 0 <= i + by < length]
    return lax.ppermute(shard, axis, pairs)


def add_states(earlier, later):
    return earlier + later


def tile_attention(query, grad, key_window, value_window, lists, shard):
    token_count, width = query.shape
    heads = width // HEAD
    tiles_dev = token_count // TILE
    window_tiles = key_window.shape[0] // TILE
    valid = lists >= 0
    local_index = jnp.where(valid, lists - (shard - SPAN) * tiles_dev, 0)
    own_index = (SPAN * tiles_dev + jnp.arange(tiles_dev, dtype=jnp.int32))[:, None]
    picked = jnp.concatenate([own_index, local_index], axis=1)
    keep = jnp.concatenate([jnp.ones((tiles_dev, 1), jnp.bool_), valid], axis=1)
    key_set = key_window.reshape(window_tiles, TILE, heads, HEAD)[picked].reshape(
        tiles_dev, (LIST + 1) * TILE, heads, HEAD
    )
    value_set = value_window.reshape(window_tiles, TILE, heads, HEAD)[picked].reshape(
        tiles_dev, (LIST + 1) * TILE, heads, HEAD
    )
    query_tiles = query.reshape(tiles_dev, TILE, heads, HEAD)
    grad_tiles = grad.reshape(tiles_dev, TILE, heads, HEAD)
    scale = HEAD ** (-0.5)
    scores = (
        jnp.einsum("athd,ashd->ahts", query_tiles, key_set, preferred_element_type=jnp.float32)
        * scale
    )
    rows_idx = jnp.arange(TILE)[:, None]
    cols_idx = jnp.arange((LIST + 1) * TILE)[None, :]
    allowed = jnp.where(cols_idx // TILE == 0, cols_idx % TILE <= rows_idx, True)
    live = jnp.repeat(keep, TILE, axis=1)
    allowed_all = allowed[None, None, :, :] & live[:, None, None, :]
    scores = jnp.where(allowed_all, scores, -jnp.inf)
    top_score = jnp.max(scores, axis=-1, keepdims=True)
    expo = jnp.exp(scores - top_score)
    probs = expo / jnp.sum(expo, axis=-1, keepdims=True)
    probs_half = probs.astype(jnp.bfloat16)
    attended = jnp.einsum(
        "ahts,ashd->athd", probs_half, value_set, preferred_element_type=jnp.float32
    )
    delta = jnp.transpose(jnp.sum(grad_tiles.astype(jnp.float32) * attended, axis=-1), (0, 2, 1))[
        ..., None
    ]
    grad_probs = jnp.einsum(
        "athd,ashd->ahts", grad_tiles, value_set, preferred_element_type=jnp.float32
    )
    grad_logits = (probs * (grad_probs - delta) * scale).astype(jnp.bfloat16)
    query_grad = (
        jnp.einsum("ahts,ashd->athd", grad_logits, key_set, preferred_element_type=jnp.float32)
        .reshape(token_count, width)
        .astype(jnp.bfloat16)
    )
    key_part = jnp.einsum(
        "ahts,athd->ashd", grad_logits, query_tiles, preferred_element_type=jnp.float32
    ).reshape(tiles_dev * (LIST + 1), TILE, width)
    value_part = jnp.einsum(
        "ahts,athd->ashd", probs_half, grad_tiles, preferred_element_type=jnp.float32
    ).reshape(tiles_dev * (LIST + 1), TILE, width)
    flat_index = picked.reshape(-1)
    key_acc = jnp.zeros((window_tiles, TILE, width), jnp.float32).at[flat_index].add(key_part)
    value_acc = jnp.zeros((window_tiles, TILE, width), jnp.float32).at[flat_index].add(value_part)
    return (query_grad, key_acc, value_acc)


def per_device(
    lin_query,
    lin_key,
    lin_value,
    norm_gain,
    lin_grad,
    sm_query,
    sm_key,
    sm_value,
    sm_grad,
    tile_lists,
):
    token_count = lin_query.shape[0]
    lin_width = lin_query.shape[1]
    heads_lin = lin_width // HEAD
    query_lin = lin_query.reshape(token_count, heads_lin, HEAD)
    key_lin = lin_key.reshape(token_count, heads_lin, HEAD)
    value_lin = lin_value.reshape(token_count, heads_lin, HEAD)
    key_value = jnp.einsum("thi,thj->hij", key_lin, value_lin, preferred_element_type=jnp.float32)
    state_low = carried_in(key_value, False)
    state_half = state_low.astype(jnp.bfloat16)
    causal = jnp.tril(jnp.ones((token_count, token_count), jnp.bool_))
    attn_lin = jnp.where(
        causal[None],
        jnp.einsum("thd,shd->hts", query_lin, key_lin, preferred_element_type=jnp.float32),
        0.0,
    ).astype(jnp.bfloat16)
    output_lin = jnp.einsum(
        "hts,shd->thd", attn_lin, value_lin, preferred_element_type=jnp.float32
    ) + jnp.einsum("thi,hij->thj", query_lin, state_half, preferred_element_type=jnp.float32)
    gain_grad = norm_gain.reshape(1, heads_lin, HEAD) * lin_grad.reshape(
        token_count, heads_lin, HEAD
    ).astype(jnp.float32)
    square_sum = jnp.sum(output_lin * output_lin, axis=(1, 2))
    cross_sum = jnp.sum(gain_grad * output_lin, axis=(1, 2))
    sums = jnp.stack([square_sum, cross_sum])
    heads_dev = lax.axis_size("head")
    step = 1
    while step < heads_dev:
        sums = sums + lax.ppermute(sums, "head", [(i, i ^ step) for i in range(heads_dev)])
        step *= 2
    square_sum, cross_sum = sums[0], sums[1]
    full_width = LIN_HEADS * HEAD
    inv_rms = lax.rsqrt(square_sum / full_width + 1e-06)[:, None, None]
    grad_out = (
        gain_grad * inv_rms - output_lin * inv_rms**3 * (cross_sum / full_width)[:, None, None]
    ).astype(jnp.bfloat16)
    adjoint_local = jnp.einsum(
        "thi,thj->hij", query_lin, grad_out, preferred_element_type=jnp.float32
    )
    adjoint_high = carried_in(adjoint_local, True)
    adjoint_half = adjoint_high.astype(jnp.bfloat16)
    grad_scores = jnp.where(
        causal[None],
        jnp.einsum("thd,shd->hts", grad_out, value_lin, preferred_element_type=jnp.float32),
        0.0,
    ).astype(jnp.bfloat16)
    lin_dq = jnp.einsum(
        "hts,shd->thd", grad_scores, key_lin, preferred_element_type=jnp.float32
    ) + jnp.einsum("thj,hij->thi", grad_out, state_half, preferred_element_type=jnp.float32)
    lin_dk = jnp.einsum(
        "hts,thd->shd", grad_scores, query_lin, preferred_element_type=jnp.float32
    ) + jnp.einsum("shj,hij->shi", value_lin, adjoint_half, preferred_element_type=jnp.float32)
    lin_dv = jnp.einsum(
        "hts,thd->shd", attn_lin, grad_out, preferred_element_type=jnp.float32
    ) + jnp.einsum("shi,hij->shj", key_lin, adjoint_half, preferred_element_type=jnp.float32)
    lin_dq = lin_dq.reshape(token_count, lin_width).astype(jnp.bfloat16)
    lin_dk = lin_dk.reshape(token_count, lin_width).astype(jnp.bfloat16)
    lin_dv = lin_dv.reshape(token_count, lin_width).astype(jnp.bfloat16)
    width = sm_key.shape[1]
    pair = jnp.concatenate([sm_key, sm_value], axis=1)
    arrived = []
    moving = pair
    for distance in range(1, SPAN + 1):
        moving = from_behind(moving, CTX, 1)
        arrived.append(moving)
    key_window = jnp.concatenate(
        [arrived[SPAN - 1 - place][:, :width] for place in range(SPAN)] + [sm_key], axis=0
    )
    value_window = jnp.concatenate(
        [arrived[SPAN - 1 - place][:, width:] for place in range(SPAN)] + [sm_value], axis=0
    )
    shard = lax.axis_index(CTX)
    sm_dq, key_acc, value_acc = tile_attention(
        sm_query, sm_grad, key_window, value_window, tile_lists, shard
    )
    key_total = key_acc[SPAN]
    value_total = value_acc[SPAN]
    owed = None
    for distance in range(SPAN, 0, -1):
        term = jnp.concatenate(
            [key_acc[SPAN - distance], value_acc[SPAN - distance]], axis=1
        ).astype(jnp.bfloat16).astype(jnp.float32)
        owed = term if owed is None else owed + term
        owed = from_behind(owed.astype(jnp.bfloat16), CTX, -1).astype(jnp.float32)
    key_total = key_total + owed[:, :width]
    value_total = value_total + owed[:, width:]
    return (
        lin_dq,
        lin_dk,
        lin_dv,
        sm_dq,
        key_total.astype(jnp.bfloat16),
        value_total.astype(jnp.bfloat16),
    )


def solution(mesh):
    placed = (
        P(CTX, "head"),
        P(CTX, "head"),
        P(CTX, "head"),
        P("head"),
        P(CTX, "head"),
        P(CTX, "head"),
        P(CTX, "head"),
        P(CTX, "head"),
        P(CTX, "head"),
        P(CTX, None),
    )
    count = mesh.shape["ctx"]
    inner = INNER if count % INNER == 0 else 1
    split = jax.sharding.Mesh(
        mesh.devices.reshape(count // inner, inner, mesh.shape["head"]), CTX + ("head",)
    )
    return jax.shard_map(
        per_device,
        mesh=split,
        in_specs=placed,
        out_specs=(
            P(CTX, "head"),
            P(CTX, "head"),
            P(CTX, "head"),
            P(CTX, "head"),
            P(CTX, "head"),
            P(CTX, "head"),
        ),
        check_vma=False,
    )
```

```python
import math

import jax
import jax.numpy as jnp
from jax import lax
from jax.sharding import PartitionSpec as P

HEAD = 128
LIN_HEADS = 16
TILE = 128
LIST = 3
SPAN = 4


CTX = ("outer", "inner")
INNER = 8
PLAN = (4, 4)


def scan_over(total, axis, backward):
    count = lax.axis_size(axis)
    plan = PLAN
    if math.prod(plan) != count:
        plan = (2,) * max(1, (count - 1).bit_length())
    own = total
    stride = 1
    for radix in plan:
        arrived = []
        for step in range(1, radix):
            distance = step * stride
            if distance >= count:
                break
            if backward:
                pairs = [(i, i - distance) for i in range(distance, count)]
            else:
                pairs = [(i, i + distance) for i in range(count - distance)]
            arrived.append(lax.ppermute(total.astype(jnp.bfloat16), axis, pairs))
        for part in arrived:
            total = total + part.astype(jnp.float32)
        stride *= radix
    return total - own


def carried_in(shard, backward):
    members = lax.axis_size("inner")
    slices = shard.astype(jnp.bfloat16).reshape(members, -1)
    mine = lax.all_to_all(slices, "inner", 0, 0, tiled=True).astype(jnp.float32)
    running = jnp.cumsum(mine, axis=0)
    group = jnp.sum(mine, axis=0)
    within = group[None] - running if backward else running - mine
    earlier = scan_over(group, "outer", backward)
    states = (within + earlier[None]).astype(jnp.bfloat16)
    back = lax.all_to_all(states, "inner", 0, 0, tiled=True)
    return back.reshape(shard.shape).astype(shard.dtype)


def from_behind(shard, axis, by):
    length = lax.axis_size(axis)
    pairs = [(i, i + by) for i in range(length) if 0 <= i + by < length]
    return lax.ppermute(shard, axis, pairs)


def add_states(earlier, later):
    return earlier + later


def tile_attention(query, grad, key_window, value_window, lists, shard):
    token_count, width = query.shape
    heads = width // HEAD
    tiles_dev = token_count // TILE
    window_tiles = key_window.shape[0] // TILE
    valid = lists >= 0
    local_index = jnp.where(valid, lists - (shard - SPAN) * tiles_dev, 0)
    own_index = (SPAN * tiles_dev + jnp.arange(tiles_dev, dtype=jnp.int32))[:, None]
    picked = jnp.concatenate([own_index, local_index], axis=1)
    keep = jnp.concatenate([jnp.ones((tiles_dev, 1), jnp.bool_), valid], axis=1)
    key_set = key_window.reshape(window_tiles, TILE, heads, HEAD)[picked].reshape(
        tiles_dev, (LIST + 1) * TILE, heads, HEAD
    )
    value_set = value_window.reshape(window_tiles, TILE, heads, HEAD)[picked].reshape(
        tiles_dev, (LIST + 1) * TILE, heads, HEAD
    )
    query_tiles = query.reshape(tiles_dev, TILE, heads, HEAD)
    grad_tiles = grad.reshape(tiles_dev, TILE, heads, HEAD)
    scale = HEAD ** (-0.5)
    scores = (
        jnp.einsum("athd,ashd->ahts", query_tiles, key_set, preferred_element_type=jnp.float32)
        * scale
    )
    rows_idx = jnp.arange(TILE)[:, None]
    cols_idx = jnp.arange((LIST + 1) * TILE)[None, :]
    allowed = jnp.where(cols_idx // TILE == 0, cols_idx % TILE <= rows_idx, True)
    live = jnp.repeat(keep, TILE, axis=1)
    allowed_all = allowed[None, None, :, :] & live[:, None, None, :]
    scores = jnp.where(allowed_all, scores, -jnp.inf)
    top_score = jnp.max(scores, axis=-1, keepdims=True)
    expo = jnp.exp(scores - top_score)
    probs = expo / jnp.sum(expo, axis=-1, keepdims=True)
    probs_half = probs.astype(jnp.bfloat16)
    attended = jnp.einsum(
        "ahts,ashd->athd", probs_half, value_set, preferred_element_type=jnp.float32
    )
    delta = jnp.transpose(jnp.sum(grad_tiles.astype(jnp.float32) * attended, axis=-1), (0, 2, 1))[
        ..., None
    ]
    grad_probs = jnp.einsum(
        "athd,ashd->ahts", grad_tiles, value_set, preferred_element_type=jnp.float32
    )
    grad_logits = (probs * (grad_probs - delta) * scale).astype(jnp.bfloat16)
    query_grad = (
        jnp.einsum("ahts,ashd->athd", grad_logits, key_set, preferred_element_type=jnp.float32)
        .reshape(token_count, width)
        .astype(jnp.bfloat16)
    )
    key_part = jnp.einsum(
        "ahts,athd->ashd", grad_logits, query_tiles, preferred_element_type=jnp.float32
    ).reshape(tiles_dev * (LIST + 1), TILE, width)
    value_part = jnp.einsum(
        "ahts,athd->ashd", probs_half, grad_tiles, preferred_element_type=jnp.float32
    ).reshape(tiles_dev * (LIST + 1), TILE, width)
    flat_index = picked.reshape(-1)
    key_acc = jnp.zeros((window_tiles, TILE, width), jnp.float32).at[flat_index].add(key_part)
    value_acc = jnp.zeros((window_tiles, TILE, width), jnp.float32).at[flat_index].add(value_part)
    return (query_grad, key_acc, value_acc)


def per_device(
    lin_query,
    lin_key,
    lin_value,
    norm_gain,
    lin_grad,
    sm_query,
    sm_key,
    sm_value,
    sm_grad,
    tile_lists,
):
    token_count = lin_query.shape[0]
    lin_width = lin_query.shape[1]
    heads_lin = lin_width // HEAD
    query_lin = lin_query.reshape(token_count, heads_lin, HEAD)
    key_lin = lin_key.reshape(token_count, heads_lin, HEAD)
    value_lin = lin_value.reshape(token_count, heads_lin, HEAD)
    key_value = jnp.einsum("thi,thj->hij", key_lin, value_lin, preferred_element_type=jnp.float32)
    state_low = carried_in(key_value, False)
    state_half = state_low.astype(jnp.bfloat16)
    causal = jnp.tril(jnp.ones((token_count, token_count), jnp.bool_))
    attn_lin = jnp.where(
        causal[None],
        jnp.einsum("thd,shd->hts", query_lin, key_lin, preferred_element_type=jnp.float32),
        0.0,
    ).astype(jnp.bfloat16)
    output_lin = jnp.einsum(
        "hts,shd->thd", attn_lin, value_lin, preferred_element_type=jnp.float32
    ) + jnp.einsum("thi,hij->thj", query_lin, state_half, preferred_element_type=jnp.float32)
    gain_grad = norm_gain.reshape(1, heads_lin, HEAD) * lin_grad.reshape(
        token_count, heads_lin, HEAD
    ).astype(jnp.float32)
    square_sum = jnp.sum(output_lin * output_lin, axis=(1, 2))
    cross_sum = jnp.sum(gain_grad * output_lin, axis=(1, 2))
    sums = jnp.stack([square_sum, cross_sum])
    heads_dev = lax.axis_size("head")
    step = 1
    while step < heads_dev:
        sums = sums + lax.ppermute(sums, "head", [(i, i ^ step) for i in range(heads_dev)])
        step *= 2
    square_sum, cross_sum = sums[0], sums[1]
    full_width = LIN_HEADS * HEAD
    inv_rms = lax.rsqrt(square_sum / full_width + 1e-06)[:, None, None]
    grad_out = (
        gain_grad * inv_rms - output_lin * inv_rms**3 * (cross_sum / full_width)[:, None, None]
    ).astype(jnp.bfloat16)
    adjoint_local = jnp.einsum(
        "thi,thj->hij", query_lin, grad_out, preferred_element_type=jnp.float32
    )
    adjoint_high = carried_in(adjoint_local, True)
    adjoint_half = adjoint_high.astype(jnp.bfloat16)
    grad_scores = jnp.where(
        causal[None],
        jnp.einsum("thd,shd->hts", grad_out, value_lin, preferred_element_type=jnp.float32),
        0.0,
    ).astype(jnp.bfloat16)
    lin_dq = jnp.einsum(
        "hts,shd->thd", grad_scores, key_lin, preferred_element_type=jnp.float32
    ) + jnp.einsum("thj,hij->thi", grad_out, state_half, preferred_element_type=jnp.float32)
    lin_dk = jnp.einsum(
        "hts,thd->shd", grad_scores, query_lin, preferred_element_type=jnp.float32
    ) + jnp.einsum("shj,hij->shi", value_lin, adjoint_half, preferred_element_type=jnp.float32)
    lin_dv = jnp.einsum(
        "hts,thd->shd", attn_lin, grad_out, preferred_element_type=jnp.float32
    ) + jnp.einsum("shi,hij->shj", key_lin, adjoint_half, preferred_element_type=jnp.float32)
    lin_dq = lin_dq.reshape(token_count, lin_width).astype(jnp.bfloat16)
    lin_dk = lin_dk.reshape(token_count, lin_width).astype(jnp.bfloat16)
    lin_dv = lin_dv.reshape(token_count, lin_width).astype(jnp.bfloat16)
    width = sm_key.shape[1]
    pair = jnp.concatenate([sm_key, sm_value], axis=1)
    arrived = []
    moving = pair
    for distance in range(1, SPAN + 1):
        moving = from_behind(moving, CTX, 1)
        arrived.append(moving)
    key_window = jnp.concatenate(
        [arrived[SPAN - 1 - place][:, :width] for place in range(SPAN)] + [sm_key], axis=0
    )
    value_window = jnp.concatenate(
        [arrived[SPAN - 1 - place][:, width:] for place in range(SPAN)] + [sm_value], axis=0
    )
    shard = lax.axis_index(CTX)
    sm_dq, key_acc, value_acc = tile_attention(
        sm_query, sm_grad, key_window, value_window, tile_lists, shard
    )
    key_total = key_acc[SPAN]
    value_total = value_acc[SPAN]
    owed = None
    for distance in range(SPAN, 0, -1):
        term = jnp.concatenate(
            [key_acc[SPAN - distance], value_acc[SPAN - distance]], axis=1
        ).astype(jnp.bfloat16).astype(jnp.float32)
        owed = term if owed is None else owed + term
        owed = from_behind(owed.astype(jnp.bfloat16), CTX, -1).astype(jnp.float32)
    key_total = key_total + owed[:, :width]
    value_total = value_total + owed[:, width:]
    return (
        lin_dq,
        lin_dk,
        lin_dv,
        sm_dq,
        key_total.astype(jnp.bfloat16),
        value_total.astype(jnp.bfloat16),
    )


def solution(mesh):
    placed = (
        P(CTX, "head"),
        P(CTX, "head"),
        P(CTX, "head"),
        P("head"),
        P(CTX, "head"),
        P(CTX, "head"),
        P(CTX, "head"),
        P(CTX, "head"),
        P(CTX, "head"),
        P(CTX, None),
    )
    count = mesh.shape["ctx"]
    inner = INNER if count % INNER == 0 else 1
    split = jax.sharding.Mesh(
        mesh.devices.reshape(count // inner, inner, mesh.shape["head"]), CTX + ("head",)
    )
    return jax.shard_map(
        per_device,
        mesh=split,
        in_specs=placed,
        out_specs=(
            P(CTX, "head"),
            P(CTX, "head"),
            P(CTX, "head"),
            P(CTX, "head"),
            P(CTX, "head"),
            P(CTX, "head"),
        ),
        check_vma=False,
    )
```

```python
import math

import jax
import jax.numpy as jnp
from jax import lax
from jax.sharding import PartitionSpec as P

HEAD = 128
LIN_HEADS = 16
TILE = 128
LIST = 3
SPAN = 4


CTX = ("outer", "inner")
INNER = 8
PLAN = (4, 4)


def scan_over(total, axis, backward):
    count = lax.axis_size(axis)
    plan = PLAN
    if math.prod(plan) != count:
        plan = (2,) * max(1, (count - 1).bit_length())
    own = total
    stride = 1
    for radix in plan:
        arrived = []
        for step in range(1, radix):
            distance = step * stride
            if distance >= count:
                break
            if backward:
                pairs = [(i, i - distance) for i in range(distance, count)]
            else:
                pairs = [(i, i + distance) for i in range(count - distance)]
            arrived.append(lax.ppermute(total.astype(jnp.bfloat16), axis, pairs))
        for part in arrived:
            total = total + part.astype(jnp.float32)
        stride *= radix
    return total - own


def gathered_before(total, axis, backward):
    count = lax.axis_size(axis)
    sent = jnp.broadcast_to(total.astype(jnp.bfloat16)[None], (count,) + total.shape)
    got = lax.all_to_all(sent, axis, 0, 0, tiled=True).astype(jnp.float32)
    index = jnp.arange(count)
    place = lax.axis_index(axis)
    mask = index > place if backward else index < place
    return jnp.sum(jnp.where(mask.reshape((-1,) + (1,) * total.ndim), got, 0.0), axis=0)


def carried_in(shard, backward):
    members = lax.axis_size("inner")
    slices = shard.astype(jnp.bfloat16).reshape(members, -1)
    mine = lax.all_to_all(slices, "inner", 0, 0, tiled=True).astype(jnp.float32)
    running = jnp.cumsum(mine, axis=0)
    group = jnp.sum(mine, axis=0)
    within = group[None] - running if backward else running - mine
    earlier = gathered_before(group, "outer", backward)
    states = (within + earlier[None]).astype(jnp.bfloat16)
    back = lax.all_to_all(states, "inner", 0, 0, tiled=True)
    return back.reshape(shard.shape).astype(shard.dtype)


def from_behind(shard, axis, by):
    length = lax.axis_size(axis)
    pairs = [(i, i + by) for i in range(length) if 0 <= i + by < length]
    return lax.ppermute(shard, axis, pairs)


def add_states(earlier, later):
    return earlier + later


def tile_attention(query, grad, key_window, value_window, lists, shard):
    token_count, width = query.shape
    heads = width // HEAD
    tiles_dev = token_count // TILE
    window_tiles = key_window.shape[0] // TILE
    valid = lists >= 0
    local_index = jnp.where(valid, lists - (shard - SPAN) * tiles_dev, 0)
    own_index = (SPAN * tiles_dev + jnp.arange(tiles_dev, dtype=jnp.int32))[:, None]
    picked = jnp.concatenate([own_index, local_index], axis=1)
    keep = jnp.concatenate([jnp.ones((tiles_dev, 1), jnp.bool_), valid], axis=1)
    key_set = key_window.reshape(window_tiles, TILE, heads, HEAD)[picked].reshape(
        tiles_dev, (LIST + 1) * TILE, heads, HEAD
    )
    value_set = value_window.reshape(window_tiles, TILE, heads, HEAD)[picked].reshape(
        tiles_dev, (LIST + 1) * TILE, heads, HEAD
    )
    query_tiles = query.reshape(tiles_dev, TILE, heads, HEAD)
    grad_tiles = grad.reshape(tiles_dev, TILE, heads, HEAD)
    scale = HEAD ** (-0.5)
    scores = (
        jnp.einsum("athd,ashd->ahts", query_tiles, key_set, preferred_element_type=jnp.float32)
        * scale
    )
    rows_idx = jnp.arange(TILE)[:, None]
    cols_idx = jnp.arange((LIST + 1) * TILE)[None, :]
    allowed = jnp.where(cols_idx // TILE == 0, cols_idx % TILE <= rows_idx, True)
    live = jnp.repeat(keep, TILE, axis=1)
    allowed_all = allowed[None, None, :, :] & live[:, None, None, :]
    scores = jnp.where(allowed_all, scores, -jnp.inf)
    top_score = jnp.max(scores, axis=-1, keepdims=True)
    expo = jnp.exp(scores - top_score)
    probs = expo / jnp.sum(expo, axis=-1, keepdims=True)
    probs_half = probs.astype(jnp.bfloat16)
    attended = jnp.einsum(
        "ahts,ashd->athd", probs_half, value_set, preferred_element_type=jnp.float32
    )
    delta = jnp.transpose(jnp.sum(grad_tiles.astype(jnp.float32) * attended, axis=-1), (0, 2, 1))[
        ..., None
    ]
    grad_probs = jnp.einsum(
        "athd,ashd->ahts", grad_tiles, value_set, preferred_element_type=jnp.float32
    )
    grad_logits = (probs * (grad_probs - delta) * scale).astype(jnp.bfloat16)
    query_grad = (
        jnp.einsum("ahts,ashd->athd", grad_logits, key_set, preferred_element_type=jnp.float32)
        .reshape(token_count, width)
        .astype(jnp.bfloat16)
    )
    key_part = jnp.einsum(
        "ahts,athd->ashd", grad_logits, query_tiles, preferred_element_type=jnp.float32
    ).reshape(tiles_dev * (LIST + 1), TILE, width)
    value_part = jnp.einsum(
        "ahts,athd->ashd", probs_half, grad_tiles, preferred_element_type=jnp.float32
    ).reshape(tiles_dev * (LIST + 1), TILE, width)
    flat_index = picked.reshape(-1)
    key_acc = jnp.zeros((window_tiles, TILE, width), jnp.float32).at[flat_index].add(key_part)
    value_acc = jnp.zeros((window_tiles, TILE, width), jnp.float32).at[flat_index].add(value_part)
    return (query_grad, key_acc, value_acc)


def per_device(
    lin_query,
    lin_key,
    lin_value,
    norm_gain,
    lin_grad,
    sm_query,
    sm_key,
    sm_value,
    sm_grad,
    tile_lists,
):
    token_count = lin_query.shape[0]
    lin_width = lin_query.shape[1]
    heads_lin = lin_width // HEAD
    query_lin = lin_query.reshape(token_count, heads_lin, HEAD)
    key_lin = lin_key.reshape(token_count, heads_lin, HEAD)
    value_lin = lin_value.reshape(token_count, heads_lin, HEAD)
    key_value = jnp.einsum("thi,thj->hij", key_lin, value_lin, preferred_element_type=jnp.float32)
    state_low = carried_in(key_value, False)
    state_half = state_low.astype(jnp.bfloat16)
    causal = jnp.tril(jnp.ones((token_count, token_count), jnp.bool_))
    attn_lin = jnp.where(
        causal[None],
        jnp.einsum("thd,shd->hts", query_lin, key_lin, preferred_element_type=jnp.float32),
        0.0,
    ).astype(jnp.bfloat16)
    output_lin = jnp.einsum(
        "hts,shd->thd", attn_lin, value_lin, preferred_element_type=jnp.float32
    ) + jnp.einsum("thi,hij->thj", query_lin, state_half, preferred_element_type=jnp.float32)
    gain_grad = norm_gain.reshape(1, heads_lin, HEAD) * lin_grad.reshape(
        token_count, heads_lin, HEAD
    ).astype(jnp.float32)
    square_sum = jnp.sum(output_lin * output_lin, axis=(1, 2))
    cross_sum = jnp.sum(gain_grad * output_lin, axis=(1, 2))
    sums = jnp.stack([square_sum, cross_sum])
    heads_dev = lax.axis_size("head")
    spread = jnp.broadcast_to(sums[None], (heads_dev,) + sums.shape)
    sums = jnp.sum(lax.all_to_all(spread, "head", 0, 0, tiled=True), axis=0)
    square_sum, cross_sum = sums[0], sums[1]
    full_width = LIN_HEADS * HEAD
    inv_rms = lax.rsqrt(square_sum / full_width + 1e-06)[:, None, None]
    grad_out = (
        gain_grad * inv_rms - output_lin * inv_rms**3 * (cross_sum / full_width)[:, None, None]
    ).astype(jnp.bfloat16)
    adjoint_local = jnp.einsum(
        "thi,thj->hij", query_lin, grad_out, preferred_element_type=jnp.float32
    )
    adjoint_high = carried_in(adjoint_local, True)
    adjoint_half = adjoint_high.astype(jnp.bfloat16)
    grad_scores = jnp.where(
        causal[None],
        jnp.einsum("thd,shd->hts", grad_out, value_lin, preferred_element_type=jnp.float32),
        0.0,
    ).astype(jnp.bfloat16)
    lin_dq = jnp.einsum(
        "hts,shd->thd", grad_scores, key_lin, preferred_element_type=jnp.float32
    ) + jnp.einsum("thj,hij->thi", grad_out, state_half, preferred_element_type=jnp.float32)
    lin_dk = jnp.einsum(
        "hts,thd->shd", grad_scores, query_lin, preferred_element_type=jnp.float32
    ) + jnp.einsum("shj,hij->shi", value_lin, adjoint_half, preferred_element_type=jnp.float32)
    lin_dv = jnp.einsum(
        "hts,thd->shd", attn_lin, grad_out, preferred_element_type=jnp.float32
    ) + jnp.einsum("shi,hij->shj", key_lin, adjoint_half, preferred_element_type=jnp.float32)
    lin_dq = lin_dq.reshape(token_count, lin_width).astype(jnp.bfloat16)
    lin_dk = lin_dk.reshape(token_count, lin_width).astype(jnp.bfloat16)
    lin_dv = lin_dv.reshape(token_count, lin_width).astype(jnp.bfloat16)
    width = sm_key.shape[1]
    pair = jnp.concatenate([sm_key, sm_value], axis=1)
    arrived = []
    moving = pair
    for distance in range(1, SPAN + 1):
        moving = from_behind(moving, CTX, 1)
        arrived.append(moving)
    key_window = jnp.concatenate(
        [arrived[SPAN - 1 - place][:, :width] for place in range(SPAN)] + [sm_key], axis=0
    )
    value_window = jnp.concatenate(
        [arrived[SPAN - 1 - place][:, width:] for place in range(SPAN)] + [sm_value], axis=0
    )
    shard = lax.axis_index(CTX)
    sm_dq, key_acc, value_acc = tile_attention(
        sm_query, sm_grad, key_window, value_window, tile_lists, shard
    )
    key_total = key_acc[SPAN]
    value_total = value_acc[SPAN]
    owed = None
    for distance in range(SPAN, 0, -1):
        term = jnp.concatenate(
            [key_acc[SPAN - distance], value_acc[SPAN - distance]], axis=1
        ).astype(jnp.bfloat16).astype(jnp.float32)
        owed = term if owed is None else owed + term
        owed = from_behind(owed.astype(jnp.bfloat16), CTX, -1).astype(jnp.float32)
    key_total = key_total + owed[:, :width]
    value_total = value_total + owed[:, width:]
    return (
        lin_dq,
        lin_dk,
        lin_dv,
        sm_dq,
        key_total.astype(jnp.bfloat16),
        value_total.astype(jnp.bfloat16),
    )


def solution(mesh):
    placed = (
        P(CTX, "head"),
        P(CTX, "head"),
        P(CTX, "head"),
        P("head"),
        P(CTX, "head"),
        P(CTX, "head"),
        P(CTX, "head"),
        P(CTX, "head"),
        P(CTX, "head"),
        P(CTX, None),
    )
    count = mesh.shape["ctx"]
    inner = INNER if count % INNER == 0 else 1
    split = jax.sharding.Mesh(
        mesh.devices.reshape(count // inner, inner, mesh.shape["head"]), CTX + ("head",)
    )
    return jax.shard_map(
        per_device,
        mesh=split,
        in_specs=placed,
        out_specs=(
            P(CTX, "head"),
            P(CTX, "head"),
            P(CTX, "head"),
            P(CTX, "head"),
            P(CTX, "head"),
            P(CTX, "head"),
        ),
        check_vma=False,
    )
```

```python
import math

import jax
import jax.numpy as jnp
from jax import lax
from jax.sharding import PartitionSpec as P

HEAD = 128
LIN_HEADS = 16
TILE = 128
LIST = 3
SPAN = 4


CTX = ("outer", "inner")
INNER = 8
PLAN = (4, 4)


def scan_over(total, axis, backward):
    count = lax.axis_size(axis)
    plan = PLAN
    if math.prod(plan) != count:
        plan = (2,) * max(1, (count - 1).bit_length())
    own = total
    stride = 1
    for radix in plan:
        arrived = []
        for step in range(1, radix):
            distance = step * stride
            if distance >= count:
                break
            if backward:
                pairs = [(i, i - distance) for i in range(distance, count)]
            else:
                pairs = [(i, i + distance) for i in range(count - distance)]
            arrived.append(lax.ppermute(total.astype(jnp.bfloat16), axis, pairs))
        for part in arrived:
            total = total + part.astype(jnp.float32)
        stride *= radix
    return total - own


def carried_in(shard, backward):
    members = lax.axis_size("inner")
    slices = shard.astype(jnp.bfloat16).reshape(members, -1)
    mine = lax.all_to_all(slices, "inner", 0, 0, tiled=True).astype(jnp.float32)
    running = jnp.cumsum(mine, axis=0)
    group = jnp.sum(mine, axis=0)
    within = group[None] - running if backward else running - mine
    earlier = scan_over(group, "outer", backward)
    states = (within + earlier[None]).astype(jnp.bfloat16)
    back = lax.all_to_all(states, "inner", 0, 0, tiled=True)
    return back.reshape(shard.shape).astype(shard.dtype)


def from_behind(shard, axis, by):
    length = lax.axis_size(axis)
    pairs = [(i, i + by) for i in range(length) if 0 <= i + by < length]
    return lax.ppermute(shard, axis, pairs)


def add_states(earlier, later):
    return earlier + later


def tile_attention(query, grad, key_window, value_window, lists, shard):
    token_count, width = query.shape
    heads = width // HEAD
    tiles_dev = token_count // TILE
    window_tiles = key_window.shape[0] // TILE
    valid = lists >= 0
    local_index = jnp.where(valid, lists - (shard - SPAN) * tiles_dev, 0)
    own_index = (SPAN * tiles_dev + jnp.arange(tiles_dev, dtype=jnp.int32))[:, None]
    picked = jnp.concatenate([own_index, local_index], axis=1)
    keep = jnp.concatenate([jnp.ones((tiles_dev, 1), jnp.bool_), valid], axis=1)
    key_set = key_window.reshape(window_tiles, TILE, heads, HEAD)[picked].reshape(
        tiles_dev, (LIST + 1) * TILE, heads, HEAD
    )
    value_set = value_window.reshape(window_tiles, TILE, heads, HEAD)[picked].reshape(
        tiles_dev, (LIST + 1) * TILE, heads, HEAD
    )
    query_tiles = query.reshape(tiles_dev, TILE, heads, HEAD)
    grad_tiles = grad.reshape(tiles_dev, TILE, heads, HEAD)
    scale = HEAD ** (-0.5)
    scores = (
        jnp.einsum("athd,ashd->ahts", query_tiles, key_set, preferred_element_type=jnp.float32)
        * scale
    )
    rows_idx = jnp.arange(TILE)[:, None]
    cols_idx = jnp.arange((LIST + 1) * TILE)[None, :]
    allowed = jnp.where(cols_idx // TILE == 0, cols_idx % TILE <= rows_idx, True)
    live = jnp.repeat(keep, TILE, axis=1)
    allowed_all = allowed[None, None, :, :] & live[:, None, None, :]
    scores = jnp.where(allowed_all, scores, -jnp.inf)
    top_score = jnp.max(scores, axis=-1, keepdims=True)
    expo = jnp.exp(scores - top_score)
    probs = expo / jnp.sum(expo, axis=-1, keepdims=True)
    probs_half = probs.astype(jnp.bfloat16)
    attended = jnp.einsum(
        "ahts,ashd->athd", probs_half, value_set, preferred_element_type=jnp.float32
    )
    delta = jnp.transpose(jnp.sum(grad_tiles.astype(jnp.float32) * attended, axis=-1), (0, 2, 1))[
        ..., None
    ]
    grad_probs = jnp.einsum(
        "athd,ashd->ahts", grad_tiles, value_set, preferred_element_type=jnp.float32
    )
    grad_logits = (probs * (grad_probs - delta) * scale).astype(jnp.bfloat16)
    query_grad = (
        jnp.einsum("ahts,ashd->athd", grad_logits, key_set, preferred_element_type=jnp.float32)
        .reshape(token_count, width)
        .astype(jnp.bfloat16)
    )
    key_part = jnp.einsum(
        "ahts,athd->ashd", grad_logits, query_tiles, preferred_element_type=jnp.float32
    ).reshape(tiles_dev * (LIST + 1), TILE, width)
    value_part = jnp.einsum(
        "ahts,athd->ashd", probs_half, grad_tiles, preferred_element_type=jnp.float32
    ).reshape(tiles_dev * (LIST + 1), TILE, width)
    flat_index = picked.reshape(-1)
    key_acc = jnp.zeros((window_tiles, TILE, width), jnp.float32).at[flat_index].add(key_part)
    value_acc = jnp.zeros((window_tiles, TILE, width), jnp.float32).at[flat_index].add(value_part)
    return (query_grad, key_acc, value_acc)


def per_device(
    lin_query,
    lin_key,
    lin_value,
    norm_gain,
    lin_grad,
    sm_query,
    sm_key,
    sm_value,
    sm_grad,
    tile_lists,
):
    token_count = lin_query.shape[0]
    lin_width = lin_query.shape[1]
    heads_lin = lin_width // HEAD
    query_lin = lin_query.reshape(token_count, heads_lin, HEAD)
    key_lin = lin_key.reshape(token_count, heads_lin, HEAD)
    value_lin = lin_value.reshape(token_count, heads_lin, HEAD)
    key_value = jnp.einsum("thi,thj->hij", key_lin, value_lin, preferred_element_type=jnp.float32)
    state_low = carried_in(key_value, False)
    state_half = state_low.astype(jnp.bfloat16)
    causal = jnp.tril(jnp.ones((token_count, token_count), jnp.bool_))
    attn_lin = jnp.where(
        causal[None],
        jnp.einsum("thd,shd->hts", query_lin, key_lin, preferred_element_type=jnp.float32),
        0.0,
    ).astype(jnp.bfloat16)
    output_lin = jnp.einsum(
        "hts,shd->thd", attn_lin, value_lin, preferred_element_type=jnp.float32
    ) + jnp.einsum("thi,hij->thj", query_lin, state_half, preferred_element_type=jnp.float32)
    gain_grad = norm_gain.reshape(1, heads_lin, HEAD) * lin_grad.reshape(
        token_count, heads_lin, HEAD
    ).astype(jnp.float32)
    square_sum = jnp.sum(output_lin * output_lin, axis=(1, 2))
    cross_sum = jnp.sum(gain_grad * output_lin, axis=(1, 2))
    sums = jnp.stack([square_sum, cross_sum])
    heads_dev = lax.axis_size("head")
    spread = jnp.broadcast_to(sums[None], (heads_dev,) + sums.shape)
    sums = jnp.sum(lax.all_to_all(spread, "head", 0, 0, tiled=True), axis=0)
    square_sum, cross_sum = sums[0], sums[1]
    full_width = LIN_HEADS * HEAD
    inv_rms = lax.rsqrt(square_sum / full_width + 1e-06)[:, None, None]
    grad_out = (
        gain_grad * inv_rms - output_lin * inv_rms**3 * (cross_sum / full_width)[:, None, None]
    ).astype(jnp.bfloat16)
    adjoint_local = jnp.einsum(
        "thi,thj->hij", query_lin, grad_out, preferred_element_type=jnp.float32
    )
    adjoint_high = carried_in(adjoint_local, True)
    adjoint_half = adjoint_high.astype(jnp.bfloat16)
    grad_scores = jnp.where(
        causal[None],
        jnp.einsum("thd,shd->hts", grad_out, value_lin, preferred_element_type=jnp.float32),
        0.0,
    ).astype(jnp.bfloat16)
    lin_dq = jnp.einsum(
        "hts,shd->thd", grad_scores, key_lin, preferred_element_type=jnp.float32
    ) + jnp.einsum("thj,hij->thi", grad_out, state_half, preferred_element_type=jnp.float32)
    lin_dk = jnp.einsum(
        "hts,thd->shd", grad_scores, query_lin, preferred_element_type=jnp.float32
    ) + jnp.einsum("shj,hij->shi", value_lin, adjoint_half, preferred_element_type=jnp.float32)
    lin_dv = jnp.einsum(
        "hts,thd->shd", attn_lin, grad_out, preferred_element_type=jnp.float32
    ) + jnp.einsum("shi,hij->shj", key_lin, adjoint_half, preferred_element_type=jnp.float32)
    lin_dq = lin_dq.reshape(token_count, lin_width).astype(jnp.bfloat16)
    lin_dk = lin_dk.reshape(token_count, lin_width).astype(jnp.bfloat16)
    lin_dv = lin_dv.reshape(token_count, lin_width).astype(jnp.bfloat16)
    width = sm_key.shape[1]
    pair = jnp.concatenate([sm_key, sm_value], axis=1)
    arrived = []
    moving = pair
    for distance in range(1, SPAN + 1):
        moving = from_behind(moving, CTX, 1)
        arrived.append(moving)
    key_window = jnp.concatenate(
        [arrived[SPAN - 1 - place][:, :width] for place in range(SPAN)] + [sm_key], axis=0
    )
    value_window = jnp.concatenate(
        [arrived[SPAN - 1 - place][:, width:] for place in range(SPAN)] + [sm_value], axis=0
    )
    shard = lax.axis_index(CTX)
    sm_dq, key_acc, value_acc = tile_attention(
        sm_query, sm_grad, key_window, value_window, tile_lists, shard
    )
    key_total = key_acc[SPAN]
    value_total = value_acc[SPAN]
    owed = None
    for distance in range(SPAN, 0, -1):
        term = jnp.concatenate(
            [key_acc[SPAN - distance], value_acc[SPAN - distance]], axis=1
        ).astype(jnp.bfloat16).astype(jnp.float32)
        owed = term if owed is None else owed + term
        owed = from_behind(owed.astype(jnp.bfloat16), CTX, -1).astype(jnp.float32)
    key_total = key_total + owed[:, :width]
    value_total = value_total + owed[:, width:]
    return (
        lin_dq,
        lin_dk,
        lin_dv,
        sm_dq,
        key_total.astype(jnp.bfloat16),
        value_total.astype(jnp.bfloat16),
    )


def solution(mesh):
    placed = (
        P(CTX, "head"),
        P(CTX, "head"),
        P(CTX, "head"),
        P("head"),
        P(CTX, "head"),
        P(CTX, "head"),
        P(CTX, "head"),
        P(CTX, "head"),
        P(CTX, "head"),
        P(CTX, None),
    )
    count = mesh.shape["ctx"]
    inner = INNER if count % INNER == 0 else 1
    split = jax.sharding.Mesh(
        mesh.devices.reshape(count // inner, inner, mesh.shape["head"]), CTX + ("head",)
    )
    return jax.shard_map(
        per_device,
        mesh=split,
        in_specs=placed,
        out_specs=(
            P(CTX, "head"),
            P(CTX, "head"),
            P(CTX, "head"),
            P(CTX, "head"),
            P(CTX, "head"),
            P(CTX, "head"),
        ),
        check_vma=False,
    )
```

```python
import math

import jax
import jax.numpy as jnp
from jax import lax
from jax.sharding import PartitionSpec as P

HEAD = 128
LIN_HEADS = 16
TILE = 128
LIST = 3
SPAN = 4


CTX = ("upper", "lower", "inner")
INNER = 8
LOWER = 4
PLAN = (4, 4)


def scan_over(total, axis, backward):
    count = lax.axis_size(axis)
    plan = PLAN
    if math.prod(plan) != count:
        plan = (2,) * max(1, (count - 1).bit_length())
    own = total
    stride = 1
    for radix in plan:
        arrived = []
        for step in range(1, radix):
            distance = step * stride
            if distance >= count:
                break
            if backward:
                pairs = [(i, i - distance) for i in range(distance, count)]
            else:
                pairs = [(i, i + distance) for i in range(count - distance)]
            arrived.append(lax.ppermute(total.astype(jnp.bfloat16), axis, pairs))
        for part in arrived:
            total = total + part.astype(jnp.float32)
        stride *= radix
    return total - own


def gathered_before(total, axis, backward):
    count = lax.axis_size(axis)
    sent = jnp.broadcast_to(total.astype(jnp.bfloat16)[None], (count,) + total.shape)
    got = lax.all_to_all(sent, axis, 0, 0, tiled=True).astype(jnp.float32)
    index = jnp.arange(count)
    place = lax.axis_index(axis)
    mask = index > place if backward else index < place
    picked = jnp.where(mask.reshape((-1,) + (1,) * total.ndim), got, 0.0)
    return jnp.sum(picked, axis=0), jnp.sum(got, axis=0)


def carried_in(shard, backward):
    members = lax.axis_size("inner")
    slices = shard.astype(jnp.bfloat16).reshape(members, -1)
    mine = lax.all_to_all(slices, "inner", 0, 0, tiled=True).astype(jnp.float32)
    running = jnp.cumsum(mine, axis=0)
    group = jnp.sum(mine, axis=0)
    within = group[None] - running if backward else running - mine
    near, lower = gathered_before(group, "lower", backward)
    far, _ = gathered_before(lower, "upper", backward)
    earlier = near + far
    states = (within + earlier[None]).astype(jnp.bfloat16)
    back = lax.all_to_all(states, "inner", 0, 0, tiled=True)
    return back.reshape(shard.shape).astype(shard.dtype)


def from_behind(shard, axis, by):
    length = lax.axis_size(axis)
    pairs = [(i, i + by) for i in range(length) if 0 <= i + by < length]
    return lax.ppermute(shard, axis, pairs)


def add_states(earlier, later):
    return earlier + later


def tile_attention(query, grad, key_window, value_window, lists, shard):
    token_count, width = query.shape
    heads = width // HEAD
    tiles_dev = token_count // TILE
    window_tiles = key_window.shape[0] // TILE
    valid = lists >= 0
    local_index = jnp.where(valid, lists - (shard - SPAN) * tiles_dev, 0)
    own_index = (SPAN * tiles_dev + jnp.arange(tiles_dev, dtype=jnp.int32))[:, None]
    picked = jnp.concatenate([own_index, local_index], axis=1)
    keep = jnp.concatenate([jnp.ones((tiles_dev, 1), jnp.bool_), valid], axis=1)
    key_set = key_window.reshape(window_tiles, TILE, heads, HEAD)[picked].reshape(
        tiles_dev, (LIST + 1) * TILE, heads, HEAD
    )
    value_set = value_window.reshape(window_tiles, TILE, heads, HEAD)[picked].reshape(
        tiles_dev, (LIST + 1) * TILE, heads, HEAD
    )
    query_tiles = query.reshape(tiles_dev, TILE, heads, HEAD)
    grad_tiles = grad.reshape(tiles_dev, TILE, heads, HEAD)
    scale = HEAD ** (-0.5)
    scores = (
        jnp.einsum("athd,ashd->ahts", query_tiles, key_set, preferred_element_type=jnp.float32)
        * scale
    )
    rows_idx = jnp.arange(TILE)[:, None]
    cols_idx = jnp.arange((LIST + 1) * TILE)[None, :]
    allowed = jnp.where(cols_idx // TILE == 0, cols_idx % TILE <= rows_idx, True)
    live = jnp.repeat(keep, TILE, axis=1)
    allowed_all = allowed[None, None, :, :] & live[:, None, None, :]
    scores = jnp.where(allowed_all, scores, -jnp.inf)
    top_score = jnp.max(scores, axis=-1, keepdims=True)
    expo = jnp.exp(scores - top_score)
    probs = expo / jnp.sum(expo, axis=-1, keepdims=True)
    probs_half = probs.astype(jnp.bfloat16)
    attended = jnp.einsum(
        "ahts,ashd->athd", probs_half, value_set, preferred_element_type=jnp.float32
    )
    delta = jnp.transpose(jnp.sum(grad_tiles.astype(jnp.float32) * attended, axis=-1), (0, 2, 1))[
        ..., None
    ]
    grad_probs = jnp.einsum(
        "athd,ashd->ahts", grad_tiles, value_set, preferred_element_type=jnp.float32
    )
    grad_logits = (probs * (grad_probs - delta) * scale).astype(jnp.bfloat16)
    query_grad = (
        jnp.einsum("ahts,ashd->athd", grad_logits, key_set, preferred_element_type=jnp.float32)
        .reshape(token_count, width)
        .astype(jnp.bfloat16)
    )
    key_part = jnp.einsum(
        "ahts,athd->ashd", grad_logits, query_tiles, preferred_element_type=jnp.float32
    ).reshape(tiles_dev * (LIST + 1), TILE, width)
    value_part = jnp.einsum(
        "ahts,athd->ashd", probs_half, grad_tiles, preferred_element_type=jnp.float32
    ).reshape(tiles_dev * (LIST + 1), TILE, width)
    flat_index = picked.reshape(-1)
    key_acc = jnp.zeros((window_tiles, TILE, width), jnp.float32).at[flat_index].add(key_part)
    value_acc = jnp.zeros((window_tiles, TILE, width), jnp.float32).at[flat_index].add(value_part)
    return (query_grad, key_acc, value_acc)


def per_device(
    lin_query,
    lin_key,
    lin_value,
    norm_gain,
    lin_grad,
    sm_query,
    sm_key,
    sm_value,
    sm_grad,
    tile_lists,
):
    token_count = lin_query.shape[0]
    lin_width = lin_query.shape[1]
    heads_lin = lin_width // HEAD
    query_lin = lin_query.reshape(token_count, heads_lin, HEAD)
    key_lin = lin_key.reshape(token_count, heads_lin, HEAD)
    value_lin = lin_value.reshape(token_count, heads_lin, HEAD)
    key_value = jnp.einsum("thi,thj->hij", key_lin, value_lin, preferred_element_type=jnp.float32)
    state_low = carried_in(key_value, False)
    state_half = state_low.astype(jnp.bfloat16)
    causal = jnp.tril(jnp.ones((token_count, token_count), jnp.bool_))
    attn_lin = jnp.where(
        causal[None],
        jnp.einsum("thd,shd->hts", query_lin, key_lin, preferred_element_type=jnp.float32),
        0.0,
    ).astype(jnp.bfloat16)
    output_lin = jnp.einsum(
        "hts,shd->thd", attn_lin, value_lin, preferred_element_type=jnp.float32
    ) + jnp.einsum("thi,hij->thj", query_lin, state_half, preferred_element_type=jnp.float32)
    gain_grad = norm_gain.reshape(1, heads_lin, HEAD) * lin_grad.reshape(
        token_count, heads_lin, HEAD
    ).astype(jnp.float32)
    square_sum = jnp.sum(output_lin * output_lin, axis=(1, 2))
    cross_sum = jnp.sum(gain_grad * output_lin, axis=(1, 2))
    sums = jnp.stack([square_sum, cross_sum])
    heads_dev = lax.axis_size("head")
    step = 1
    while step < heads_dev:
        sums = sums + lax.ppermute(sums, "head", [(i, i ^ step) for i in range(heads_dev)])
        step *= 2
    square_sum, cross_sum = sums[0], sums[1]
    full_width = LIN_HEADS * HEAD
    inv_rms = lax.rsqrt(square_sum / full_width + 1e-06)[:, None, None]
    grad_out = (
        gain_grad * inv_rms - output_lin * inv_rms**3 * (cross_sum / full_width)[:, None, None]
    ).astype(jnp.bfloat16)
    adjoint_local = jnp.einsum(
        "thi,thj->hij", query_lin, grad_out, preferred_element_type=jnp.float32
    )
    adjoint_high = carried_in(adjoint_local, True)
    adjoint_half = adjoint_high.astype(jnp.bfloat16)
    grad_scores = jnp.where(
        causal[None],
        jnp.einsum("thd,shd->hts", grad_out, value_lin, preferred_element_type=jnp.float32),
        0.0,
    ).astype(jnp.bfloat16)
    lin_dq = jnp.einsum(
        "hts,shd->thd", grad_scores, key_lin, preferred_element_type=jnp.float32
    ) + jnp.einsum("thj,hij->thi", grad_out, state_half, preferred_element_type=jnp.float32)
    lin_dk = jnp.einsum(
        "hts,thd->shd", grad_scores, query_lin, preferred_element_type=jnp.float32
    ) + jnp.einsum("shj,hij->shi", value_lin, adjoint_half, preferred_element_type=jnp.float32)
    lin_dv = jnp.einsum(
        "hts,thd->shd", attn_lin, grad_out, preferred_element_type=jnp.float32
    ) + jnp.einsum("shi,hij->shj", key_lin, adjoint_half, preferred_element_type=jnp.float32)
    lin_dq = lin_dq.reshape(token_count, lin_width).astype(jnp.bfloat16)
    lin_dk = lin_dk.reshape(token_count, lin_width).astype(jnp.bfloat16)
    lin_dv = lin_dv.reshape(token_count, lin_width).astype(jnp.bfloat16)
    width = sm_key.shape[1]
    pair = jnp.concatenate([sm_key, sm_value], axis=1)
    arrived = []
    moving = pair
    for distance in range(1, SPAN + 1):
        moving = from_behind(moving, CTX, 1)
        arrived.append(moving)
    key_window = jnp.concatenate(
        [arrived[SPAN - 1 - place][:, :width] for place in range(SPAN)] + [sm_key], axis=0
    )
    value_window = jnp.concatenate(
        [arrived[SPAN - 1 - place][:, width:] for place in range(SPAN)] + [sm_value], axis=0
    )
    shard = lax.axis_index(CTX)
    sm_dq, key_acc, value_acc = tile_attention(
        sm_query, sm_grad, key_window, value_window, tile_lists, shard
    )
    key_total = key_acc[SPAN]
    value_total = value_acc[SPAN]
    owed = None
    for distance in range(SPAN, 0, -1):
        term = jnp.concatenate(
            [key_acc[SPAN - distance], value_acc[SPAN - distance]], axis=1
        ).astype(jnp.bfloat16).astype(jnp.float32)
        owed = term if owed is None else owed + term
        owed = from_behind(owed.astype(jnp.bfloat16), CTX, -1).astype(jnp.float32)
    key_total = key_total + owed[:, :width]
    value_total = value_total + owed[:, width:]
    return (
        lin_dq,
        lin_dk,
        lin_dv,
        sm_dq,
        key_total.astype(jnp.bfloat16),
        value_total.astype(jnp.bfloat16),
    )


def solution(mesh):
    placed = (
        P(CTX, "head"),
        P(CTX, "head"),
        P(CTX, "head"),
        P("head"),
        P(CTX, "head"),
        P(CTX, "head"),
        P(CTX, "head"),
        P(CTX, "head"),
        P(CTX, "head"),
        P(CTX, None),
    )
    count = mesh.shape["ctx"]
    inner = INNER if count % INNER == 0 else 1
    outer = count // inner
    lower = LOWER if outer % LOWER == 0 else 1
    split = jax.sharding.Mesh(
        mesh.devices.reshape(outer // lower, lower, inner, mesh.shape["head"]), CTX + ("head",)
    )
    return jax.shard_map(
        per_device,
        mesh=split,
        in_specs=placed,
        out_specs=(
            P(CTX, "head"),
            P(CTX, "head"),
            P(CTX, "head"),
            P(CTX, "head"),
            P(CTX, "head"),
            P(CTX, "head"),
        ),
        check_vma=False,
    )
```

```python
import math

import jax
import jax.numpy as jnp
from jax import lax
from jax.sharding import PartitionSpec as P

HEAD = 128
LIN_HEADS = 16
TILE = 128
LIST = 3
SPAN = 4


CTX = ("outer", "inner")
INNER = 32
PLAN = (4,)


def scan_over(total, axis, backward):
    count = lax.axis_size(axis)
    plan = PLAN
    if math.prod(plan) != count:
        plan = (2,) * max(1, (count - 1).bit_length())
    own = total
    stride = 1
    for radix in plan:
        arrived = []
        for step in range(1, radix):
            distance = step * stride
            if distance >= count:
                break
            if backward:
                pairs = [(i, i - distance) for i in range(distance, count)]
            else:
                pairs = [(i, i + distance) for i in range(count - distance)]
            arrived.append(lax.ppermute(total.astype(jnp.bfloat16), axis, pairs))
        for part in arrived:
            total = total + part.astype(jnp.float32)
        stride *= radix
    return total - own


def carried_in(shard, backward):
    members = lax.axis_size("inner")
    slices = shard.astype(jnp.bfloat16).reshape(members, -1)
    mine = lax.all_to_all(slices, "inner", 0, 0, tiled=True).astype(jnp.float32)
    running = jnp.cumsum(mine, axis=0)
    group = jnp.sum(mine, axis=0)
    within = group[None] - running if backward else running - mine
    earlier = scan_over(group, "outer", backward)
    states = (within + earlier[None]).astype(jnp.bfloat16)
    back = lax.all_to_all(states, "inner", 0, 0, tiled=True)
    return back.reshape(shard.shape).astype(shard.dtype)


def from_behind(shard, axis, by):
    length = lax.axis_size(axis)
    pairs = [(i, i + by) for i in range(length) if 0 <= i + by < length]
    return lax.ppermute(shard, axis, pairs)


def add_states(earlier, later):
    return earlier + later


def tile_attention(query, grad, key_window, value_window, lists, shard):
    token_count, width = query.shape
    heads = width // HEAD
    tiles_dev = token_count // TILE
    window_tiles = key_window.shape[0] // TILE
    valid = lists >= 0
    local_index = jnp.where(valid, lists - (shard - SPAN) * tiles_dev, 0)
    own_index = (SPAN * tiles_dev + jnp.arange(tiles_dev, dtype=jnp.int32))[:, None]
    picked = jnp.concatenate([own_index, local_index], axis=1)
    keep = jnp.concatenate([jnp.ones((tiles_dev, 1), jnp.bool_), valid], axis=1)
    key_set = key_window.reshape(window_tiles, TILE, heads, HEAD)[picked].reshape(
        tiles_dev, (LIST + 1) * TILE, heads, HEAD
    )
    value_set = value_window.reshape(window_tiles, TILE, heads, HEAD)[picked].reshape(
        tiles_dev, (LIST + 1) * TILE, heads, HEAD
    )
    query_tiles = query.reshape(tiles_dev, TILE, heads, HEAD)
    grad_tiles = grad.reshape(tiles_dev, TILE, heads, HEAD)
    scale = HEAD ** (-0.5)
    scores = (
        jnp.einsum("athd,ashd->ahts", query_tiles, key_set, preferred_element_type=jnp.float32)
        * scale
    )
    rows_idx = jnp.arange(TILE)[:, None]
    cols_idx = jnp.arange((LIST + 1) * TILE)[None, :]
    allowed = jnp.where(cols_idx // TILE == 0, cols_idx % TILE <= rows_idx, True)
    live = jnp.repeat(keep, TILE, axis=1)
    allowed_all = allowed[None, None, :, :] & live[:, None, None, :]
    scores = jnp.where(allowed_all, scores, -jnp.inf)
    top_score = jnp.max(scores, axis=-1, keepdims=True)
    expo = jnp.exp(scores - top_score)
    probs = expo / jnp.sum(expo, axis=-1, keepdims=True)
    probs_half = probs.astype(jnp.bfloat16)
    attended = jnp.einsum(
        "ahts,ashd->athd", probs_half, value_set, preferred_element_type=jnp.float32
    )
    delta = jnp.transpose(jnp.sum(grad_tiles.astype(jnp.float32) * attended, axis=-1), (0, 2, 1))[
        ..., None
    ]
    grad_probs = jnp.einsum(
        "athd,ashd->ahts", grad_tiles, value_set, preferred_element_type=jnp.float32
    )
    grad_logits = (probs * (grad_probs - delta) * scale).astype(jnp.bfloat16)
    query_grad = (
        jnp.einsum("ahts,ashd->athd", grad_logits, key_set, preferred_element_type=jnp.float32)
        .reshape(token_count, width)
        .astype(jnp.bfloat16)
    )
    key_part = jnp.einsum(
        "ahts,athd->ashd", grad_logits, query_tiles, preferred_element_type=jnp.float32
    ).reshape(tiles_dev * (LIST + 1), TILE, width)
    value_part = jnp.einsum(
        "ahts,athd->ashd", probs_half, grad_tiles, preferred_element_type=jnp.float32
    ).reshape(tiles_dev * (LIST + 1), TILE, width)
    flat_index = picked.reshape(-1)
    key_acc = jnp.zeros((window_tiles, TILE, width), jnp.float32).at[flat_index].add(key_part)
    value_acc = jnp.zeros((window_tiles, TILE, width), jnp.float32).at[flat_index].add(value_part)
    return (query_grad, key_acc, value_acc)


def per_device(
    lin_query,
    lin_key,
    lin_value,
    norm_gain,
    lin_grad,
    sm_query,
    sm_key,
    sm_value,
    sm_grad,
    tile_lists,
):
    token_count = lin_query.shape[0]
    lin_width = lin_query.shape[1]
    heads_lin = lin_width // HEAD
    query_lin = lin_query.reshape(token_count, heads_lin, HEAD)
    key_lin = lin_key.reshape(token_count, heads_lin, HEAD)
    value_lin = lin_value.reshape(token_count, heads_lin, HEAD)
    key_value = jnp.einsum("thi,thj->hij", key_lin, value_lin, preferred_element_type=jnp.float32)
    state_low = carried_in(key_value, False)
    state_half = state_low.astype(jnp.bfloat16)
    causal = jnp.tril(jnp.ones((token_count, token_count), jnp.bool_))
    attn_lin = jnp.where(
        causal[None],
        jnp.einsum("thd,shd->hts", query_lin, key_lin, preferred_element_type=jnp.float32),
        0.0,
    ).astype(jnp.bfloat16)
    output_lin = jnp.einsum(
        "hts,shd->thd", attn_lin, value_lin, preferred_element_type=jnp.float32
    ) + jnp.einsum("thi,hij->thj", query_lin, state_half, preferred_element_type=jnp.float32)
    gain_grad = norm_gain.reshape(1, heads_lin, HEAD) * lin_grad.reshape(
        token_count, heads_lin, HEAD
    ).astype(jnp.float32)
    square_sum = jnp.sum(output_lin * output_lin, axis=(1, 2))
    cross_sum = jnp.sum(gain_grad * output_lin, axis=(1, 2))
    sums = jnp.stack([square_sum, cross_sum])
    heads_dev = lax.axis_size("head")
    step = 1
    while step < heads_dev:
        sums = sums + lax.ppermute(sums, "head", [(i, i ^ step) for i in range(heads_dev)])
        step *= 2
    square_sum, cross_sum = sums[0], sums[1]
    full_width = LIN_HEADS * HEAD
    inv_rms = lax.rsqrt(square_sum / full_width + 1e-06)[:, None, None]
    grad_out = (
        gain_grad * inv_rms - output_lin * inv_rms**3 * (cross_sum / full_width)[:, None, None]
    ).astype(jnp.bfloat16)
    adjoint_local = jnp.einsum(
        "thi,thj->hij", query_lin, grad_out, preferred_element_type=jnp.float32
    )
    adjoint_high = carried_in(adjoint_local, True)
    adjoint_half = adjoint_high.astype(jnp.bfloat16)
    grad_scores = jnp.where(
        causal[None],
        jnp.einsum("thd,shd->hts", grad_out, value_lin, preferred_element_type=jnp.float32),
        0.0,
    ).astype(jnp.bfloat16)
    lin_dq = jnp.einsum(
        "hts,shd->thd", grad_scores, key_lin, preferred_element_type=jnp.float32
    ) + jnp.einsum("thj,hij->thi", grad_out, state_half, preferred_element_type=jnp.float32)
    lin_dk = jnp.einsum(
        "hts,thd->shd", grad_scores, query_lin, preferred_element_type=jnp.float32
    ) + jnp.einsum("shj,hij->shi", value_lin, adjoint_half, preferred_element_type=jnp.float32)
    lin_dv = jnp.einsum(
        "hts,thd->shd", attn_lin, grad_out, preferred_element_type=jnp.float32
    ) + jnp.einsum("shi,hij->shj", key_lin, adjoint_half, preferred_element_type=jnp.float32)
    lin_dq = lin_dq.reshape(token_count, lin_width).astype(jnp.bfloat16)
    lin_dk = lin_dk.reshape(token_count, lin_width).astype(jnp.bfloat16)
    lin_dv = lin_dv.reshape(token_count, lin_width).astype(jnp.bfloat16)
    width = sm_key.shape[1]
    pair = jnp.concatenate([sm_key, sm_value], axis=1)
    arrived = []
    moving = pair
    for distance in range(1, SPAN + 1):
        moving = from_behind(moving, CTX, 1)
        arrived.append(moving)
    key_window = jnp.concatenate(
        [arrived[SPAN - 1 - place][:, :width] for place in range(SPAN)] + [sm_key], axis=0
    )
    value_window = jnp.concatenate(
        [arrived[SPAN - 1 - place][:, width:] for place in range(SPAN)] + [sm_value], axis=0
    )
    shard = lax.axis_index(CTX)
    sm_dq, key_acc, value_acc = tile_attention(
        sm_query, sm_grad, key_window, value_window, tile_lists, shard
    )
    key_total = key_acc[SPAN]
    value_total = value_acc[SPAN]
    owed = None
    for distance in range(SPAN, 0, -1):
        term = jnp.concatenate(
            [key_acc[SPAN - distance], value_acc[SPAN - distance]], axis=1
        ).astype(jnp.bfloat16).astype(jnp.float32)
        owed = term if owed is None else owed + term
        owed = from_behind(owed.astype(jnp.bfloat16), CTX, -1).astype(jnp.float32)
    key_total = key_total + owed[:, :width]
    value_total = value_total + owed[:, width:]
    return (
        lin_dq,
        lin_dk,
        lin_dv,
        sm_dq,
        key_total.astype(jnp.bfloat16),
        value_total.astype(jnp.bfloat16),
    )


def solution(mesh):
    placed = (
        P(CTX, "head"),
        P(CTX, "head"),
        P(CTX, "head"),
        P("head"),
        P(CTX, "head"),
        P(CTX, "head"),
        P(CTX, "head"),
        P(CTX, "head"),
        P(CTX, "head"),
        P(CTX, None),
    )
    count = mesh.shape["ctx"]
    inner = INNER if count % INNER == 0 else 1
    split = jax.sharding.Mesh(
        mesh.devices.reshape(count // inner, inner, mesh.shape["head"]), CTX + ("head",)
    )
    return jax.shard_map(
        per_device,
        mesh=split,
        in_specs=placed,
        out_specs=(
            P(CTX, "head"),
            P(CTX, "head"),
            P(CTX, "head"),
            P(CTX, "head"),
            P(CTX, "head"),
            P(CTX, "head"),
        ),
        check_vma=False,
    )
```

```python
import math

import jax
import jax.numpy as jnp
from jax import lax
from jax.sharding import PartitionSpec as P

HEAD = 128
LIN_HEADS = 16
TILE = 128
LIST = 3
SPAN = 4


CTX = ("outer", "inner")
INNER = 32
PLAN = (4,)


def scan_over(total, axis, backward):
    count = lax.axis_size(axis)
    plan = PLAN
    if math.prod(plan) != count:
        plan = (2,) * max(1, (count - 1).bit_length())
    own = total
    stride = 1
    for radix in plan:
        arrived = []
        for step in range(1, radix):
            distance = step * stride
            if distance >= count:
                break
            if backward:
                pairs = [(i, i - distance) for i in range(distance, count)]
            else:
                pairs = [(i, i + distance) for i in range(count - distance)]
            arrived.append(lax.ppermute(total.astype(jnp.bfloat16), axis, pairs))
        for part in arrived:
            total = total + part.astype(jnp.float32)
        stride *= radix
    return total - own


def carried_in(shard, backward, tied=None):
    members = lax.axis_size("inner")
    slices = shard.astype(jnp.bfloat16).reshape(members, -1)
    mine = lax.all_to_all(slices, "inner", 0, 0, tiled=True).astype(jnp.float32)
    running = jnp.cumsum(mine, axis=0)
    group = jnp.sum(mine, axis=0)
    within = group[None] - running if backward else running - mine
    earlier = scan_over(group, "outer", backward)
    states = (within + earlier[None]).astype(jnp.bfloat16)
    if tied is not None:
        states, tied = lax.optimization_barrier((states, tied))
    back = lax.all_to_all(states, "inner", 0, 0, tiled=True)
    return back.reshape(shard.shape).astype(shard.dtype), tied


def from_behind(shard, axis, by):
    length = lax.axis_size(axis)
    pairs = [(i, i + by) for i in range(length) if 0 <= i + by < length]
    return lax.ppermute(shard, axis, pairs)


def add_states(earlier, later):
    return earlier + later


def tile_attention(query, grad, key_window, value_window, lists, shard):
    token_count, width = query.shape
    heads = width // HEAD
    tiles_dev = token_count // TILE
    window_tiles = key_window.shape[0] // TILE
    valid = lists >= 0
    local_index = jnp.where(valid, lists - (shard - SPAN) * tiles_dev, 0)
    own_index = (SPAN * tiles_dev + jnp.arange(tiles_dev, dtype=jnp.int32))[:, None]
    picked = jnp.concatenate([own_index, local_index], axis=1)
    keep = jnp.concatenate([jnp.ones((tiles_dev, 1), jnp.bool_), valid], axis=1)
    key_set = key_window.reshape(window_tiles, TILE, heads, HEAD)[picked].reshape(
        tiles_dev, (LIST + 1) * TILE, heads, HEAD
    )
    value_set = value_window.reshape(window_tiles, TILE, heads, HEAD)[picked].reshape(
        tiles_dev, (LIST + 1) * TILE, heads, HEAD
    )
    query_tiles = query.reshape(tiles_dev, TILE, heads, HEAD)
    grad_tiles = grad.reshape(tiles_dev, TILE, heads, HEAD)
    scale = HEAD ** (-0.5)
    scores = (
        jnp.einsum("athd,ashd->ahts", query_tiles, key_set, preferred_element_type=jnp.float32)
        * scale
    )
    rows_idx = jnp.arange(TILE)[:, None]
    cols_idx = jnp.arange((LIST + 1) * TILE)[None, :]
    allowed = jnp.where(cols_idx // TILE == 0, cols_idx % TILE <= rows_idx, True)
    live = jnp.repeat(keep, TILE, axis=1)
    allowed_all = allowed[None, None, :, :] & live[:, None, None, :]
    scores = jnp.where(allowed_all, scores, -jnp.inf)
    top_score = jnp.max(scores, axis=-1, keepdims=True)
    expo = jnp.exp(scores - top_score)
    probs = expo / jnp.sum(expo, axis=-1, keepdims=True)
    probs_half = probs.astype(jnp.bfloat16)
    attended = jnp.einsum(
        "ahts,ashd->athd", probs_half, value_set, preferred_element_type=jnp.float32
    )
    delta = jnp.transpose(jnp.sum(grad_tiles.astype(jnp.float32) * attended, axis=-1), (0, 2, 1))[
        ..., None
    ]
    grad_probs = jnp.einsum(
        "athd,ashd->ahts", grad_tiles, value_set, preferred_element_type=jnp.float32
    )
    grad_logits = (probs * (grad_probs - delta) * scale).astype(jnp.bfloat16)
    query_grad = (
        jnp.einsum("ahts,ashd->athd", grad_logits, key_set, preferred_element_type=jnp.float32)
        .reshape(token_count, width)
        .astype(jnp.bfloat16)
    )
    key_part = jnp.einsum(
        "ahts,athd->ashd", grad_logits, query_tiles, preferred_element_type=jnp.float32
    ).reshape(tiles_dev * (LIST + 1), TILE, width)
    value_part = jnp.einsum(
        "ahts,athd->ashd", probs_half, grad_tiles, preferred_element_type=jnp.float32
    ).reshape(tiles_dev * (LIST + 1), TILE, width)
    flat_index = picked.reshape(-1)
    key_acc = jnp.zeros((window_tiles, TILE, width), jnp.float32).at[flat_index].add(key_part)
    value_acc = jnp.zeros((window_tiles, TILE, width), jnp.float32).at[flat_index].add(value_part)
    return (query_grad, key_acc, value_acc)


def per_device(
    lin_query,
    lin_key,
    lin_value,
    norm_gain,
    lin_grad,
    sm_query,
    sm_key,
    sm_value,
    sm_grad,
    tile_lists,
):
    token_count = lin_query.shape[0]
    lin_width = lin_query.shape[1]
    heads_lin = lin_width // HEAD
    query_lin = lin_query.reshape(token_count, heads_lin, HEAD)
    key_lin = lin_key.reshape(token_count, heads_lin, HEAD)
    value_lin = lin_value.reshape(token_count, heads_lin, HEAD)
    key_value = jnp.einsum("thi,thj->hij", key_lin, value_lin, preferred_element_type=jnp.float32)
    width = sm_key.shape[1]
    pair = jnp.concatenate([sm_key, sm_value], axis=1)
    arrived = []
    moving = pair
    for distance in range(1, SPAN + 1):
        moving = from_behind(moving, CTX, 1)
        arrived.append(moving)
    key_window = jnp.concatenate(
        [arrived[SPAN - 1 - place][:, :width] for place in range(SPAN)] + [sm_key], axis=0
    )
    value_window = jnp.concatenate(
        [arrived[SPAN - 1 - place][:, width:] for place in range(SPAN)] + [sm_value], axis=0
    )
    shard = lax.axis_index(CTX)
    sm_dq, key_acc, value_acc = tile_attention(
        sm_query, sm_grad, key_window, value_window, tile_lists, shard
    )
    state_low, (sm_dq, key_acc, value_acc) = carried_in(
        key_value, False, (sm_dq, key_acc, value_acc)
    )
    state_half = state_low.astype(jnp.bfloat16)
    causal = jnp.tril(jnp.ones((token_count, token_count), jnp.bool_))
    attn_lin = jnp.where(
        causal[None],
        jnp.einsum("thd,shd->hts", query_lin, key_lin, preferred_element_type=jnp.float32),
        0.0,
    ).astype(jnp.bfloat16)
    output_lin = jnp.einsum(
        "hts,shd->thd", attn_lin, value_lin, preferred_element_type=jnp.float32
    ) + jnp.einsum("thi,hij->thj", query_lin, state_half, preferred_element_type=jnp.float32)
    gain_grad = norm_gain.reshape(1, heads_lin, HEAD) * lin_grad.reshape(
        token_count, heads_lin, HEAD
    ).astype(jnp.float32)
    square_sum = jnp.sum(output_lin * output_lin, axis=(1, 2))
    cross_sum = jnp.sum(gain_grad * output_lin, axis=(1, 2))
    sums = jnp.stack([square_sum, cross_sum])
    heads_dev = lax.axis_size("head")
    step = 1
    while step < heads_dev:
        sums = sums + lax.ppermute(sums, "head", [(i, i ^ step) for i in range(heads_dev)])
        step *= 2
    square_sum, cross_sum = sums[0], sums[1]
    full_width = LIN_HEADS * HEAD
    inv_rms = lax.rsqrt(square_sum / full_width + 1e-06)[:, None, None]
    grad_out = (
        gain_grad * inv_rms - output_lin * inv_rms**3 * (cross_sum / full_width)[:, None, None]
    ).astype(jnp.bfloat16)
    adjoint_local = jnp.einsum(
        "thi,thj->hij", query_lin, grad_out, preferred_element_type=jnp.float32
    )
    adjoint_high, _ = carried_in(adjoint_local, True)
    adjoint_half = adjoint_high.astype(jnp.bfloat16)
    grad_scores = jnp.where(
        causal[None],
        jnp.einsum("thd,shd->hts", grad_out, value_lin, preferred_element_type=jnp.float32),
        0.0,
    ).astype(jnp.bfloat16)
    lin_dq = jnp.einsum(
        "hts,shd->thd", grad_scores, key_lin, preferred_element_type=jnp.float32
    ) + jnp.einsum("thj,hij->thi", grad_out, state_half, preferred_element_type=jnp.float32)
    lin_dk = jnp.einsum(
        "hts,thd->shd", grad_scores, query_lin, preferred_element_type=jnp.float32
    ) + jnp.einsum("shj,hij->shi", value_lin, adjoint_half, preferred_element_type=jnp.float32)
    lin_dv = jnp.einsum(
        "hts,thd->shd", attn_lin, grad_out, preferred_element_type=jnp.float32
    ) + jnp.einsum("shi,hij->shj", key_lin, adjoint_half, preferred_element_type=jnp.float32)
    lin_dq = lin_dq.reshape(token_count, lin_width).astype(jnp.bfloat16)
    lin_dk = lin_dk.reshape(token_count, lin_width).astype(jnp.bfloat16)
    lin_dv = lin_dv.reshape(token_count, lin_width).astype(jnp.bfloat16)
    key_total = key_acc[SPAN]
    value_total = value_acc[SPAN]
    owed = None
    for distance in range(SPAN, 0, -1):
        term = jnp.concatenate(
            [key_acc[SPAN - distance], value_acc[SPAN - distance]], axis=1
        ).astype(jnp.bfloat16).astype(jnp.float32)
        owed = term if owed is None else owed + term
        owed = from_behind(owed.astype(jnp.bfloat16), CTX, -1).astype(jnp.float32)
    key_total = key_total + owed[:, :width]
    value_total = value_total + owed[:, width:]
    return (
        lin_dq,
        lin_dk,
        lin_dv,
        sm_dq,
        key_total.astype(jnp.bfloat16),
        value_total.astype(jnp.bfloat16),
    )


def solution(mesh):
    placed = (
        P(CTX, "head"),
        P(CTX, "head"),
        P(CTX, "head"),
        P("head"),
        P(CTX, "head"),
        P(CTX, "head"),
        P(CTX, "head"),
        P(CTX, "head"),
        P(CTX, "head"),
        P(CTX, None),
    )
    count = mesh.shape["ctx"]
    inner = INNER if count % INNER == 0 else 1
    split = jax.sharding.Mesh(
        mesh.devices.reshape(count // inner, inner, mesh.shape["head"]), CTX + ("head",)
    )
    return jax.shard_map(
        per_device,
        mesh=split,
        in_specs=placed,
        out_specs=(
            P(CTX, "head"),
            P(CTX, "head"),
            P(CTX, "head"),
            P(CTX, "head"),
            P(CTX, "head"),
            P(CTX, "head"),
        ),
        check_vma=False,
    )
```

```python
import math

import jax
import jax.numpy as jnp
from jax import lax
from jax.sharding import PartitionSpec as P

HEAD = 128
LIN_HEADS = 16
TILE = 128
LIST = 3
SPAN = 4


CTX = ("outer", "inner")
INNER = 16
PLAN = (2, 4)


def scan_over(total, axis, backward):
    count = lax.axis_size(axis)
    plan = PLAN
    if math.prod(plan) != count:
        plan = (2,) * max(1, (count - 1).bit_length())
    own = total
    stride = 1
    for radix in plan:
        arrived = []
        for step in range(1, radix):
            distance = step * stride
            if distance >= count:
                break
            if backward:
                pairs = [(i, i - distance) for i in range(distance, count)]
            else:
                pairs = [(i, i + distance) for i in range(count - distance)]
            arrived.append(lax.ppermute(total.astype(jnp.bfloat16), axis, pairs))
        for part in arrived:
            total = total + part.astype(jnp.float32)
        stride *= radix
    return total - own


def carried_in(shard, backward):
    members = lax.axis_size("inner")
    slices = shard.astype(jnp.bfloat16).reshape(members, -1)
    mine = lax.all_to_all(slices, "inner", 0, 0, tiled=True).astype(jnp.float32)
    running = jnp.cumsum(mine, axis=0)
    group = jnp.sum(mine, axis=0)
    within = group[None] - running if backward else running - mine
    earlier = scan_over(group, "outer", backward)
    states = (within + earlier[None]).astype(jnp.bfloat16)
    back = lax.all_to_all(states, "inner", 0, 0, tiled=True)
    return back.reshape(shard.shape).astype(shard.dtype)


def from_behind(shard, axis, by):
    length = lax.axis_size(axis)
    pairs = [(i, i + by) for i in range(length) if 0 <= i + by < length]
    return lax.ppermute(shard, axis, pairs)


def add_states(earlier, later):
    return earlier + later


def tile_attention(query, grad, key_window, value_window, lists, shard):
    token_count, width = query.shape
    heads = width // HEAD
    tiles_dev = token_count // TILE
    window_tiles = key_window.shape[0] // TILE
    valid = lists >= 0
    local_index = jnp.where(valid, lists - (shard - SPAN) * tiles_dev, 0)
    own_index = (SPAN * tiles_dev + jnp.arange(tiles_dev, dtype=jnp.int32))[:, None]
    picked = jnp.concatenate([own_index, local_index], axis=1)
    keep = jnp.concatenate([jnp.ones((tiles_dev, 1), jnp.bool_), valid], axis=1)
    key_set = key_window.reshape(window_tiles, TILE, heads, HEAD)[picked].reshape(
        tiles_dev, (LIST + 1) * TILE, heads, HEAD
    )
    value_set = value_window.reshape(window_tiles, TILE, heads, HEAD)[picked].reshape(
        tiles_dev, (LIST + 1) * TILE, heads, HEAD
    )
    query_tiles = query.reshape(tiles_dev, TILE, heads, HEAD)
    grad_tiles = grad.reshape(tiles_dev, TILE, heads, HEAD)
    scale = HEAD ** (-0.5)
    scores = (
        jnp.einsum("athd,ashd->ahts", query_tiles, key_set, preferred_element_type=jnp.float32)
        * scale
    )
    rows_idx = jnp.arange(TILE)[:, None]
    cols_idx = jnp.arange((LIST + 1) * TILE)[None, :]
    allowed = jnp.where(cols_idx // TILE == 0, cols_idx % TILE <= rows_idx, True)
    live = jnp.repeat(keep, TILE, axis=1)
    allowed_all = allowed[None, None, :, :] & live[:, None, None, :]
    scores = jnp.where(allowed_all, scores, -jnp.inf)
    top_score = jnp.max(scores, axis=-1, keepdims=True)
    expo = jnp.exp(scores - top_score)
    probs = expo / jnp.sum(expo, axis=-1, keepdims=True)
    probs_half = probs.astype(jnp.bfloat16)
    attended = jnp.einsum(
        "ahts,ashd->athd", probs_half, value_set, preferred_element_type=jnp.float32
    )
    delta = jnp.transpose(jnp.sum(grad_tiles.astype(jnp.float32) * attended, axis=-1), (0, 2, 1))[
        ..., None
    ]
    grad_probs = jnp.einsum(
        "athd,ashd->ahts", grad_tiles, value_set, preferred_element_type=jnp.float32
    )
    grad_logits = (probs * (grad_probs - delta) * scale).astype(jnp.bfloat16)
    query_grad = (
        jnp.einsum("ahts,ashd->athd", grad_logits, key_set, preferred_element_type=jnp.float32)
        .reshape(token_count, width)
        .astype(jnp.bfloat16)
    )
    key_part = jnp.einsum(
        "ahts,athd->ashd", grad_logits, query_tiles, preferred_element_type=jnp.float32
    ).reshape(tiles_dev * (LIST + 1), TILE, width)
    value_part = jnp.einsum(
        "ahts,athd->ashd", probs_half, grad_tiles, preferred_element_type=jnp.float32
    ).reshape(tiles_dev * (LIST + 1), TILE, width)
    flat_index = picked.reshape(-1)
    key_acc = jnp.zeros((window_tiles, TILE, width), jnp.float32).at[flat_index].add(key_part)
    value_acc = jnp.zeros((window_tiles, TILE, width), jnp.float32).at[flat_index].add(value_part)
    return (query_grad, key_acc, value_acc)


def per_device(
    lin_query,
    lin_key,
    lin_value,
    norm_gain,
    lin_grad,
    sm_query,
    sm_key,
    sm_value,
    sm_grad,
    tile_lists,
):
    token_count = lin_query.shape[0]
    lin_width = lin_query.shape[1]
    heads_lin = lin_width // HEAD
    query_lin = lin_query.reshape(token_count, heads_lin, HEAD)
    key_lin = lin_key.reshape(token_count, heads_lin, HEAD)
    value_lin = lin_value.reshape(token_count, heads_lin, HEAD)
    key_value = jnp.einsum("thi,thj->hij", key_lin, value_lin, preferred_element_type=jnp.float32)
    state_low = carried_in(key_value, False)
    state_half = state_low.astype(jnp.bfloat16)
    causal = jnp.tril(jnp.ones((token_count, token_count), jnp.bool_))
    attn_lin = jnp.where(
        causal[None],
        jnp.einsum("thd,shd->hts", query_lin, key_lin, preferred_element_type=jnp.float32),
        0.0,
    ).astype(jnp.bfloat16)
    output_lin = jnp.einsum(
        "hts,shd->thd", attn_lin, value_lin, preferred_element_type=jnp.float32
    ) + jnp.einsum("thi,hij->thj", query_lin, state_half, preferred_element_type=jnp.float32)
    gain_grad = norm_gain.reshape(1, heads_lin, HEAD) * lin_grad.reshape(
        token_count, heads_lin, HEAD
    ).astype(jnp.float32)
    square_sum = jnp.sum(output_lin * output_lin, axis=(1, 2))
    cross_sum = jnp.sum(gain_grad * output_lin, axis=(1, 2))
    sums = jnp.stack([square_sum, cross_sum])
    heads_dev = lax.axis_size("head")
    step = 1
    while step < heads_dev:
        sums = sums + lax.ppermute(sums, "head", [(i, i ^ step) for i in range(heads_dev)])
        step *= 2
    square_sum, cross_sum = sums[0], sums[1]
    full_width = LIN_HEADS * HEAD
    inv_rms = lax.rsqrt(square_sum / full_width + 1e-06)[:, None, None]
    grad_out = (
        gain_grad * inv_rms - output_lin * inv_rms**3 * (cross_sum / full_width)[:, None, None]
    ).astype(jnp.bfloat16)
    adjoint_local = jnp.einsum(
        "thi,thj->hij", query_lin, grad_out, preferred_element_type=jnp.float32
    )
    adjoint_high = carried_in(adjoint_local, True)
    adjoint_half = adjoint_high.astype(jnp.bfloat16)
    grad_scores = jnp.where(
        causal[None],
        jnp.einsum("thd,shd->hts", grad_out, value_lin, preferred_element_type=jnp.float32),
        0.0,
    ).astype(jnp.bfloat16)
    lin_dq = jnp.einsum(
        "hts,shd->thd", grad_scores, key_lin, preferred_element_type=jnp.float32
    ) + jnp.einsum("thj,hij->thi", grad_out, state_half, preferred_element_type=jnp.float32)
    lin_dk = jnp.einsum(
        "hts,thd->shd", grad_scores, query_lin, preferred_element_type=jnp.float32
    ) + jnp.einsum("shj,hij->shi", value_lin, adjoint_half, preferred_element_type=jnp.float32)
    lin_dv = jnp.einsum(
        "hts,thd->shd", attn_lin, grad_out, preferred_element_type=jnp.float32
    ) + jnp.einsum("shi,hij->shj", key_lin, adjoint_half, preferred_element_type=jnp.float32)
    lin_dq = lin_dq.reshape(token_count, lin_width).astype(jnp.bfloat16)
    lin_dk = lin_dk.reshape(token_count, lin_width).astype(jnp.bfloat16)
    lin_dv = lin_dv.reshape(token_count, lin_width).astype(jnp.bfloat16)
    width = sm_key.shape[1]
    pair = jnp.concatenate([sm_key, sm_value], axis=1)
    arrived = []
    moving = pair
    for distance in range(1, SPAN + 1):
        moving = from_behind(moving, CTX, 1)
        arrived.append(moving)
    key_window = jnp.concatenate(
        [arrived[SPAN - 1 - place][:, :width] for place in range(SPAN)] + [sm_key], axis=0
    )
    value_window = jnp.concatenate(
        [arrived[SPAN - 1 - place][:, width:] for place in range(SPAN)] + [sm_value], axis=0
    )
    shard = lax.axis_index(CTX)
    sm_dq, key_acc, value_acc = tile_attention(
        sm_query, sm_grad, key_window, value_window, tile_lists, shard
    )
    key_total = key_acc[SPAN]
    value_total = value_acc[SPAN]
    owed = None
    for distance in range(SPAN, 0, -1):
        term = jnp.concatenate(
            [key_acc[SPAN - distance], value_acc[SPAN - distance]], axis=1
        ).astype(jnp.bfloat16).astype(jnp.float32)
        owed = term if owed is None else owed + term
        owed = from_behind(owed.astype(jnp.bfloat16), CTX, -1).astype(jnp.float32)
    key_total = key_total + owed[:, :width]
    value_total = value_total + owed[:, width:]
    return (
        lin_dq,
        lin_dk,
        lin_dv,
        sm_dq,
        key_total.astype(jnp.bfloat16),
        value_total.astype(jnp.bfloat16),
    )


def solution(mesh):
    placed = (
        P(CTX, "head"),
        P(CTX, "head"),
        P(CTX, "head"),
        P("head"),
        P(CTX, "head"),
        P(CTX, "head"),
        P(CTX, "head"),
        P(CTX, "head"),
        P(CTX, "head"),
        P(CTX, None),
    )
    count = mesh.shape["ctx"]
    inner = INNER if count % INNER == 0 else 1
    split = jax.sharding.Mesh(
        mesh.devices.reshape(count // inner, inner, mesh.shape["head"]), CTX + ("head",)
    )
    return jax.shard_map(
        per_device,
        mesh=split,
        in_specs=placed,
        out_specs=(
            P(CTX, "head"),
            P(CTX, "head"),
            P(CTX, "head"),
            P(CTX, "head"),
            P(CTX, "head"),
            P(CTX, "head"),
        ),
        check_vma=False,
    )
```

```python
import math

import jax
import jax.numpy as jnp
from jax import lax
from jax.sharding import PartitionSpec as P

HEAD = 128
LIN_HEADS = 16
TILE = 128
LIST = 3
SPAN = 4


CTX = ("outer", "inner")
INNER = 32
PLAN = (4,)


def scan_over(total, axis, backward):
    count = lax.axis_size(axis)
    plan = PLAN
    if math.prod(plan) != count:
        plan = (2,) * max(1, (count - 1).bit_length())
    own = total
    stride = 1
    for radix in plan:
        arrived = []
        for step in range(1, radix):
            distance = step * stride
            if distance >= count:
                break
            if backward:
                pairs = [(i, i - distance) for i in range(distance, count)]
            else:
                pairs = [(i, i + distance) for i in range(count - distance)]
            arrived.append(lax.ppermute(total.astype(jnp.bfloat16), axis, pairs))
        for part in arrived:
            total = total + part.astype(jnp.float32)
        stride *= radix
    return total - own


def carried_in(shard, backward):
    members = lax.axis_size("inner")
    slices = shard.astype(jnp.bfloat16).reshape(members, -1)
    mine = lax.all_to_all(slices, "inner", 0, 0, tiled=True).astype(jnp.float32)
    running = jnp.cumsum(mine, axis=0)
    group = jnp.sum(mine, axis=0)
    within = group[None] - running if backward else running - mine
    earlier = scan_over(group, "outer", backward)
    states = (within + earlier[None]).astype(jnp.bfloat16)
    back = lax.all_to_all(states, "inner", 0, 0, tiled=True)
    return back.reshape(shard.shape).astype(shard.dtype)


def from_behind(shard, axis, by):
    length = lax.axis_size(axis)
    pairs = [(i, i + by) for i in range(length) if 0 <= i + by < length]
    return lax.ppermute(shard, axis, pairs)


def add_states(earlier, later):
    return earlier + later


def tile_attention(query, grad, key_window, value_window, lists, shard):
    token_count, width = query.shape
    heads = width // HEAD
    tiles_dev = token_count // TILE
    window_tiles = key_window.shape[0] // TILE
    valid = lists >= 0
    local_index = jnp.where(valid, lists - (shard - SPAN) * tiles_dev, 0)
    own_index = (SPAN * tiles_dev + jnp.arange(tiles_dev, dtype=jnp.int32))[:, None]
    picked = jnp.concatenate([own_index, local_index], axis=1)
    keep = jnp.concatenate([jnp.ones((tiles_dev, 1), jnp.bool_), valid], axis=1)
    key_set = key_window.reshape(window_tiles, TILE, heads, HEAD)[picked].reshape(
        tiles_dev, (LIST + 1) * TILE, heads, HEAD
    )
    value_set = value_window.reshape(window_tiles, TILE, heads, HEAD)[picked].reshape(
        tiles_dev, (LIST + 1) * TILE, heads, HEAD
    )
    query_tiles = query.reshape(tiles_dev, TILE, heads, HEAD)
    grad_tiles = grad.reshape(tiles_dev, TILE, heads, HEAD)
    scale = HEAD ** (-0.5)
    scores = (
        jnp.einsum("athd,ashd->ahts", query_tiles, key_set, preferred_element_type=jnp.float32)
        * scale
    )
    rows_idx = jnp.arange(TILE)[:, None]
    cols_idx = jnp.arange((LIST + 1) * TILE)[None, :]
    allowed = jnp.where(cols_idx // TILE == 0, cols_idx % TILE <= rows_idx, True)
    live = jnp.repeat(keep, TILE, axis=1)
    allowed_all = allowed[None, None, :, :] & live[:, None, None, :]
    scores = jnp.where(allowed_all, scores, -jnp.inf)
    top_score = jnp.max(scores, axis=-1, keepdims=True)
    expo = jnp.exp(scores - top_score)
    probs = expo / jnp.sum(expo, axis=-1, keepdims=True)
    probs_half = probs.astype(jnp.bfloat16)
    attended = jnp.einsum(
        "ahts,ashd->athd", probs_half, value_set, preferred_element_type=jnp.float32
    )
    delta = jnp.transpose(jnp.sum(grad_tiles.astype(jnp.float32) * attended, axis=-1), (0, 2, 1))[
        ..., None
    ]
    grad_probs = jnp.einsum(
        "athd,ashd->ahts", grad_tiles, value_set, preferred_element_type=jnp.float32
    )
    grad_logits = (probs * (grad_probs - delta) * scale).astype(jnp.bfloat16)
    query_grad = (
        jnp.einsum("ahts,ashd->athd", grad_logits, key_set, preferred_element_type=jnp.float32)
        .reshape(token_count, width)
        .astype(jnp.bfloat16)
    )
    key_part = jnp.einsum(
        "ahts,athd->ashd", grad_logits, query_tiles, preferred_element_type=jnp.float32
    ).reshape(tiles_dev * (LIST + 1), TILE, width)
    value_part = jnp.einsum(
        "ahts,athd->ashd", probs_half, grad_tiles, preferred_element_type=jnp.float32
    ).reshape(tiles_dev * (LIST + 1), TILE, width)
    flat_index = picked.reshape(-1)
    key_acc = jnp.zeros((window_tiles, TILE, width), jnp.float32).at[flat_index].add(key_part)
    value_acc = jnp.zeros((window_tiles, TILE, width), jnp.float32).at[flat_index].add(value_part)
    return (query_grad, key_acc, value_acc)


def per_device(
    lin_query,
    lin_key,
    lin_value,
    norm_gain,
    lin_grad,
    sm_query,
    sm_key,
    sm_value,
    sm_grad,
    tile_lists,
):
    token_count = lin_query.shape[0]
    lin_width = lin_query.shape[1]
    heads_lin = lin_width // HEAD
    query_lin = lin_query.reshape(token_count, heads_lin, HEAD)
    key_lin = lin_key.reshape(token_count, heads_lin, HEAD)
    value_lin = lin_value.reshape(token_count, heads_lin, HEAD)
    key_value = jnp.einsum("thi,thj->hij", key_lin, value_lin, preferred_element_type=jnp.float32)
    state_low = carried_in(key_value, False)
    state_half = state_low.astype(jnp.bfloat16)
    causal = jnp.tril(jnp.ones((token_count, token_count), jnp.bool_))
    attn_lin = jnp.where(
        causal[None],
        jnp.einsum("thd,shd->hts", query_lin, key_lin, preferred_element_type=jnp.float32),
        0.0,
    ).astype(jnp.bfloat16)
    output_lin = jnp.einsum(
        "hts,shd->thd", attn_lin, value_lin, preferred_element_type=jnp.float32
    ) + jnp.einsum("thi,hij->thj", query_lin, state_half, preferred_element_type=jnp.float32)
    gain_grad = norm_gain.reshape(1, heads_lin, HEAD) * lin_grad.reshape(
        token_count, heads_lin, HEAD
    ).astype(jnp.float32)
    square_sum = jnp.sum(output_lin * output_lin, axis=(1, 2))
    cross_sum = jnp.sum(gain_grad * output_lin, axis=(1, 2))
    sums = jnp.stack([square_sum, cross_sum])
    heads_dev = lax.axis_size("head")
    step = 1
    while step < heads_dev:
        sums = sums + lax.ppermute(sums, "head", [(i, i ^ step) for i in range(heads_dev)])
        step *= 2
    square_sum, cross_sum = sums[0], sums[1]
    full_width = LIN_HEADS * HEAD
    inv_rms = lax.rsqrt(square_sum / full_width + 1e-06)[:, None, None]
    grad_out = (
        gain_grad * inv_rms - output_lin * inv_rms**3 * (cross_sum / full_width)[:, None, None]
    ).astype(jnp.bfloat16)
    adjoint_local = jnp.einsum(
        "thi,thj->hij", query_lin, grad_out, preferred_element_type=jnp.float32
    )
    adjoint_high = carried_in(adjoint_local, True)
    adjoint_half = adjoint_high.astype(jnp.bfloat16)
    grad_scores = jnp.where(
        causal[None],
        jnp.einsum("thd,shd->hts", grad_out, value_lin, preferred_element_type=jnp.float32),
        0.0,
    ).astype(jnp.bfloat16)
    lin_dq = jnp.einsum(
        "hts,shd->thd", grad_scores, key_lin, preferred_element_type=jnp.float32
    ) + jnp.einsum("thj,hij->thi", grad_out, state_half, preferred_element_type=jnp.float32)
    lin_dk = jnp.einsum(
        "hts,thd->shd", grad_scores, query_lin, preferred_element_type=jnp.float32
    ) + jnp.einsum("shj,hij->shi", value_lin, adjoint_half, preferred_element_type=jnp.float32)
    lin_dv = jnp.einsum(
        "hts,thd->shd", attn_lin, grad_out, preferred_element_type=jnp.float32
    ) + jnp.einsum("shi,hij->shj", key_lin, adjoint_half, preferred_element_type=jnp.float32)
    lin_dq = lin_dq.reshape(token_count, lin_width).astype(jnp.bfloat16)
    lin_dk = lin_dk.reshape(token_count, lin_width).astype(jnp.bfloat16)
    lin_dv = lin_dv.reshape(token_count, lin_width).astype(jnp.bfloat16)
    width = sm_key.shape[1]
    pair = jnp.concatenate([sm_key, sm_value], axis=1)
    arrived = [from_behind(pair, CTX, distance) for distance in range(1, SPAN + 1)]
    key_window = jnp.concatenate(
        [arrived[SPAN - 1 - place][:, :width] for place in range(SPAN)] + [sm_key], axis=0
    )
    value_window = jnp.concatenate(
        [arrived[SPAN - 1 - place][:, width:] for place in range(SPAN)] + [sm_value], axis=0
    )
    shard = lax.axis_index(CTX)
    sm_dq, key_acc, value_acc = tile_attention(
        sm_query, sm_grad, key_window, value_window, tile_lists, shard
    )
    key_total = key_acc[SPAN]
    value_total = value_acc[SPAN]
    for distance in range(1, SPAN + 1):
        back = from_behind(
            jnp.concatenate(
                [key_acc[SPAN - distance], value_acc[SPAN - distance]], axis=1
            ).astype(jnp.bfloat16),
            CTX,
            -distance,
        ).astype(jnp.float32)
        key_total = key_total + back[:, :width]
        value_total = value_total + back[:, width:]
    return (
        lin_dq,
        lin_dk,
        lin_dv,
        sm_dq,
        key_total.astype(jnp.bfloat16),
        value_total.astype(jnp.bfloat16),
    )


def solution(mesh):
    placed = (
        P(CTX, "head"),
        P(CTX, "head"),
        P(CTX, "head"),
        P("head"),
        P(CTX, "head"),
        P(CTX, "head"),
        P(CTX, "head"),
        P(CTX, "head"),
        P(CTX, "head"),
        P(CTX, None),
    )
    count = mesh.shape["ctx"]
    inner = INNER if count % INNER == 0 else 1
    split = jax.sharding.Mesh(
        mesh.devices.reshape(count // inner, inner, mesh.shape["head"]), CTX + ("head",)
    )
    return jax.shard_map(
        per_device,
        mesh=split,
        in_specs=placed,
        out_specs=(
            P(CTX, "head"),
            P(CTX, "head"),
            P(CTX, "head"),
            P(CTX, "head"),
            P(CTX, "head"),
            P(CTX, "head"),
        ),
        check_vma=False,
    )
```

```python
import math

import jax
import jax.numpy as jnp
from jax import lax
from jax.sharding import PartitionSpec as P

HEAD = 128
LIN_HEADS = 16
TILE = 128
LIST = 3
SPAN = 4


CTX = ("outer", "inner")
INNER = 32
PLAN = (4,)


def scan_over(total, axis, backward):
    count = lax.axis_size(axis)
    plan = PLAN
    if math.prod(plan) != count:
        plan = (2,) * max(1, (count - 1).bit_length())
    own = total
    stride = 1
    for radix in plan:
        arrived = []
        for step in range(1, radix):
            distance = step * stride
            if distance >= count:
                break
            if backward:
                pairs = [(i, i - distance) for i in range(distance, count)]
            else:
                pairs = [(i, i + distance) for i in range(count - distance)]
            arrived.append(lax.ppermute(total.astype(jnp.bfloat16), axis, pairs))
        for part in arrived:
            total = total + part.astype(jnp.float32)
        stride *= radix
    return total - own


def carried_in(shard, backward):
    members = lax.axis_size("inner")
    slices = shard.astype(jnp.bfloat16).reshape(members, -1)
    mine = lax.all_to_all(slices, "inner", 0, 0, tiled=True).astype(jnp.float32)
    running = jnp.cumsum(mine, axis=0)
    group = jnp.sum(mine, axis=0)
    within = group[None] - running if backward else running - mine
    earlier = scan_over(group, "outer", backward)
    states = (within + earlier[None]).astype(jnp.bfloat16)
    back = lax.all_to_all(states, "inner", 0, 0, tiled=True)
    return back.reshape(shard.shape).astype(shard.dtype)


def from_behind(shard, axis, by):
    length = lax.axis_size(axis)
    pairs = [(i, i + by) for i in range(length) if 0 <= i + by < length]
    return lax.ppermute(shard, axis, pairs)


def add_states(earlier, later):
    return earlier + later


def tile_attention(query, grad, key_window, value_window, lists, shard):
    token_count, width = query.shape
    heads = width // HEAD
    tiles_dev = token_count // TILE
    window_tiles = key_window.shape[0] // TILE
    valid = lists >= 0
    local_index = jnp.where(valid, lists - (shard - SPAN) * tiles_dev, 0)
    own_index = (SPAN * tiles_dev + jnp.arange(tiles_dev, dtype=jnp.int32))[:, None]
    picked = jnp.concatenate([own_index, local_index], axis=1)
    keep = jnp.concatenate([jnp.ones((tiles_dev, 1), jnp.bool_), valid], axis=1)
    key_set = key_window.reshape(window_tiles, TILE, heads, HEAD)[picked].reshape(
        tiles_dev, (LIST + 1) * TILE, heads, HEAD
    )
    value_set = value_window.reshape(window_tiles, TILE, heads, HEAD)[picked].reshape(
        tiles_dev, (LIST + 1) * TILE, heads, HEAD
    )
    query_tiles = query.reshape(tiles_dev, TILE, heads, HEAD)
    grad_tiles = grad.reshape(tiles_dev, TILE, heads, HEAD)
    scale = HEAD ** (-0.5)
    scores = (
        jnp.einsum("athd,ashd->ahts", query_tiles, key_set, preferred_element_type=jnp.float32)
        * scale
    )
    rows_idx = jnp.arange(TILE)[:, None]
    cols_idx = jnp.arange((LIST + 1) * TILE)[None, :]
    allowed = jnp.where(cols_idx // TILE == 0, cols_idx % TILE <= rows_idx, True)
    live = jnp.repeat(keep, TILE, axis=1)
    allowed_all = allowed[None, None, :, :] & live[:, None, None, :]
    scores = jnp.where(allowed_all, scores, -jnp.inf)
    top_score = jnp.max(scores, axis=-1, keepdims=True)
    expo = jnp.exp(scores - top_score)
    probs = expo / jnp.sum(expo, axis=-1, keepdims=True)
    probs_half = probs.astype(jnp.bfloat16)
    attended = jnp.einsum(
        "ahts,ashd->athd", probs_half, value_set, preferred_element_type=jnp.float32
    )
    delta = jnp.transpose(jnp.sum(grad_tiles.astype(jnp.float32) * attended, axis=-1), (0, 2, 1))[
        ..., None
    ]
    grad_probs = jnp.einsum(
        "athd,ashd->ahts", grad_tiles, value_set, preferred_element_type=jnp.float32
    )
    grad_logits = (probs * (grad_probs - delta) * scale).astype(jnp.bfloat16)
    query_grad = (
        jnp.einsum("ahts,ashd->athd", grad_logits, key_set, preferred_element_type=jnp.float32)
        .reshape(token_count, width)
        .astype(jnp.bfloat16)
    )
    key_part = jnp.einsum(
        "ahts,athd->ashd", grad_logits, query_tiles, preferred_element_type=jnp.float32
    ).reshape(tiles_dev * (LIST + 1), TILE, width)
    value_part = jnp.einsum(
        "ahts,athd->ashd", probs_half, grad_tiles, preferred_element_type=jnp.float32
    ).reshape(tiles_dev * (LIST + 1), TILE, width)
    flat_index = picked.reshape(-1)
    key_acc = jnp.zeros((window_tiles, TILE, width), jnp.float32).at[flat_index].add(key_part)
    value_acc = jnp.zeros((window_tiles, TILE, width), jnp.float32).at[flat_index].add(value_part)
    return (query_grad, key_acc, value_acc)


def per_device(
    lin_query,
    lin_key,
    lin_value,
    norm_gain,
    lin_grad,
    sm_query,
    sm_key,
    sm_value,
    sm_grad,
    tile_lists,
):
    token_count = lin_query.shape[0]
    lin_width = lin_query.shape[1]
    heads_lin = lin_width // HEAD
    query_lin = lin_query.reshape(token_count, heads_lin, HEAD)
    key_lin = lin_key.reshape(token_count, heads_lin, HEAD)
    value_lin = lin_value.reshape(token_count, heads_lin, HEAD)
    key_value = jnp.einsum("thi,thj->hij", key_lin, value_lin, preferred_element_type=jnp.float32)
    state_low = carried_in(key_value, False)
    state_half = state_low.astype(jnp.bfloat16)
    causal = jnp.tril(jnp.ones((token_count, token_count), jnp.bool_))
    attn_lin = jnp.where(
        causal[None],
        jnp.einsum("thd,shd->hts", query_lin, key_lin, preferred_element_type=jnp.float32),
        0.0,
    ).astype(jnp.bfloat16)
    output_lin = jnp.einsum(
        "hts,shd->thd", attn_lin, value_lin, preferred_element_type=jnp.float32
    ) + jnp.einsum("thi,hij->thj", query_lin, state_half, preferred_element_type=jnp.float32)
    gain_grad = norm_gain.reshape(1, heads_lin, HEAD) * lin_grad.reshape(
        token_count, heads_lin, HEAD
    ).astype(jnp.float32)
    square_sum = jnp.sum(output_lin * output_lin, axis=(1, 2))
    cross_sum = jnp.sum(gain_grad * output_lin, axis=(1, 2))
    sums = jnp.stack([square_sum, cross_sum])
    heads_dev = lax.axis_size("head")
    step = 1
    while step < heads_dev:
        sums = sums + lax.ppermute(sums, "head", [(i, i ^ step) for i in range(heads_dev)])
        step *= 2
    square_sum, cross_sum = sums[0], sums[1]
    full_width = LIN_HEADS * HEAD
    inv_rms = lax.rsqrt(square_sum / full_width + 1e-06)[:, None, None]
    grad_out = (
        gain_grad * inv_rms - output_lin * inv_rms**3 * (cross_sum / full_width)[:, None, None]
    ).astype(jnp.bfloat16)
    adjoint_local = jnp.einsum(
        "thi,thj->hij", query_lin, grad_out, preferred_element_type=jnp.float32
    )
    adjoint_high = carried_in(adjoint_local, True)
    adjoint_half = adjoint_high.astype(jnp.bfloat16)
    grad_scores = jnp.where(
        causal[None],
        jnp.einsum("thd,shd->hts", grad_out, value_lin, preferred_element_type=jnp.float32),
        0.0,
    ).astype(jnp.bfloat16)
    lin_dq = jnp.einsum(
        "hts,shd->thd", grad_scores, key_lin, preferred_element_type=jnp.float32
    ) + jnp.einsum("thj,hij->thi", grad_out, state_half, preferred_element_type=jnp.float32)
    lin_dk = jnp.einsum(
        "hts,thd->shd", grad_scores, query_lin, preferred_element_type=jnp.float32
    ) + jnp.einsum("shj,hij->shi", value_lin, adjoint_half, preferred_element_type=jnp.float32)
    lin_dv = jnp.einsum(
        "hts,thd->shd", attn_lin, grad_out, preferred_element_type=jnp.float32
    ) + jnp.einsum("shi,hij->shj", key_lin, adjoint_half, preferred_element_type=jnp.float32)
    lin_dq = lin_dq.reshape(token_count, lin_width).astype(jnp.bfloat16)
    lin_dk = lin_dk.reshape(token_count, lin_width).astype(jnp.bfloat16)
    lin_dv = lin_dv.reshape(token_count, lin_width).astype(jnp.bfloat16)
    width = sm_key.shape[1]
    pair = jnp.concatenate([sm_key, sm_value], axis=1)
    arrived = [from_behind(pair, CTX, distance) for distance in range(1, SPAN + 1)]
    key_window = jnp.concatenate(
        [arrived[SPAN - 1 - place][:, :width] for place in range(SPAN)] + [sm_key], axis=0
    )
    value_window = jnp.concatenate(
        [arrived[SPAN - 1 - place][:, width:] for place in range(SPAN)] + [sm_value], axis=0
    )
    shard = lax.axis_index(CTX)
    sm_dq, key_acc, value_acc = tile_attention(
        sm_query, sm_grad, key_window, value_window, tile_lists, shard
    )
    key_total = key_acc[SPAN]
    value_total = value_acc[SPAN]
    owed = None
    for distance in range(SPAN, 0, -1):
        term = jnp.concatenate(
            [key_acc[SPAN - distance], value_acc[SPAN - distance]], axis=1
        ).astype(jnp.bfloat16).astype(jnp.float32)
        owed = term if owed is None else owed + term
        owed = from_behind(owed.astype(jnp.bfloat16), CTX, -1).astype(jnp.float32)
    key_total = key_total + owed[:, :width]
    value_total = value_total + owed[:, width:]
    return (
        lin_dq,
        lin_dk,
        lin_dv,
        sm_dq,
        key_total.astype(jnp.bfloat16),
        value_total.astype(jnp.bfloat16),
    )


def solution(mesh):
    placed = (
        P(CTX, "head"),
        P(CTX, "head"),
        P(CTX, "head"),
        P("head"),
        P(CTX, "head"),
        P(CTX, "head"),
        P(CTX, "head"),
        P(CTX, "head"),
        P(CTX, "head"),
        P(CTX, None),
    )
    count = mesh.shape["ctx"]
    inner = INNER if count % INNER == 0 else 1
    split = jax.sharding.Mesh(
        mesh.devices.reshape(count // inner, inner, mesh.shape["head"]), CTX + ("head",)
    )
    return jax.shard_map(
        per_device,
        mesh=split,
        in_specs=placed,
        out_specs=(
            P(CTX, "head"),
            P(CTX, "head"),
            P(CTX, "head"),
            P(CTX, "head"),
            P(CTX, "head"),
            P(CTX, "head"),
        ),
        check_vma=False,
    )
```

```python
import math

import jax
import jax.numpy as jnp
from jax import lax
from jax.sharding import PartitionSpec as P

HEAD = 128
LIN_HEADS = 16
TILE = 128
LIST = 3
SPAN = 4


CTX = ("outer", "inner")
INNER = 32
PLAN = (4,)


def scan_over(total, axis, backward):
    count = lax.axis_size(axis)
    plan = PLAN
    if math.prod(plan) != count:
        plan = (2,) * max(1, (count - 1).bit_length())
    own = total
    stride = 1
    for radix in plan:
        arrived = []
        for step in range(1, radix):
            distance = step * stride
            if distance >= count:
                break
            if backward:
                pairs = [(i, i - distance) for i in range(distance, count)]
            else:
                pairs = [(i, i + distance) for i in range(count - distance)]
            arrived.append(lax.ppermute(total.astype(jnp.bfloat16), axis, pairs))
        for part in arrived:
            total = total + part.astype(jnp.float32)
        stride *= radix
    return total - own


def carried_in(shard, backward):
    members = lax.axis_size("inner")
    slices = shard.astype(jnp.bfloat16).reshape(members, -1)
    mine = lax.all_to_all(slices, "inner", 0, 0, tiled=True).astype(jnp.float32)
    running = jnp.cumsum(mine, axis=0)
    group = jnp.sum(mine, axis=0)
    within = group[None] - running if backward else running - mine
    earlier = scan_over(group, "outer", backward)
    states = (within + earlier[None]).astype(jnp.bfloat16)
    back = lax.all_to_all(states, "inner", 0, 0, tiled=True)
    return back.reshape(shard.shape).astype(shard.dtype)


def from_behind(shard, axis, by):
    length = lax.axis_size(axis)
    pairs = [(i, i + by) for i in range(length) if 0 <= i + by < length]
    return lax.ppermute(shard, axis, pairs)


def add_states(earlier, later):
    return earlier + later


def tile_attention(query, grad, key_window, value_window, lists, shard):
    token_count, width = query.shape
    heads = width // HEAD
    tiles_dev = token_count // TILE
    window_tiles = key_window.shape[0] // TILE
    valid = lists >= 0
    local_index = jnp.where(valid, lists - (shard - SPAN) * tiles_dev, 0)
    own_index = (SPAN * tiles_dev + jnp.arange(tiles_dev, dtype=jnp.int32))[:, None]
    picked = jnp.concatenate([own_index, local_index], axis=1)
    keep = jnp.concatenate([jnp.ones((tiles_dev, 1), jnp.bool_), valid], axis=1)
    key_set = key_window.reshape(window_tiles, TILE, heads, HEAD)[picked].reshape(
        tiles_dev, (LIST + 1) * TILE, heads, HEAD
    )
    value_set = value_window.reshape(window_tiles, TILE, heads, HEAD)[picked].reshape(
        tiles_dev, (LIST + 1) * TILE, heads, HEAD
    )
    query_tiles = query.reshape(tiles_dev, TILE, heads, HEAD)
    grad_tiles = grad.reshape(tiles_dev, TILE, heads, HEAD)
    scale = HEAD ** (-0.5)
    scores = (
        jnp.einsum("athd,ashd->ahts", query_tiles, key_set, preferred_element_type=jnp.float32)
        * scale
    )
    rows_idx = jnp.arange(TILE)[:, None]
    cols_idx = jnp.arange((LIST + 1) * TILE)[None, :]
    allowed = jnp.where(cols_idx // TILE == 0, cols_idx % TILE <= rows_idx, True)
    live = jnp.repeat(keep, TILE, axis=1)
    allowed_all = allowed[None, None, :, :] & live[:, None, None, :]
    scores = jnp.where(allowed_all, scores, -jnp.inf)
    top_score = jnp.max(scores, axis=-1, keepdims=True)
    expo = jnp.exp(scores - top_score)
    probs = expo / jnp.sum(expo, axis=-1, keepdims=True)
    probs_half = probs.astype(jnp.bfloat16)
    attended = jnp.einsum(
        "ahts,ashd->athd", probs_half, value_set, preferred_element_type=jnp.float32
    )
    delta = jnp.transpose(jnp.sum(grad_tiles.astype(jnp.float32) * attended, axis=-1), (0, 2, 1))[
        ..., None
    ]
    grad_probs = jnp.einsum(
        "athd,ashd->ahts", grad_tiles, value_set, preferred_element_type=jnp.float32
    )
    grad_logits = (probs * (grad_probs - delta) * scale).astype(jnp.bfloat16)
    query_grad = (
        jnp.einsum("ahts,ashd->athd", grad_logits, key_set, preferred_element_type=jnp.float32)
        .reshape(token_count, width)
        .astype(jnp.bfloat16)
    )
    key_part = jnp.einsum(
        "ahts,athd->ashd", grad_logits, query_tiles, preferred_element_type=jnp.float32
    ).reshape(tiles_dev * (LIST + 1), TILE, width)
    value_part = jnp.einsum(
        "ahts,athd->ashd", probs_half, grad_tiles, preferred_element_type=jnp.float32
    ).reshape(tiles_dev * (LIST + 1), TILE, width)
    flat_index = picked.reshape(-1)
    key_acc = jnp.zeros((window_tiles, TILE, width), jnp.float32).at[flat_index].add(key_part)
    value_acc = jnp.zeros((window_tiles, TILE, width), jnp.float32).at[flat_index].add(value_part)
    return (query_grad, key_acc, value_acc)


def per_device(
    lin_query,
    lin_key,
    lin_value,
    norm_gain,
    lin_grad,
    sm_query,
    sm_key,
    sm_value,
    sm_grad,
    tile_lists,
):
    token_count = lin_query.shape[0]
    lin_width = lin_query.shape[1]
    heads_lin = lin_width // HEAD
    query_lin = lin_query.reshape(token_count, heads_lin, HEAD)
    key_lin = lin_key.reshape(token_count, heads_lin, HEAD)
    value_lin = lin_value.reshape(token_count, heads_lin, HEAD)
    key_value = jnp.einsum("thi,thj->hij", key_lin, value_lin, preferred_element_type=jnp.float32)
    state_low = carried_in(key_value, False)
    state_half = state_low.astype(jnp.bfloat16)
    causal = jnp.tril(jnp.ones((token_count, token_count), jnp.bool_))
    attn_lin = jnp.where(
        causal[None],
        jnp.einsum("thd,shd->hts", query_lin, key_lin, preferred_element_type=jnp.float32),
        0.0,
    ).astype(jnp.bfloat16)
    output_lin = jnp.einsum(
        "hts,shd->thd", attn_lin, value_lin, preferred_element_type=jnp.float32
    ) + jnp.einsum("thi,hij->thj", query_lin, state_half, preferred_element_type=jnp.float32)
    gain_grad = norm_gain.reshape(1, heads_lin, HEAD) * lin_grad.reshape(
        token_count, heads_lin, HEAD
    ).astype(jnp.float32)
    square_sum = jnp.sum(output_lin * output_lin, axis=(1, 2))
    cross_sum = jnp.sum(gain_grad * output_lin, axis=(1, 2))
    sums = jnp.stack([square_sum, cross_sum])
    heads_dev = lax.axis_size("head")
    spread = jnp.broadcast_to(sums[None], (heads_dev,) + sums.shape)
    sums = jnp.sum(lax.all_to_all(spread, "head", 0, 0, tiled=True), axis=0)
    square_sum, cross_sum = sums[0], sums[1]
    full_width = LIN_HEADS * HEAD
    inv_rms = lax.rsqrt(square_sum / full_width + 1e-06)[:, None, None]
    grad_out = (
        gain_grad * inv_rms - output_lin * inv_rms**3 * (cross_sum / full_width)[:, None, None]
    ).astype(jnp.bfloat16)
    adjoint_local = jnp.einsum(
        "thi,thj->hij", query_lin, grad_out, preferred_element_type=jnp.float32
    )
    adjoint_high = carried_in(adjoint_local, True)
    adjoint_half = adjoint_high.astype(jnp.bfloat16)
    grad_scores = jnp.where(
        causal[None],
        jnp.einsum("thd,shd->hts", grad_out, value_lin, preferred_element_type=jnp.float32),
        0.0,
    ).astype(jnp.bfloat16)
    lin_dq = jnp.einsum(
        "hts,shd->thd", grad_scores, key_lin, preferred_element_type=jnp.float32
    ) + jnp.einsum("thj,hij->thi", grad_out, state_half, preferred_element_type=jnp.float32)
    lin_dk = jnp.einsum(
        "hts,thd->shd", grad_scores, query_lin, preferred_element_type=jnp.float32
    ) + jnp.einsum("shj,hij->shi", value_lin, adjoint_half, preferred_element_type=jnp.float32)
    lin_dv = jnp.einsum(
        "hts,thd->shd", attn_lin, grad_out, preferred_element_type=jnp.float32
    ) + jnp.einsum("shi,hij->shj", key_lin, adjoint_half, preferred_element_type=jnp.float32)
    lin_dq = lin_dq.reshape(token_count, lin_width).astype(jnp.bfloat16)
    lin_dk = lin_dk.reshape(token_count, lin_width).astype(jnp.bfloat16)
    lin_dv = lin_dv.reshape(token_count, lin_width).astype(jnp.bfloat16)
    width = sm_key.shape[1]
    pair = jnp.concatenate([sm_key, sm_value], axis=1)
    arrived = []
    moving = pair
    for distance in range(1, SPAN + 1):
        moving = from_behind(moving, CTX, 1)
        arrived.append(moving)
    key_window = jnp.concatenate(
        [arrived[SPAN - 1 - place][:, :width] for place in range(SPAN)] + [sm_key], axis=0
    )
    value_window = jnp.concatenate(
        [arrived[SPAN - 1 - place][:, width:] for place in range(SPAN)] + [sm_value], axis=0
    )
    shard = lax.axis_index(CTX)
    sm_dq, key_acc, value_acc = tile_attention(
        sm_query, sm_grad, key_window, value_window, tile_lists, shard
    )
    key_total = key_acc[SPAN]
    value_total = value_acc[SPAN]
    owed = None
    for distance in range(SPAN, 0, -1):
        term = jnp.concatenate(
            [key_acc[SPAN - distance], value_acc[SPAN - distance]], axis=1
        ).astype(jnp.bfloat16).astype(jnp.float32)
        owed = term if owed is None else owed + term
        owed = from_behind(owed.astype(jnp.bfloat16), CTX, -1).astype(jnp.float32)
    key_total = key_total + owed[:, :width]
    value_total = value_total + owed[:, width:]
    return (
        lin_dq,
        lin_dk,
        lin_dv,
        sm_dq,
        key_total.astype(jnp.bfloat16),
        value_total.astype(jnp.bfloat16),
    )


def solution(mesh):
    placed = (
        P(CTX, "head"),
        P(CTX, "head"),
        P(CTX, "head"),
        P("head"),
        P(CTX, "head"),
        P(CTX, "head"),
        P(CTX, "head"),
        P(CTX, "head"),
        P(CTX, "head"),
        P(CTX, None),
    )
    count = mesh.shape["ctx"]
    inner = INNER if count % INNER == 0 else 1
    split = jax.sharding.Mesh(
        mesh.devices.reshape(count // inner, inner, mesh.shape["head"]), CTX + ("head",)
    )
    return jax.shard_map(
        per_device,
        mesh=split,
        in_specs=placed,
        out_specs=(
            P(CTX, "head"),
            P(CTX, "head"),
            P(CTX, "head"),
            P(CTX, "head"),
            P(CTX, "head"),
            P(CTX, "head"),
        ),
        check_vma=False,
    )
```

```python
import math

import jax
import jax.numpy as jnp
from jax import lax
from jax.sharding import PartitionSpec as P

HEAD = 128
LIN_HEADS = 16
TILE = 128
LIST = 3
SPAN = 4


CTX = ("outer", "inner")
INNER = 32
PLAN = (4,)


def scan_over(total, axis, backward):
    count = lax.axis_size(axis)
    plan = PLAN
    if math.prod(plan) != count:
        plan = (2,) * max(1, (count - 1).bit_length())
    own = total
    stride = 1
    for radix in plan:
        arrived = []
        for step in range(1, radix):
            distance = step * stride
            if distance >= count:
                break
            if backward:
                pairs = [(i, i - distance) for i in range(distance, count)]
            else:
                pairs = [(i, i + distance) for i in range(count - distance)]
            arrived.append(lax.ppermute(total.astype(jnp.bfloat16), axis, pairs))
        for part in arrived:
            total = total + part.astype(jnp.float32)
        stride *= radix
    return total - own


def carried_in(shard, backward):
    members = lax.axis_size("inner")
    slices = shard.astype(jnp.bfloat16).reshape(members, -1)
    mine = lax.all_to_all(slices, "inner", 0, 0, tiled=True).astype(jnp.float32)
    running = jnp.cumsum(mine, axis=0)
    group = jnp.sum(mine, axis=0)
    within = group[None] - running if backward else running - mine
    earlier = scan_over(group, "outer", backward)
    states = (within + earlier[None]).astype(jnp.bfloat16)
    back = lax.all_to_all(states, "inner", 0, 0, tiled=True)
    return back.reshape(shard.shape).astype(shard.dtype)


def from_behind(shard, axis, by):
    length = lax.axis_size(axis)
    pairs = [(i, i + by) for i in range(length) if 0 <= i + by < length]
    return lax.ppermute(shard, axis, pairs)


def add_states(earlier, later):
    return earlier + later


def tile_attention(query, grad, key_window, value_window, lists, shard):
    token_count, width = query.shape
    heads = width // HEAD
    tiles_dev = token_count // TILE
    window_tiles = key_window.shape[0] // TILE
    valid = lists >= 0
    local_index = jnp.where(valid, lists - (shard - SPAN) * tiles_dev, 0)
    own_index = (SPAN * tiles_dev + jnp.arange(tiles_dev, dtype=jnp.int32))[:, None]
    picked = jnp.concatenate([own_index, local_index], axis=1)
    keep = jnp.concatenate([jnp.ones((tiles_dev, 1), jnp.bool_), valid], axis=1)
    key_set = key_window.reshape(window_tiles, TILE, heads, HEAD)[picked].reshape(
        tiles_dev, (LIST + 1) * TILE, heads, HEAD
    )
    value_set = value_window.reshape(window_tiles, TILE, heads, HEAD)[picked].reshape(
        tiles_dev, (LIST + 1) * TILE, heads, HEAD
    )
    query_tiles = query.reshape(tiles_dev, TILE, heads, HEAD)
    grad_tiles = grad.reshape(tiles_dev, TILE, heads, HEAD)
    scale = HEAD ** (-0.5)
    scores = (
        jnp.einsum("athd,ashd->ahts", query_tiles, key_set, preferred_element_type=jnp.float32)
        * scale
    )
    rows_idx = jnp.arange(TILE)[:, None]
    cols_idx = jnp.arange((LIST + 1) * TILE)[None, :]
    allowed = jnp.where(cols_idx // TILE == 0, cols_idx % TILE <= rows_idx, True)
    live = jnp.repeat(keep, TILE, axis=1)
    allowed_all = allowed[None, None, :, :] & live[:, None, None, :]
    scores = jnp.where(allowed_all, scores, -jnp.inf)
    top_score = jnp.max(scores, axis=-1, keepdims=True)
    expo = jnp.exp(scores - top_score)
    probs = expo / jnp.sum(expo, axis=-1, keepdims=True)
    probs_half = probs.astype(jnp.bfloat16)
    attended = jnp.einsum(
        "ahts,ashd->athd", probs_half, value_set, preferred_element_type=jnp.float32
    )
    delta = jnp.transpose(jnp.sum(grad_tiles.astype(jnp.float32) * attended, axis=-1), (0, 2, 1))[
        ..., None
    ]
    grad_probs = jnp.einsum(
        "athd,ashd->ahts", grad_tiles, value_set, preferred_element_type=jnp.float32
    )
    grad_logits = (probs * (grad_probs - delta) * scale).astype(jnp.bfloat16)
    query_grad = (
        jnp.einsum("ahts,ashd->athd", grad_logits, key_set, preferred_element_type=jnp.float32)
        .reshape(token_count, width)
        .astype(jnp.bfloat16)
    )
    key_part = jnp.einsum(
        "ahts,athd->ashd", grad_logits, query_tiles, preferred_element_type=jnp.float32
    ).reshape(tiles_dev * (LIST + 1), TILE, width)
    value_part = jnp.einsum(
        "ahts,athd->ashd", probs_half, grad_tiles, preferred_element_type=jnp.float32
    ).reshape(tiles_dev * (LIST + 1), TILE, width)
    flat_index = picked.reshape(-1)
    key_acc = jnp.zeros((window_tiles, TILE, width), jnp.float32).at[flat_index].add(key_part)
    value_acc = jnp.zeros((window_tiles, TILE, width), jnp.float32).at[flat_index].add(value_part)
    return (query_grad, key_acc, value_acc)


def per_device(
    lin_query,
    lin_key,
    lin_value,
    norm_gain,
    lin_grad,
    sm_query,
    sm_key,
    sm_value,
    sm_grad,
    tile_lists,
):
    token_count = lin_query.shape[0]
    lin_width = lin_query.shape[1]
    heads_lin = lin_width // HEAD
    query_lin = lin_query.reshape(token_count, heads_lin, HEAD)
    key_lin = lin_key.reshape(token_count, heads_lin, HEAD)
    value_lin = lin_value.reshape(token_count, heads_lin, HEAD)
    key_value = jnp.einsum("thi,thj->hij", key_lin, value_lin, preferred_element_type=jnp.float32)
    state_low = carried_in(key_value, False)
    state_half = state_low.astype(jnp.bfloat16)
    causal = jnp.tril(jnp.ones((token_count, token_count), jnp.bool_))
    attn_lin = jnp.where(
        causal[None],
        jnp.einsum("thd,shd->hts", query_lin, key_lin, preferred_element_type=jnp.float32),
        0.0,
    ).astype(jnp.bfloat16)
    output_lin = jnp.einsum(
        "hts,shd->thd", attn_lin, value_lin, preferred_element_type=jnp.float32
    ) + jnp.einsum("thi,hij->thj", query_lin, state_half, preferred_element_type=jnp.float32)
    gain_grad = norm_gain.reshape(1, heads_lin, HEAD) * lin_grad.reshape(
        token_count, heads_lin, HEAD
    ).astype(jnp.float32)
    square_sum = jnp.sum(output_lin * output_lin, axis=(1, 2))
    cross_sum = jnp.sum(gain_grad * output_lin, axis=(1, 2))
    sums = jnp.stack([square_sum, cross_sum])
    heads_dev = lax.axis_size("head")
    spread = jnp.broadcast_to(sums[None], (heads_dev,) + sums.shape)
    sums = jnp.sum(lax.all_to_all(spread, "head", 0, 0, tiled=True), axis=0)
    square_sum, cross_sum = sums[0], sums[1]
    full_width = LIN_HEADS * HEAD
    inv_rms = lax.rsqrt(square_sum / full_width + 1e-06)[:, None, None]
    grad_out = (
        gain_grad * inv_rms - output_lin * inv_rms**3 * (cross_sum / full_width)[:, None, None]
    ).astype(jnp.bfloat16)
    adjoint_local = jnp.einsum(
        "thi,thj->hij", query_lin, grad_out, preferred_element_type=jnp.float32
    )
    adjoint_high = carried_in(adjoint_local, True)
    adjoint_half = adjoint_high.astype(jnp.bfloat16)
    grad_scores = jnp.where(
        causal[None],
        jnp.einsum("thd,shd->hts", grad_out, value_lin, preferred_element_type=jnp.float32),
        0.0,
    ).astype(jnp.bfloat16)
    lin_dq = jnp.einsum(
        "hts,shd->thd", grad_scores, key_lin, preferred_element_type=jnp.float32
    ) + jnp.einsum("thj,hij->thi", grad_out, state_half, preferred_element_type=jnp.float32)
    lin_dk = jnp.einsum(
        "hts,thd->shd", grad_scores, query_lin, preferred_element_type=jnp.float32
    ) + jnp.einsum("shj,hij->shi", value_lin, adjoint_half, preferred_element_type=jnp.float32)
    lin_dv = jnp.einsum(
        "hts,thd->shd", attn_lin, grad_out, preferred_element_type=jnp.float32
    ) + jnp.einsum("shi,hij->shj", key_lin, adjoint_half, preferred_element_type=jnp.float32)
    lin_dq = lin_dq.reshape(token_count, lin_width).astype(jnp.bfloat16)
    lin_dk = lin_dk.reshape(token_count, lin_width).astype(jnp.bfloat16)
    lin_dv = lin_dv.reshape(token_count, lin_width).astype(jnp.bfloat16)
    width = sm_key.shape[1]
    pair = jnp.concatenate([sm_key, sm_value], axis=1)
    arrived = []
    moving = pair
    for distance in range(1, SPAN + 1):
        moving = from_behind(moving, CTX, 1)
        arrived.append(moving)
    key_window = jnp.concatenate(
        [arrived[SPAN - 1 - place][:, :width] for place in range(SPAN)] + [sm_key], axis=0
    )
    value_window = jnp.concatenate(
        [arrived[SPAN - 1 - place][:, width:] for place in range(SPAN)] + [sm_value], axis=0
    )
    shard = lax.axis_index(CTX)
    sm_dq, key_acc, value_acc = tile_attention(
        sm_query, sm_grad, key_window, value_window, tile_lists, shard
    )
    key_total = key_acc[SPAN]
    value_total = value_acc[SPAN]
    for distance in range(1, SPAN + 1):
        back = from_behind(
            jnp.concatenate(
                [key_acc[SPAN - distance], value_acc[SPAN - distance]], axis=1
            ).astype(jnp.bfloat16),
            CTX,
            -distance,
        ).astype(jnp.float32)
        key_total = key_total + back[:, :width]
        value_total = value_total + back[:, width:]
    return (
        lin_dq,
        lin_dk,
        lin_dv,
        sm_dq,
        key_total.astype(jnp.bfloat16),
        value_total.astype(jnp.bfloat16),
    )


def solution(mesh):
    placed = (
        P(CTX, "head"),
        P(CTX, "head"),
        P(CTX, "head"),
        P("head"),
        P(CTX, "head"),
        P(CTX, "head"),
        P(CTX, "head"),
        P(CTX, "head"),
        P(CTX, "head"),
        P(CTX, None),
    )
    count = mesh.shape["ctx"]
    inner = INNER if count % INNER == 0 else 1
    split = jax.sharding.Mesh(
        mesh.devices.reshape(count // inner, inner, mesh.shape["head"]), CTX + ("head",)
    )
    return jax.shard_map(
        per_device,
        mesh=split,
        in_specs=placed,
        out_specs=(
            P(CTX, "head"),
            P(CTX, "head"),
            P(CTX, "head"),
            P(CTX, "head"),
            P(CTX, "head"),
            P(CTX, "head"),
        ),
        check_vma=False,
    )
```

```python
import math

import jax
import jax.numpy as jnp
from jax import lax
from jax.sharding import PartitionSpec as P

HEAD = 128
LIN_HEADS = 16
TILE = 128
LIST = 3
SPAN = 4


CTX = ("outer", "inner")
INNER = 32
PLAN = (4,)


def scan_over(total, axis, backward):
    count = lax.axis_size(axis)
    plan = PLAN
    if math.prod(plan) != count:
        plan = (2,) * max(1, (count - 1).bit_length())
    own = total
    stride = 1
    for radix in plan:
        arrived = []
        for step in range(1, radix):
            distance = step * stride
            if distance >= count:
                break
            if backward:
                pairs = [(i, i - distance) for i in range(distance, count)]
            else:
                pairs = [(i, i + distance) for i in range(count - distance)]
            arrived.append(lax.ppermute(total.astype(jnp.bfloat16), axis, pairs))
        for part in arrived:
            total = total + part.astype(jnp.float32)
        stride *= radix
    return total - own


def gathered_before(total, axis, backward):
    count = lax.axis_size(axis)
    sent = jnp.broadcast_to(total.astype(jnp.bfloat16)[None], (count,) + total.shape)
    got = lax.all_to_all(sent, axis, 0, 0, tiled=True).astype(jnp.float32)
    index = jnp.arange(count)
    place = lax.axis_index(axis)
    mask = index > place if backward else index < place
    picked = jnp.where(mask.reshape((-1,) + (1,) * total.ndim), got, 0.0)
    return jnp.sum(picked, axis=0)


def carried_in(shard, backward):
    members = lax.axis_size("inner")
    slices = shard.astype(jnp.bfloat16).reshape(members, -1)
    mine = lax.all_to_all(slices, "inner", 0, 0, tiled=True).astype(jnp.float32)
    running = jnp.cumsum(mine, axis=0)
    group = jnp.sum(mine, axis=0)
    within = group[None] - running if backward else running - mine
    earlier = gathered_before(group, "outer", backward)
    states = (within + earlier[None]).astype(jnp.bfloat16)
    back = lax.all_to_all(states, "inner", 0, 0, tiled=True)
    return back.reshape(shard.shape).astype(shard.dtype)


def from_behind(shard, axis, by):
    length = lax.axis_size(axis)
    pairs = [(i, i + by) for i in range(length) if 0 <= i + by < length]
    return lax.ppermute(shard, axis, pairs)


def add_states(earlier, later):
    return earlier + later


def tile_attention(query, grad, key_window, value_window, lists, shard):
    token_count, width = query.shape
    heads = width // HEAD
    tiles_dev = token_count // TILE
    window_tiles = key_window.shape[0] // TILE
    valid = lists >= 0
    local_index = jnp.where(valid, lists - (shard - SPAN) * tiles_dev, 0)
    own_index = (SPAN * tiles_dev + jnp.arange(tiles_dev, dtype=jnp.int32))[:, None]
    picked = jnp.concatenate([own_index, local_index], axis=1)
    keep = jnp.concatenate([jnp.ones((tiles_dev, 1), jnp.bool_), valid], axis=1)
    key_set = key_window.reshape(window_tiles, TILE, heads, HEAD)[picked].reshape(
        tiles_dev, (LIST + 1) * TILE, heads, HEAD
    )
    value_set = value_window.reshape(window_tiles, TILE, heads, HEAD)[picked].reshape(
        tiles_dev, (LIST + 1) * TILE, heads, HEAD
    )
    query_tiles = query.reshape(tiles_dev, TILE, heads, HEAD)
    grad_tiles = grad.reshape(tiles_dev, TILE, heads, HEAD)
    scale = HEAD ** (-0.5)
    scores = (
        jnp.einsum("athd,ashd->ahts", query_tiles, key_set, preferred_element_type=jnp.float32)
        * scale
    )
    rows_idx = jnp.arange(TILE)[:, None]
    cols_idx = jnp.arange((LIST + 1) * TILE)[None, :]
    allowed = jnp.where(cols_idx // TILE == 0, cols_idx % TILE <= rows_idx, True)
    live = jnp.repeat(keep, TILE, axis=1)
    allowed_all = allowed[None, None, :, :] & live[:, None, None, :]
    scores = jnp.where(allowed_all, scores, -jnp.inf)
    top_score = jnp.max(scores, axis=-1, keepdims=True)
    expo = jnp.exp(scores - top_score)
    probs = expo / jnp.sum(expo, axis=-1, keepdims=True)
    probs_half = probs.astype(jnp.bfloat16)
    attended = jnp.einsum(
        "ahts,ashd->athd", probs_half, value_set, preferred_element_type=jnp.float32
    )
    delta = jnp.transpose(jnp.sum(grad_tiles.astype(jnp.float32) * attended, axis=-1), (0, 2, 1))[
        ..., None
    ]
    grad_probs = jnp.einsum(
        "athd,ashd->ahts", grad_tiles, value_set, preferred_element_type=jnp.float32
    )
    grad_logits = (probs * (grad_probs - delta) * scale).astype(jnp.bfloat16)
    query_grad = (
        jnp.einsum("ahts,ashd->athd", grad_logits, key_set, preferred_element_type=jnp.float32)
        .reshape(token_count, width)
        .astype(jnp.bfloat16)
    )
    key_part = jnp.einsum(
        "ahts,athd->ashd", grad_logits, query_tiles, preferred_element_type=jnp.float32
    ).reshape(tiles_dev * (LIST + 1), TILE, width)
    value_part = jnp.einsum(
        "ahts,athd->ashd", probs_half, grad_tiles, preferred_element_type=jnp.float32
    ).reshape(tiles_dev * (LIST + 1), TILE, width)
    flat_index = picked.reshape(-1)
    key_acc = jnp.zeros((window_tiles, TILE, width), jnp.float32).at[flat_index].add(key_part)
    value_acc = jnp.zeros((window_tiles, TILE, width), jnp.float32).at[flat_index].add(value_part)
    return (query_grad, key_acc, value_acc)


def per_device(
    lin_query,
    lin_key,
    lin_value,
    norm_gain,
    lin_grad,
    sm_query,
    sm_key,
    sm_value,
    sm_grad,
    tile_lists,
):
    token_count = lin_query.shape[0]
    lin_width = lin_query.shape[1]
    heads_lin = lin_width // HEAD
    query_lin = lin_query.reshape(token_count, heads_lin, HEAD)
    key_lin = lin_key.reshape(token_count, heads_lin, HEAD)
    value_lin = lin_value.reshape(token_count, heads_lin, HEAD)
    key_value = jnp.einsum("thi,thj->hij", key_lin, value_lin, preferred_element_type=jnp.float32)
    state_low = carried_in(key_value, False)
    state_half = state_low.astype(jnp.bfloat16)
    causal = jnp.tril(jnp.ones((token_count, token_count), jnp.bool_))
    attn_lin = jnp.where(
        causal[None],
        jnp.einsum("thd,shd->hts", query_lin, key_lin, preferred_element_type=jnp.float32),
        0.0,
    ).astype(jnp.bfloat16)
    output_lin = jnp.einsum(
        "hts,shd->thd", attn_lin, value_lin, preferred_element_type=jnp.float32
    ) + jnp.einsum("thi,hij->thj", query_lin, state_half, preferred_element_type=jnp.float32)
    gain_grad = norm_gain.reshape(1, heads_lin, HEAD) * lin_grad.reshape(
        token_count, heads_lin, HEAD
    ).astype(jnp.float32)
    square_sum = jnp.sum(output_lin * output_lin, axis=(1, 2))
    cross_sum = jnp.sum(gain_grad * output_lin, axis=(1, 2))
    sums = jnp.stack([square_sum, cross_sum])
    heads_dev = lax.axis_size("head")
    spread = jnp.broadcast_to(sums[None], (heads_dev,) + sums.shape)
    sums = jnp.sum(lax.all_to_all(spread, "head", 0, 0, tiled=True), axis=0)
    square_sum, cross_sum = sums[0], sums[1]
    full_width = LIN_HEADS * HEAD
    inv_rms = lax.rsqrt(square_sum / full_width + 1e-06)[:, None, None]
    grad_out = (
        gain_grad * inv_rms - output_lin * inv_rms**3 * (cross_sum / full_width)[:, None, None]
    ).astype(jnp.bfloat16)
    adjoint_local = jnp.einsum(
        "thi,thj->hij", query_lin, grad_out, preferred_element_type=jnp.float32
    )
    adjoint_high = carried_in(adjoint_local, True)
    adjoint_half = adjoint_high.astype(jnp.bfloat16)
    grad_scores = jnp.where(
        causal[None],
        jnp.einsum("thd,shd->hts", grad_out, value_lin, preferred_element_type=jnp.float32),
        0.0,
    ).astype(jnp.bfloat16)
    lin_dq = jnp.einsum(
        "hts,shd->thd", grad_scores, key_lin, preferred_element_type=jnp.float32
    ) + jnp.einsum("thj,hij->thi", grad_out, state_half, preferred_element_type=jnp.float32)
    lin_dk = jnp.einsum(
        "hts,thd->shd", grad_scores, query_lin, preferred_element_type=jnp.float32
    ) + jnp.einsum("shj,hij->shi", value_lin, adjoint_half, preferred_element_type=jnp.float32)
    lin_dv = jnp.einsum(
        "hts,thd->shd", attn_lin, grad_out, preferred_element_type=jnp.float32
    ) + jnp.einsum("shi,hij->shj", key_lin, adjoint_half, preferred_element_type=jnp.float32)
    lin_dq = lin_dq.reshape(token_count, lin_width).astype(jnp.bfloat16)
    lin_dk = lin_dk.reshape(token_count, lin_width).astype(jnp.bfloat16)
    lin_dv = lin_dv.reshape(token_count, lin_width).astype(jnp.bfloat16)
    width = sm_key.shape[1]
    pair = jnp.concatenate([sm_key, sm_value], axis=1)
    arrived = []
    moving = pair
    for distance in range(1, SPAN + 1):
        moving = from_behind(moving, CTX, 1)
        arrived.append(moving)
    key_window = jnp.concatenate(
        [arrived[SPAN - 1 - place][:, :width] for place in range(SPAN)] + [sm_key], axis=0
    )
    value_window = jnp.concatenate(
        [arrived[SPAN - 1 - place][:, width:] for place in range(SPAN)] + [sm_value], axis=0
    )
    shard = lax.axis_index(CTX)
    sm_dq, key_acc, value_acc = tile_attention(
        sm_query, sm_grad, key_window, value_window, tile_lists, shard
    )
    key_total = key_acc[SPAN]
    value_total = value_acc[SPAN]
    for distance in range(1, SPAN + 1):
        back = from_behind(
            jnp.concatenate(
                [key_acc[SPAN - distance], value_acc[SPAN - distance]], axis=1
            ).astype(jnp.bfloat16),
            CTX,
            -distance,
        ).astype(jnp.float32)
        key_total = key_total + back[:, :width]
        value_total = value_total + back[:, width:]
    return (
        lin_dq,
        lin_dk,
        lin_dv,
        sm_dq,
        key_total.astype(jnp.bfloat16),
        value_total.astype(jnp.bfloat16),
    )


def solution(mesh):
    placed = (
        P(CTX, "head"),
        P(CTX, "head"),
        P(CTX, "head"),
        P("head"),
        P(CTX, "head"),
        P(CTX, "head"),
        P(CTX, "head"),
        P(CTX, "head"),
        P(CTX, "head"),
        P(CTX, None),
    )
    count = mesh.shape["ctx"]
    inner = INNER if count % INNER == 0 else 1
    split = jax.sharding.Mesh(
        mesh.devices.reshape(count // inner, inner, mesh.shape["head"]), CTX + ("head",)
    )
    return jax.shard_map(
        per_device,
        mesh=split,
        in_specs=placed,
        out_specs=(
            P(CTX, "head"),
            P(CTX, "head"),
            P(CTX, "head"),
            P(CTX, "head"),
            P(CTX, "head"),
            P(CTX, "head"),
        ),
        check_vma=False,
    )
```
